128 devices in a mesh: gx: 4 (over x), gy: 16 (over z, y), wa: 2 (over core).
Axes of the slice: x: 4, y: 4, z: 4, core: 2. Of those that a mesh axis runs over, the one named last changes fastest.
Arguments:
- pressure: float32 [24, 256, 512], P(None, ('gy', 'wa'), 'gx'), may hold values from -6 to 6
- saturation: float32 [24, 256, 512], P(None, ('gy', 'wa'), 'gx'), may hold values from 0.1 to 0.9
- sat_old: float32 [24, 256, 512], P(None, ('gy', 'wa'), 'gx'), may hold values from 0.1 to 0.9
- pore: float32 [24, 256, 512], P(None, ('gy', 'wa'), 'gx'), may hold values from 0.5 to 2
- trans_x: float32 [24, 256, 512], P(None, ('gy', 'wa'), 'gx'), may hold values from 0.3 to 3
- trans_y: float32 [24, 256, 512], P(None, ('gy', 'wa'), 'gx'), may hold values from 0.3 to 3
- trans_z: float32 [24, 256, 512], P(None, ('gy', 'wa'), 'gx'), may hold values from 0.3 to 3
- upwind_x: int32 [24, 256, 512], P(None, ('gy', 'wa'), 'gx'), may hold values 0 or 1
- upwind_y: int32 [24, 256, 512], P(None, ('gy', 'wa'), 'gx'), may hold values 0 or 1
- upwind_z: int32 [24, 256, 512], P(None, ('gy', 'wa'), 'gx'), may hold values 0 or 1
- directions: float32 [4, 2, 24, 256, 512], P(None, None, None, ('gy', 'wa'), 'gx'), may hold values from -6 to 6
- adjoint_weights: float32 [4, 2, 24, 256, 512], P(None, None, None, ('gy', 'wa'), 'gx'), may hold values from -6 to 6
- perf_well: int32 [4096], P(('gx', 'gy', 'wa')), may hold values from 0 to 2047, as said below
- perf_col: int32 [4096], P(('gx', 'gy', 'wa')), may hold values from 0 to 1023
- perf_top: int32 [4096], P(('gx', 'gy', 'wa')), may hold values from 0 to 11
- perf_span: int32 [4096], P(('gx', 'gy', 'wa')), may hold values from 1 to 12
- perf_index: float32 [4096], P(('gx', 'gy', 'wa')), may hold values from 0.5 to 2
- bhp: float32 [2048], replicated, may hold values from -6 to 6
- target: float32 [2048], replicated, may hold values from -4 to 4
Outputs:
- reduced_residual: float32 [2, 24, 256, 512], P(None, None, ('gy', 'wa'), 'gx')
- forward_products: float32 [4, 2, 24, 256, 512], P(None, None, None, ('gy', 'wa'), 'gx')
- adjoint_products: float32 [4, 2, 24, 256, 512], P(None, None, None, ('gy', 'wa'), 'gx')
The draws below stay inside these ranges and needn't reach their ends.
Inputs may be any that keep to these rules, and one draw needn't show every extreme that they name: `perf_well`: every well is named by at least one perforation row; well w is owned by device w // 16 of the axes gx+gy+wa.
All inputs are finite; a program needn't handle non-finite values. No bound on the sum of `upwind_x` or of `upwind_y` or of `upwind_z` on one device may be relied on, other than what follows from the above.
Results may differ from the reference program's by a relative error of at most 0.0002.
Values sent between devices are 32-bit elements; how exact they have to be, the bound alone decides.
No kernel may reach another device: no remote copies, remote signals or barrier semaphores. Data moves between devices by JAX's collectives and lax.ppermute only.
A program may use at most 64 MiB of HBM per device.

```python
import math
import jax
import jax.numpy as jnp
from jax import lax

CX = 128
CY = 8
NZ = 24
NDIR = 4
PERF_DEV = 32
NX = 512
NY = 256
NW = 2048
NPERF = 4096
N_GY = 16
N_WA = 2


def draw_perf_well(key, part):
    first, second = jax.random.split(key)
    extra = jax.random.randint(first, (NPERF - NW,), 0, NW).astype(jnp.int32)
    rows_all = jnp.concatenate([jnp.arange(NW, dtype=jnp.int32), extra])
    order = jax.random.permutation(second, NPERF)
    return rows_all[order]


def touch_ends(result, stream_key, low, largest):
    extent = result.shape
    index_at = [jax.random.randint(jax.random.fold_in(stream_key, axis), (), 0, extent[axis]) for axis in range(len(extent))]
    result = result.at[tuple(index_at)].set(low)
    longest = extent.index(max(extent))
    index_at[longest] = (index_at[longest] + 1) % extent[longest]
    return result.at[tuple(index_at)].set(largest)


def levels(key, dims, cuts, least, top_value):
    def one(position, shards_of):
        draws = jax.random.uniform(jax.random.fold_in(jax.random.fold_in(key, 6), position), (shards_of,), jnp.float32, least / len(cuts), top_value / len(cuts))
        return jnp.repeat(jnp.exp(draws), dims[position] // shards_of).reshape((-1,) + (1,) * (len(dims) - position - 1))

    factor_of = one(*cuts[0])
    for cut in cuts[1:]:
        factor_of = factor_of * one(*cut)
    return factor_of


def scatter_about(stream_key, dims, scale, most, pieces=(), held_as=jnp.bfloat16):
    entries = scale * jax.random.normal(stream_key, dims, jnp.float32)
    if pieces:
        entries = entries * levels(stream_key, dims, pieces, -0.22, 0.18)
    return jnp.clip(entries, -most, most).astype(held_as)


def setup_inputs(seed: int = 0) -> dict:
    key_list = jax.random.split(jax.random.key(seed), 20)
    pressure = scatter_about(key_list[0], (NZ, NY, NX), 1.0, 6.0, ((1, 32), (2, 4)), jnp.float32)
    saturation = jnp.clip(0.1 + 0.79999997 * jax.random.uniform(key_list[1], (NZ, NY, NX), jnp.float32) ** levels(key_list[1], (NZ, NY, NX), ((1, 32), (2, 4)), -0.2, 0.2), 0.1, 0.9)
    sat_old = jnp.clip(0.1 + 0.79999997 * jax.random.uniform(key_list[2], (NZ, NY, NX), jnp.float32) ** levels(key_list[2], (NZ, NY, NX), ((1, 32), (2, 4)), -0.2, 0.2), 0.1, 0.9)
    pore = jnp.clip(jnp.exp(math.log(2.0) - 1.3862944 * jax.random.uniform(key_list[3], (NZ, NY, NX), jnp.float32) ** levels(key_list[3], (NZ, NY, NX), ((1, 32), (2, 4)), -0.2, 0.2)), 0.5, 2.0)
    trans_x = jnp.clip(jnp.exp(math.log(3.0) - 2.3025851 * jax.random.uniform(key_list[4], (NZ, NY, NX), jnp.float32) ** levels(key_list[4], (NZ, NY, NX), ((1, 32), (2, 4)), -0.2, 0.2)), 0.3, 3.0)
    trans_y = jnp.clip(jnp.exp(math.log(3.0) - 2.3025851 * jax.random.uniform(key_list[5], (NZ, NY, NX), jnp.float32) ** levels(key_list[5], (NZ, NY, NX), ((1, 32), (2, 4)), -0.2, 0.2)), 0.3, 3.0)
    trans_z = jnp.clip(jnp.exp(math.log(3.0) - 2.3025851 * jax.random.uniform(key_list[6], (NZ, NY, NX), jnp.float32) ** levels(key_list[6], (NZ, NY, NX), ((1, 32), (2, 4)), -0.2, 0.2)), 0.3, 3.0)
    upwind_x = touch_ends((jax.random.randint(key_list[7], (NZ, NY, NX), 0, 2) < 1).astype(jnp.int32), jax.random.fold_in(key_list[7], 1), 0, 1)
    upwind_y = touch_ends((jax.random.randint(key_list[8], (NZ, NY, NX), 0, 2) < 1).astype(jnp.int32), jax.random.fold_in(key_list[8], 1), 0, 1)
    upwind_z = touch_ends((jax.random.randint(key_list[9], (NZ, NY, NX), 0, 2) < 1).astype(jnp.int32), jax.random.fold_in(key_list[9], 1), 0, 1)
    directions = scatter_about(key_list[10], (NDIR, 2, NZ, NY, NX), 1.0, 6.0, ((3, 32), (4, 4)), jnp.float32)
    adjoint_weights = scatter_about(key_list[11], (NDIR, 2, NZ, NY, NX), 1.0, 6.0, ((3, 32), (4, 4)), jnp.float32)
    perf_well = draw_perf_well(jax.random.fold_in(key_list[19], 71), 0)
    perf_col = touch_ends(jax.random.randint(key_list[13], (NPERF,), 0, CX * CY), jax.random.fold_in(key_list[13], 1), 0, (CX * CY) - 1).astype(jnp.int32)
    perf_top = touch_ends(jax.random.randint(key_list[14], (NPERF,), 0, NZ // 2), jax.random.fold_in(key_list[14], 1), 0, (NZ // 2) - 1).astype(jnp.int32)
    perf_span = touch_ends(jax.random.randint(key_list[15], (NPERF,), 1, NZ // 2 + 1), jax.random.fold_in(key_list[15], 1), 1, (NZ // 2 + 1) - 1).astype(jnp.int32)
    perf_index = jnp.clip(jnp.exp(math.log(2.0) - 1.3862944 * jax.random.uniform(key_list[16], (NPERF,), jnp.float32) ** levels(key_list[16], (NPERF,), ((0, 128),), -0.2, 0.2)), 0.5, 2.0)
    bhp = scatter_about(key_list[17], (NW,), 1.0, 6.0, (), jnp.float32)
    target = jnp.clip(jax.random.uniform(key_list[18], (NW,), jnp.float32, -4.0, 4.0), -4.0, 4.0)
    return dict(pressure=pressure, saturation=saturation, sat_old=sat_old, pore=pore, trans_x=trans_x, trans_y=trans_y, trans_z=trans_z, upwind_x=upwind_x, upwind_y=upwind_y, upwind_z=upwind_z, directions=directions, adjoint_weights=adjoint_weights, perf_well=perf_well, perf_col=perf_col, perf_top=perf_top, perf_span=perf_span, perf_index=perf_index, bhp=bhp, target=target)


water_visc = 0.5
oil_visc = 2.0
water_head = 0.3
oil_head = 0.2

def mobility(sat):
    return jnp.stack([sat * sat / water_visc, (1.0 - sat) * (1.0 - sat) / oil_visc])

def mobility_slope(sat):
    return jnp.stack([2.0 * sat / water_visc, -2.0 * (1.0 - sat) / oil_visc])

def face_flux(trans, lower_up, first, second, heads):
    sat_up = jnp.where(lower_up, first[1], second[1])
    drop = first[0] - second[0]
    potential = jnp.stack([drop + heads[0], drop + heads[1]])
    return trans * mobility(sat_up) * potential

def reference(pressure, saturation, sat_old, pore, trans_x, trans_y, trans_z, upwind_x, upwind_y, upwind_z, directions, adjoint_weights, perf_well, perf_col, perf_top, perf_span, perf_index, bhp, target):
    state = jnp.stack([pressure, saturation])
    rows_all = jnp.arange(NPERF, dtype=jnp.int32)
    block = rows_all // PERF_DEV
    block_x = block // (N_GY * N_WA)
    block_y = block % (N_GY * N_WA)
    cell_y = block_y * CY + perf_col // CX
    cell_x = block_x * CX + perf_col % CX
    flat = (cell_y * NX + cell_x).astype(jnp.int32)
    depth = jnp.arange(NZ, dtype=jnp.int32)[:, None]
    open_layer = jnp.logical_and(depth >= perf_top[None, :], depth < (perf_top + perf_span)[None, :])
    weight = jnp.where(open_layer, perf_index[None, :], jnp.float32(0.0))
    row_bhp = bhp[perf_well]

    def at_perfs(field):
        return field.reshape(field.shape[:-2] + (NY * NX,))[..., flat]

    def residual(st):
        fx = face_flux(trans_x[:, :, :-1], upwind_x[:, :, :-1] == 1, st[:, :, :, :-1], st[:, :, :, 1:], (0.0, 0.0))
        div = jnp.pad(fx, ((0, 0), (0, 0), (0, 0), (0, 1))) - jnp.pad(fx, ((0, 0), (0, 0), (0, 0), (1, 0)))
        fy = face_flux(trans_y[:, :-1, :], upwind_y[:, :-1, :] == 1, st[:, :, :-1, :], st[:, :, 1:, :], (0.0, 0.0))
        div = div + jnp.pad(fy, ((0, 0), (0, 0), (0, 1), (0, 0))) - jnp.pad(fy, ((0, 0), (0, 0), (1, 0), (0, 0)))
        fz = face_flux(trans_z[:-1], upwind_z[:-1] == 1, st[:, :-1], st[:, 1:], (water_head, oil_head))
        div = div + jnp.pad(fz, ((0, 0), (0, 1), (0, 0), (0, 0))) - jnp.pad(fz, ((0, 0), (1, 0), (0, 0), (0, 0)))
        change = st[1] - sat_old
        accum = jnp.stack([pore * change, -pore * change])
        p_cells = at_perfs(st[0])
        s_cells = at_perfs(st[1])
        rates = weight * mobility(s_cells) * (p_cells - row_bhp)
        wells = jnp.zeros((2, NZ, NY * NX), jnp.float32).at[:, :, flat].add(rates).reshape(2, NZ, NY, NX)
        return div + accum + wells
    value, pullback = jax.vjp(residual, state)

    def pulled(cot):
        return pullback(cot)[0]
    unused, pushback = jax.vjp(pulled, jnp.zeros_like(value))
    forward = lax.map(lambda item: pushback(item)[0], directions)
    adjoint = lax.map(pulled, adjoint_weights)
    p_cells = at_perfs(pressure)
    s_cells = at_perfs(saturation)
    mob = mobility(s_cells)
    slope = mobility_slope(s_cells)
    drive = p_cells - row_bhp
    mob_total = mob[0] + mob[1]
    slope_total = slope[0] + slope[1]
    dir_cells = at_perfs(directions)
    wts_cells = at_perfs(adjoint_weights)
    conduct_rows = lax.optimization_barrier(jnp.sum(weight * mob_total, axis=0))
    rate_rows = lax.optimization_barrier(jnp.sum(weight * mob_total * drive, axis=0))
    inflow_rows = lax.optimization_barrier(jnp.sum(weight * (mob_total * dir_cells[:, 0] + slope_total * drive * dir_cells[:, 1]), axis=1))
    outflow_rows = lax.optimization_barrier(jnp.sum(weight * (mob[0] * wts_cells[:, 0] + mob[1] * wts_cells[:, 1]), axis=1))
    conduct = jax.ops.segment_sum(conduct_rows, perf_well, num_segments=NW)
    rate = jax.ops.segment_sum(rate_rows, perf_well, num_segments=NW)
    inflow = jax.vmap(lambda rowvals: jax.ops.segment_sum(rowvals, perf_well, num_segments=NW))(inflow_rows)
    outflow = jax.vmap(lambda rowvals: jax.ops.segment_sum(rowvals, perf_well, num_segments=NW))(outflow_rows)
    factor = ((rate - target) / conduct)[perf_well]
    infactor = (inflow / conduct[None, :])[:, perf_well]
    outfactor = (outflow / conduct[None, :])[:, perf_well]

    def spread(values):
        lead = values.shape[:-2]
        return jnp.zeros(lead + (NZ, NY * NX), jnp.float32).at[..., flat].add(values).reshape(lead + (NZ, NY, NX))
    reduced_residual = value - spread(weight * mob * factor)
    forward_products = forward - spread(weight * mob * infactor[:, None, None, :])
    out_f = outfactor[:, None, :]
    adjoint_part = jnp.stack([weight * mob_total * out_f, weight * slope_total * drive * out_f], axis=1)
    adjoint_products = adjoint - spread(adjoint_part)
    return (reduced_residual, forward_products, adjoint_products)
```

```python
import functools

import jax
import jax.numpy as jnp
from jax import lax
from jax.sharding import Mesh
from jax.sharding import PartitionSpec as P

GY_WA = ("gy_0", "gy_1", "wa")
GX_GY_WA = ("gx", "gy_0", "gy_1", "wa")


water_visc = 0.5
oil_visc = 2.0
water_head = 0.3
oil_head = 0.2


def extended(shard, sides, width):
    edges = {}
    for axis, dim in sides:
        peers, length = (lax.axis_size(axis), shard.shape[dim])
        up = [(i, (i + 1) % peers) for i in range(peers - 1)]
        last = lax.slice_in_dim(shard, length - width, length, axis=dim)
        initial = lax.slice_in_dim(shard, 0, width, axis=dim)
        edges[dim] = (
            lax.ppermute(last, axis, up),
            lax.ppermute(initial, axis, [(b, a) for a, b in up]),
        )
    done = []
    for _, dim in sides:
        low, high = edges[dim]
        around = [(width, width) if d in done else (0, 0) for d in range(shard.ndim)]
        shard = jnp.concatenate([jnp.pad(low, around), shard, jnp.pad(high, around)], axis=dim)
        done.append(dim)
    return shard


def gather_everywhere(block):
    held = block[None]
    for axis in ("wa", "gx", "gy_1", "gy_0"):
        size = lax.axis_size(axis)
        step = 1
        while step < size:
            other = lax.ppermute(held, axis, [(i, i ^ step) for i in range(size)])
            held = jnp.concatenate([held, other], axis=0)
            step *= 2
    return held


def mobility(sat):
    return jnp.stack([sat * sat / water_visc, (1.0 - sat) * (1.0 - sat) / oil_visc])


def mobility_slope(sat):
    return jnp.stack([2.0 * sat / water_visc, -2.0 * (1.0 - sat) / oil_visc])


def face_flux(trans, lower_up, first, second, heads):
    sat_up = jnp.where(lower_up, first[1], second[1])
    drop = first[0] - second[0]
    potential = jnp.stack([drop + heads[0], drop + heads[1]])
    return trans * mobility(sat_up) * potential


def well_factors(sums, goal):
    return jnp.concatenate([((sums[1] - goal) / sums[0])[None], sums[2:] / sums[0][None]], axis=0)


def body(
    pressure,
    saturation,
    sat_old,
    pore,
    trans_x,
    trans_y,
    trans_z,
    upwind_x,
    upwind_y,
    upwind_z,
    directions,
    adjoint_weights,
    perf_well,
    perf_col,
    perf_top,
    perf_span,
    perf_index,
    bhp,
    target,
):
    state = jnp.stack([pressure, saturation])
    layers, rows, cols = pressure.shape
    spatial = (layers, rows, cols)
    ndir = directions.shape[0]
    nwells = target.shape[0]
    last_x = lax.axis_index("gx") == lax.axis_size("gx") - 1
    last_y = lax.axis_index(GY_WA) == lax.axis_size(GY_WA) - 1
    col_keep = jnp.where(jnp.logical_and(last_x, jnp.arange(cols) == cols - 1), 0.0, 1.0)
    row_keep = jnp.where(jnp.logical_and(last_y, jnp.arange(rows) == rows - 1), 0.0, 1.0)
    trans_xe = trans_x * col_keep[None, None, :]
    trans_ye = trans_y * row_keep[None, :, None]
    flag_x = upwind_x.astype(jnp.float32)
    flag_y = upwind_y.astype(jnp.float32)
    count = 2 + 4 * ndir
    cell_data = jnp.concatenate(
        [
            state,
            directions.reshape((2 * ndir,) + spatial),
            adjoint_weights.reshape((2 * ndir,) + spatial),
        ],
        axis=0,
    )
    stacked = jnp.concatenate([cell_data, jnp.stack([trans_xe, trans_ye, flag_x, flag_y])], axis=0)
    padded = extended(stacked, ((GY_WA, 2), ("gx", 3)), 1)
    cells_pad = padded[:count]
    tx_face = padded[count, :, 1:-1, :-1]
    ty_face = padded[count + 1, :, :-1, 1:-1]
    ux_face = padded[count + 2, :, 1:-1, :-1]
    uy_face = padded[count + 3, :, :-1, 1:-1]
    state_pad = cells_pad[:2]
    dir_pad = cells_pad[2 : 2 + 2 * ndir].reshape((ndir, 2) + cells_pad.shape[1:])
    wts_pad = cells_pad[2 + 2 * ndir :].reshape((ndir, 2) + cells_pad.shape[1:])
    lower_x = ux_face > 0.5
    lower_y = uy_face > 0.5
    lower_z = upwind_z[:-1] == 1
    trans_zf = trans_z[:-1]

    def divergence(padded_state):
        fx = face_flux(
            tx_face,
            lower_x,
            padded_state[:, :, 1:-1, :-1],
            padded_state[:, :, 1:-1, 1:],
            (0.0, 0.0),
        )
        div = jnp.pad(fx, ((0, 0), (0, 0), (1, 1), (0, 1))) - jnp.pad(
            fx, ((0, 0), (0, 0), (1, 1), (1, 0))
        )
        fy = face_flux(
            ty_face,
            lower_y,
            padded_state[:, :, :-1, 1:-1],
            padded_state[:, :, 1:, 1:-1],
            (0.0, 0.0),
        )
        div = (
            div
            + jnp.pad(fy, ((0, 0), (0, 0), (0, 1), (1, 1)))
            - jnp.pad(fy, ((0, 0), (0, 0), (1, 0), (1, 1)))
        )
        inner = padded_state[:, :, 1:-1, 1:-1]
        fz = face_flux(trans_zf, lower_z, inner[:, :-1], inner[:, 1:], (water_head, oil_head))
        vertical = jnp.pad(fz, ((0, 0), (0, 1), (0, 0), (0, 0))) - jnp.pad(
            fz, ((0, 0), (1, 0), (0, 0), (0, 0))
        )
        return div + jnp.pad(vertical, ((0, 0), (0, 0), (1, 1), (1, 1)))

    flux_div, pullback = jax.vjp(divergence, state_pad)

    def pulled(cot):
        return pullback(cot)[0]

    unused, pushback = jax.vjp(pulled, jnp.zeros_like(flux_div))
    forward_flux = jax.vmap(lambda item: pushback(item)[0])(dir_pad)[..., 1:-1, 1:-1]
    adjoint_flux = jax.vmap(pulled)(wts_pad)[..., 1:-1, 1:-1]
    change = saturation - sat_old
    accum = jnp.stack([pore * change, -pore * change])
    forward_acc = jnp.stack([pore * directions[:, 1], -pore * directions[:, 1]], axis=1)
    adjoint_acc = jnp.stack(
        [
            jnp.zeros_like(adjoint_weights[:, 0]),
            pore * (adjoint_weights[:, 0] - adjoint_weights[:, 1]),
        ],
        axis=1,
    )
    flat_count = rows * cols
    perf_rows = perf_col.shape[0]

    def at_perfs(field):
        return jnp.take(field.reshape(field.shape[:-2] + (flat_count,)), perf_col, axis=-1)

    p_cells = at_perfs(pressure)
    s_cells = at_perfs(saturation)
    depth = jnp.arange(layers)[:, None]
    open_layer = jnp.logical_and(
        depth >= perf_top[None, :], depth < (perf_top + perf_span)[None, :]
    )
    weight = jnp.where(open_layer, perf_index[None, :], 0.0)
    row_bhp = jnp.take(bhp, perf_well)
    drive = p_cells - row_bhp
    mob = mobility(s_cells)
    slope = mobility_slope(s_cells)
    mob_total = mob[0] + mob[1]
    slope_total = slope[0] + slope[1]
    rates = weight * mob * drive
    dir_cells = at_perfs(directions)
    wts_cells = at_perfs(adjoint_weights)
    rate_tangent = weight * (mob * dir_cells[:, 0:1] + slope * drive * dir_cells[:, 1:2])
    grad_p = weight * (mob[0] * wts_cells[:, 0] + mob[1] * wts_cells[:, 1])
    grad_s = weight * drive * (slope[0] * wts_cells[:, 0] + slope[1] * wts_cells[:, 1])
    row_sums = jnp.concatenate(
        [
            jnp.sum(weight * mob_total, axis=0)[None],
            jnp.sum(rates[0] + rates[1], axis=0)[None],
            jnp.sum(rate_tangent[:, 0] + rate_tangent[:, 1], axis=1),
            jnp.sum(grad_p, axis=1),
        ],
        axis=0,
    )
    packed = jnp.concatenate([row_sums, perf_well.astype(jnp.float32)[None]], axis=0)
    everyone = gather_everywhere(packed)
    all_sums = jnp.moveaxis(everyone[:, :-1], 1, 0).reshape(row_sums.shape[0], -1)
    all_wells = everyone[:, -1].reshape(-1)
    same_well = (perf_well.astype(jnp.float32)[:, None] == all_wells[None, :]).astype(jnp.float32)
    row_totals = jnp.dot(all_sums, same_well.T, precision=lax.Precision.HIGHEST)
    row_target = jnp.take(target, perf_well)
    row_factors = well_factors(row_totals, row_target)
    wells_res = rates - weight * mob * row_factors[0]
    wells_fwd = rate_tangent - (weight * mob)[None] * row_factors[1 : 1 + ndir][:, None, None, :]
    out_f = row_factors[1 + ndir :][:, None, :]
    wells_adj = jnp.stack(
        [grad_p - weight * mob_total * out_f, grad_s - weight * slope_total * drive * out_f], axis=1
    )
    combined = jnp.concatenate([wells_res[None], wells_fwd, wells_adj], axis=0)
    from_perfs = (perf_col[:, None] == jnp.arange(flat_count)[None, :]).astype(jnp.float32)
    spread = jnp.dot(
        combined.reshape(-1, perf_rows), from_perfs, precision=lax.Precision.HIGHEST
    ).reshape((1 + 2 * ndir, 2) + spatial)
    reduced_residual = flux_div[:, :, 1:-1, 1:-1] + accum + spread[0]
    forward_products = forward_flux + forward_acc + spread[1 : 1 + ndir]
    adjoint_products = adjoint_flux + adjoint_acc + spread[1 + ndir :]
    return (reduced_residual, forward_products, adjoint_products)


def solution(mesh):
    split = Mesh(
        mesh.devices.reshape(mesh.shape["gx"], 4, 4, mesh.shape["wa"]), ("gx", "gy_0", "gy_1", "wa")
    )
    return jax.shard_map(
        body,
        mesh=split,
        in_specs=(
            P(None, GY_WA, "gx"),
            P(None, GY_WA, "gx"),
            P(None, GY_WA, "gx"),
            P(None, GY_WA, "gx"),
            P(None, GY_WA, "gx"),
            P(None, GY_WA, "gx"),
            P(None, GY_WA, "gx"),
            P(None, GY_WA, "gx"),
            P(None, GY_WA, "gx"),
            P(None, GY_WA, "gx"),
            P(None, None, None, GY_WA, "gx"),
            P(None, None, None, GY_WA, "gx"),
            P(GX_GY_WA),
            P(GX_GY_WA),
            P(GX_GY_WA),
            P(GX_GY_WA),
            P(GX_GY_WA),
            P(),
            P(),
        ),
        out_specs=(
            P(None, None, GY_WA, "gx"),
            P(None, None, None, GY_WA, "gx"),
            P(None, None, None, GY_WA, "gx"),
        ),
        check_vma=False,
    )
```

```python
import jax
import jax.numpy as jnp
from jax import lax
from jax.experimental import pallas as pl
from jax.experimental.pallas import tpu as pltpu
from jax.sharding import Mesh
from jax.sharding import PartitionSpec as P

GY_WA = ("gy_0", "gy_1", "wa")
GX_GY_WA = ("gx", "gy_0", "gy_1", "wa")


water_visc = 0.5
oil_visc = 2.0
water_head = 0.3
oil_head = 0.2


def gather_everywhere(block):
    held = block[None]
    for axis in ("wa", "gx", "gy_1", "gy_0"):
        size = lax.axis_size(axis)
        step = 1
        while step < size:
            other = lax.ppermute(held, axis, [(i, i ^ step) for i in range(size)])
            held = jnp.concatenate([held, other], axis=0)
            step *= 2
    return held


def shift_along(block, axis, down):
    size = lax.axis_size(axis)
    pairs = [(i, i + 1) for i in range(size - 1)]
    if not down:
        pairs = [(b, a) for a, b in pairs]
    return lax.ppermute(block, axis, pairs)


def mobility(sat):
    return jnp.stack([sat * sat / water_visc, (1.0 - sat) * (1.0 - sat) / oil_visc])


def mobility_slope(sat):
    return jnp.stack([2.0 * sat / water_visc, -2.0 * (1.0 - sat) / oil_visc])


def well_factors(sums, goal):
    return jnp.concatenate([((sums[1] - goal) / sums[0])[None], sums[2:] / sums[0][None]], axis=0)


def face_terms(trans, up, a, b, heads, ndir):
    pa, sa, vpa, vsa, wwa, woa = a
    pb, sb, vpb, vsb, wwb, wob = b
    su = jnp.where(up, sa, sb)
    drop = pa - pb
    pot_w = drop + heads[0]
    pot_o = drop + heads[1]
    tl_w = trans * (su * su / water_visc)
    tl_o = trans * ((1.0 - su) * (1.0 - su) / oil_visc)
    f_w = tl_w * pot_w
    f_o = tl_o * pot_o
    td_w = trans * (2.0 * su / water_visc) * pot_w
    td_o = trans * (-2.0 * (1.0 - su) / oil_visc) * pot_o
    jv_w, jv_o, jt_p, jt_s = [], [], [], []
    for d in range(ndir):
        vsu = jnp.where(up, vsa[d], vsb[d])
        dvp = vpa[d] - vpb[d]
        jv_w.append(td_w * vsu + tl_w * dvp)
        jv_o.append(td_o * vsu + tl_o * dvp)
        dww = wwa[d] - wwb[d]
        dwo = woa[d] - wob[d]
        jt_p.append(dww * tl_w + dwo * tl_o)
        jt_s.append(dww * td_w + dwo * td_o)
    zero = jnp.zeros_like(su)
    as_a = [f_w, f_o] + jv_w + jv_o + jt_p + [jnp.where(up, g, zero) for g in jt_s]
    as_b = [-f_w, -f_o] + [-x for x in jv_w] + [-x for x in jv_o] + [-x for x in jt_p]
    as_b = as_b + [jnp.where(up, zero, g) for g in jt_s]
    return as_a, as_b


def stencil_kernel(
    edge_ref,
    p_ref,
    s_ref,
    so_ref,
    pore_ref,
    tx_ref,
    ty_ref,
    tz_ref,
    ux_ref,
    uy_ref,
    uz_ref,
    d_ref,
    w_ref,
    hxl_ref,
    hxr_ref,
    hyd_ref,
    hyu_ref,
    r_out,
    jv_out,
    jt_out,
):
    ndir = d_ref.shape[0]
    layers, rows, cols = p_ref.shape
    lane = lax.broadcasted_iota(jnp.int32, (rows, cols), 1)
    sub = lax.broadcasted_iota(jnp.int32, (rows, cols), 0)
    first_lane = lane == 0
    last_lane = lane == cols - 1
    first_sub = sub == 0
    last_sub = sub == rows - 1
    cut_x = jnp.logical_and(last_lane, edge_ref[0] == 1)
    cut_y = jnp.logical_and(last_sub, edge_ref[1] == 1)
    nf = 2 + 4 * ndir

    def cells(k):
        out = [p_ref[k], s_ref[k]]
        for half in range(2):
            out += [d_ref[d, half, k] for d in range(ndir)]
        for half in range(2):
            out += [w_ref[d, half, k] for d in range(ndir)]
        return out

    def group(flat):
        return (
            flat[0],
            flat[1],
            flat[2 : 2 + ndir],
            flat[2 + ndir : 2 + 2 * ndir],
            flat[2 + 2 * ndir : 2 + 3 * ndir],
            flat[2 + 3 * ndir : 2 + 4 * ndir],
        )

    def col(ref, k, f):
        return jnp.broadcast_to(ref[k, :, pl.ds(f, 1)], (rows, cols))

    def row(ref, k, f):
        return jnp.broadcast_to(ref[k, pl.ds(f, 1), :], (rows, cols))

    def store(k, vals, add_prev):
        for i in range(nf):
            if i < 2:
                ref, idx = r_out, (i, k)
            elif i < 2 + 2 * ndir:
                j = i - 2
                ref, idx = jv_out, (j % ndir, j // ndir, k)
            else:
                j = i - 2 - 2 * ndir
                ref, idx = jt_out, (j % ndir, j // ndir, k)
            if add_prev:
                ref[idx] = ref[idx] + vals[i]
            else:
                ref[idx] = vals[i]

    def body(k, carry):
        here = cells(k)
        kn = jnp.minimum(k + 1, layers - 1)
        above = cells(kn)
        left = [jnp.where(first_lane, col(hxl_ref, k, f), pltpu.roll(x, 1, 1)) for f, x in enumerate(here)]
        right = [jnp.where(last_lane, col(hxr_ref, k, f), pltpu.roll(x, cols - 1, 1)) for f, x in enumerate(here)]
        down = [jnp.where(first_sub, row(hyd_ref, k, f), pltpu.roll(x, 1, 0)) for f, x in enumerate(here)]
        up_ = [jnp.where(last_sub, row(hyu_ref, k, f), pltpu.roll(x, rows - 1, 0)) for f, x in enumerate(here)]

        tx = tx_ref[k]
        ux = ux_ref[k].astype(jnp.float32)
        ty = ty_ref[k]
        uy = uy_ref[k].astype(jnp.float32)
        tx_f = jnp.where(cut_x, 0.0, tx)
        ty_f = jnp.where(cut_y, 0.0, ty)
        tx_b = jnp.where(first_lane, col(hxl_ref, k, nf), pltpu.roll(tx, 1, 1))
        ux_b = jnp.where(first_lane, col(hxl_ref, k, nf + 1), pltpu.roll(ux, 1, 1))
        ty_b = jnp.where(first_sub, row(hyd_ref, k, nf), pltpu.roll(ty, 1, 0))
        uy_b = jnp.where(first_sub, row(hyd_ref, k, nf + 1), pltpu.roll(uy, 1, 0))
        tz = jnp.where(k < layers - 1, tz_ref[k], 0.0)
        uz = uz_ref[k] == 1

        g_here = group(here)
        acc, _ = face_terms(tx_f, ux > 0.5, g_here, group(right), (0.0, 0.0), ndir)
        _, xb = face_terms(tx_b, ux_b > 0.5, group(left), g_here, (0.0, 0.0), ndir)
        yf, _ = face_terms(ty_f, uy > 0.5, g_here, group(up_), (0.0, 0.0), ndir)
        _, yb = face_terms(ty_b, uy_b > 0.5, group(down), g_here, (0.0, 0.0), ndir)
        zf, zb = face_terms(tz, uz, g_here, group(above), (water_head, oil_head), ndir)
        acc = [a + b + c + e for a, b, c, e in zip(acc, xb, yf, yb)]
        acc = [a + z for a, z in zip(acc, zf)]

        change = here[1] - so_ref[k]
        pore = pore_ref[k]
        acc[0] = acc[0] + pore * change
        acc[1] = acc[1] - pore * change
        for d in range(ndir):
            vs = here[2 + ndir + d]
            acc[2 + d] = acc[2 + d] + pore * vs
            acc[2 + ndir + d] = acc[2 + ndir + d] - pore * vs
            jt_s = 2 + 3 * ndir + d
            acc[jt_s] = acc[jt_s] + pore * (here[2 + 2 * ndir + d] - here[2 + 3 * ndir + d])
        acc = [a + c for a, c in zip(acc, carry)]
        store(k, acc, False)
        return tuple(zb)

    zero = jnp.zeros((rows, cols), jnp.float32)
    lax.fori_loop(0, layers, body, tuple([zero] * nf))


def body(
    pressure,
    saturation,
    sat_old,
    pore,
    trans_x,
    trans_y,
    trans_z,
    upwind_x,
    upwind_y,
    upwind_z,
    directions,
    adjoint_weights,
    perf_well,
    perf_col,
    perf_top,
    perf_span,
    perf_index,
    bhp,
    target,
):
    layers, rows, cols = pressure.shape
    spatial = (layers, rows, cols)
    ndir = directions.shape[0]
    last_x = lax.axis_index("gx") == lax.axis_size("gx") - 1
    last_y = lax.axis_index(GY_WA) == lax.axis_size(GY_WA) - 1
    edge = jnp.stack([last_x, last_y]).astype(jnp.int32)

    lane_hit = (jnp.arange(cols)[:, None] == (perf_col % cols)[None, :]).astype(jnp.float32)
    row_hit = (jnp.arange(rows)[:, None] == (perf_col // cols)[None, :]).astype(jnp.float32)

    def at_perfs(field):
        by_lane = jnp.dot(field, lane_hit, precision=lax.Precision.HIGHEST)
        return jnp.sum(by_lane * row_hit, axis=-2)

    p_cells = at_perfs(pressure)
    s_cells = at_perfs(saturation)
    dir_cells = at_perfs(directions)
    wts_cells = at_perfs(adjoint_weights)
    depth = jnp.arange(layers)[:, None]
    open_layer = jnp.logical_and(
        depth >= perf_top[None, :], depth < (perf_top + perf_span)[None, :]
    )
    weight = jnp.where(open_layer, perf_index[None, :], 0.0)
    row_bhp = jnp.take(bhp, perf_well)
    drive = p_cells - row_bhp
    mob = mobility(s_cells)
    slope = mobility_slope(s_cells)
    mob_total = mob[0] + mob[1]
    slope_total = slope[0] + slope[1]
    rates = weight * mob * drive
    rate_tangent = weight * (mob * dir_cells[:, 0:1] + slope * drive * dir_cells[:, 1:2])
    grad_p = weight * (mob[0] * wts_cells[:, 0] + mob[1] * wts_cells[:, 1])
    grad_s = weight * drive * (slope[0] * wts_cells[:, 0] + slope[1] * wts_cells[:, 1])
    row_sums = jnp.concatenate(
        [
            jnp.sum(weight * mob_total, axis=0)[None],
            jnp.sum(rates[0] + rates[1], axis=0)[None],
            jnp.sum(rate_tangent[:, 0] + rate_tangent[:, 1], axis=1),
            jnp.sum(grad_p, axis=1),
        ],
        axis=0,
    )
    packed = jnp.concatenate([row_sums, perf_well.astype(jnp.float32)[None]], axis=0)
    everyone = gather_everywhere(packed)

    cell_fields = [pressure, saturation] + [directions[d, h] for h in range(2) for d in range(ndir)]
    cell_fields += [adjoint_weights[d, h] for h in range(2) for d in range(ndir)]
    x_low = jnp.stack(
        [f[:, :, cols - 1] for f in cell_fields]
        + [trans_x[:, :, cols - 1], upwind_x[:, :, cols - 1].astype(jnp.float32)],
        axis=-1,
    )
    x_high = jnp.stack([f[:, :, 0] for f in cell_fields], axis=-1)
    y_low = jnp.stack(
        [f[:, rows - 1, :] for f in cell_fields]
        + [trans_y[:, rows - 1, :], upwind_y[:, rows - 1, :].astype(jnp.float32)],
        axis=1,
    )
    y_high = jnp.stack([f[:, 0, :] for f in cell_fields], axis=1)
    hxl = shift_along(x_low, "gx", True)
    hxr = shift_along(x_high, "gx", False)
    hyd = shift_along(y_low, GY_WA, True)
    hyu = shift_along(y_high, GY_WA, False)

    nf = 2 + 4 * ndir
    vmem = pl.BlockSpec(memory_space=pltpu.VMEM)
    flux_r, flux_jv, flux_jt = pl.pallas_call(
        stencil_kernel,
        out_shape=[
            jax.ShapeDtypeStruct((2,) + spatial, jnp.float32),
            jax.ShapeDtypeStruct((ndir, 2) + spatial, jnp.float32),
            jax.ShapeDtypeStruct((ndir, 2) + spatial, jnp.float32),
        ],
        in_specs=[pl.BlockSpec(memory_space=pltpu.SMEM)] + [vmem] * 16,
        out_specs=[vmem] * 3,
        cost_estimate=pl.CostEstimate(
            flops=layers * rows * cols * 1200,
            transcendentals=0,
            bytes_accessed=(10 + 4 * 4 * ndir + 2 + 2 * 2 * ndir) * layers * rows * cols * 4,
        ),
    )(
        edge,
        pressure,
        saturation,
        sat_old,
        pore,
        trans_x,
        trans_y,
        trans_z,
        upwind_x,
        upwind_y,
        upwind_z,
        directions,
        adjoint_weights,
        hxl,
        hxr,
        hyd,
        hyu,
    )

    all_sums = jnp.moveaxis(everyone[:, :-1], 1, 0).reshape(row_sums.shape[0], -1)
    all_wells = everyone[:, -1].reshape(-1)
    same_well = (perf_well.astype(jnp.float32)[:, None] == all_wells[None, :]).astype(jnp.float32)
    row_totals = jnp.dot(all_sums, same_well.T, precision=lax.Precision.HIGHEST)
    row_target = jnp.take(target, perf_well)
    row_factors = well_factors(row_totals, row_target)
    wells_res = rates - weight * mob * row_factors[0]
    wells_fwd = rate_tangent - (weight * mob)[None] * row_factors[1 : 1 + ndir][:, None, None, :]
    out_f = row_factors[1 + ndir :][:, None, :]
    wells_adj = jnp.stack(
        [grad_p - weight * mob_total * out_f, grad_s - weight * slope_total * drive * out_f], axis=1
    )
    combined = jnp.concatenate([wells_res[None], wells_fwd, wells_adj], axis=0)
    by_row = combined[..., None, :] * row_hit
    spread = jnp.dot(by_row, lane_hit.T, precision=lax.Precision.HIGHEST)
    reduced_residual = flux_r + spread[0]
    forward_products = flux_jv + spread[1 : 1 + ndir]
    adjoint_products = flux_jt + spread[1 + ndir :]
    return (reduced_residual, forward_products, adjoint_products)


def solution(mesh):
    split = Mesh(
        mesh.devices.reshape(mesh.shape["gx"], 4, 4, mesh.shape["wa"]), ("gx", "gy_0", "gy_1", "wa")
    )
    return jax.shard_map(
        body,
        mesh=split,
        in_specs=(
            P(None, GY_WA, "gx"),
            P(None, GY_WA, "gx"),
            P(None, GY_WA, "gx"),
            P(None, GY_WA, "gx"),
            P(None, GY_WA, "gx"),
            P(None, GY_WA, "gx"),
            P(None, GY_WA, "gx"),
            P(None, GY_WA, "gx"),
            P(None, GY_WA, "gx"),
            P(None, GY_WA, "gx"),
            P(None, None, None, GY_WA, "gx"),
            P(None, None, None, GY_WA, "gx"),
            P(GX_GY_WA),
            P(GX_GY_WA),
            P(GX_GY_WA),
            P(GX_GY_WA),
            P(GX_GY_WA),
            P(),
            P(),
        ),
        out_specs=(
            P(None, None, GY_WA, "gx"),
            P(None, None, None, GY_WA, "gx"),
            P(None, None, None, GY_WA, "gx"),
        ),
        check_vma=False,
    )
```

```python
import jax
import jax.numpy as jnp
from jax import lax
from jax.experimental import pallas as pl
from jax.experimental.pallas import tpu as pltpu
from jax.sharding import Mesh
from jax.sharding import PartitionSpec as P

GY_WA = ("gy_0", "gy_1", "wa")
GX_GY_WA = ("gx", "gy_0", "gy_1", "wa")


water_visc = 0.5
oil_visc = 2.0
water_head = 0.3
oil_head = 0.2


def gather_everywhere(block):
    held = block[None]
    for axis in ("wa", "gx", "gy_1", "gy_0"):
        size = lax.axis_size(axis)
        step = 1
        while step < size:
            other = lax.ppermute(held, axis, [(i, i ^ step) for i in range(size)])
            held = jnp.concatenate([held, other], axis=0)
            step *= 2
    return held


def shift_along(block, axis, down):
    size = lax.axis_size(axis)
    pairs = [(i, i + 1) for i in range(size - 1)]
    if not down:
        pairs = [(b, a) for a, b in pairs]
    return lax.ppermute(block, axis, pairs)


def mobility(sat):
    return jnp.stack([sat * sat / water_visc, (1.0 - sat) * (1.0 - sat) / oil_visc])


def mobility_slope(sat):
    return jnp.stack([2.0 * sat / water_visc, -2.0 * (1.0 - sat) / oil_visc])


def well_factors(sums, goal):
    return jnp.concatenate([((sums[1] - goal) / sums[0])[None], sums[2:] / sums[0][None]], axis=0)


def face_terms(trans, up, a, b, heads, ndir):
    pa, sa, vpa, vsa, wwa, woa = a
    pb, sb, vpb, vsb, wwb, wob = b
    su = jnp.where(up, sa, sb)
    drop = pa - pb
    pot_w = drop + heads[0]
    pot_o = drop + heads[1]
    tl_w = trans * (su * su / water_visc)
    tl_o = trans * ((1.0 - su) * (1.0 - su) / oil_visc)
    f_w = tl_w * pot_w
    f_o = tl_o * pot_o
    td_w = trans * (2.0 * su / water_visc) * pot_w
    td_o = trans * (-2.0 * (1.0 - su) / oil_visc) * pot_o
    jv_w, jv_o, jt_p, jt_s = [], [], [], []
    for d in range(ndir):
        vsu = jnp.where(up, vsa[d], vsb[d])
        dvp = vpa[d] - vpb[d]
        jv_w.append(td_w * vsu + tl_w * dvp)
        jv_o.append(td_o * vsu + tl_o * dvp)
        dww = wwa[d] - wwb[d]
        dwo = woa[d] - wob[d]
        jt_p.append(dww * tl_w + dwo * tl_o)
        jt_s.append(dww * td_w + dwo * td_o)
    zero = jnp.zeros_like(su)
    as_a = [f_w, f_o] + jv_w + jv_o + jt_p + [jnp.where(up, g, zero) for g in jt_s]
    as_b = [-f_w, -f_o] + [-x for x in jv_w] + [-x for x in jv_o] + [-x for x in jt_p]
    as_b = as_b + [jnp.where(up, zero, g) for g in jt_s]
    return as_a, as_b


def pack_kernel(p_ref, s_ref, d_ref, w_ref, tx_ref, ux_ref, ty_ref, uy_ref, xl_ref, xr_ref, yd_ref, yu_ref):
    ndir = d_ref.shape[0]
    layers, rows, cols = p_ref.shape
    lane = lax.broadcasted_iota(jnp.int32, (rows, cols), 1)
    sub = lax.broadcasted_iota(jnp.int32, (rows, cols), 0)
    nf = 2 + 4 * ndir

    def rolled(x, shift, axis):
        return x if shift == 0 else pltpu.roll(x, shift, axis)

    def rows_into(ref, k, tiles, source_row):
        count = len(tiles)
        for start in range(0, count, rows):
            acc = jnp.zeros((rows, cols), jnp.float32)
            for f in range(start, min(start + rows, count)):
                r = f - start
                acc = jnp.where(sub == r, rolled(tiles[f], (r - source_row) % rows, 0), acc)
            n = min(rows, count - start)
            ref[k, pl.ds(start, n), :] = acc[:n]

    def body(k, carry):
        cells = [p_ref[k], s_ref[k]]
        for half in range(2):
            cells += [d_ref[d, half, k] for d in range(ndir)]
        for half in range(2):
            cells += [w_ref[d, half, k] for d in range(ndir)]
        low_x = cells + [tx_ref[k], ux_ref[k].astype(jnp.float32)]
        low_y = cells + [ty_ref[k], uy_ref[k].astype(jnp.float32)]
        xl = jnp.zeros((rows, cols), jnp.float32)
        for f, t in enumerate(low_x):
            xl = jnp.where(lane == f, rolled(t, (f - (cols - 1)) % cols, 1), xl)
        xr = jnp.zeros((rows, cols), jnp.float32)
        for f, t in enumerate(cells):
            xr = jnp.where(lane == f, rolled(t, f % cols, 1), xr)
        xl_ref[k] = xl[:, : nf + 2]
        xr_ref[k] = xr[:, :nf]
        rows_into(yd_ref, k, low_y, rows - 1)
        rows_into(yu_ref, k, cells, 0)
        return carry

    lax.fori_loop(0, layers, body, 0)


def stencil_kernel(
    edge_ref,
    p_ref,
    s_ref,
    so_ref,
    pore_ref,
    tx_ref,
    ty_ref,
    tz_ref,
    ux_ref,
    uy_ref,
    uz_ref,
    d_ref,
    w_ref,
    hxl_ref,
    hxr_ref,
    hyd_ref,
    hyu_ref,
    spread_ref,
    r_out,
    jv_out,
    jt_out,
):
    ndir = d_ref.shape[0]
    layers, rows, cols = p_ref.shape
    lane = lax.broadcasted_iota(jnp.int32, (rows, cols), 1)
    sub = lax.broadcasted_iota(jnp.int32, (rows, cols), 0)
    first_lane = lane == 0
    last_lane = lane == cols - 1
    first_sub = sub == 0
    last_sub = sub == rows - 1
    cut_x = jnp.logical_and(last_lane, edge_ref[0] == 1)
    cut_y = jnp.logical_and(last_sub, edge_ref[1] == 1)
    nf = 2 + 4 * ndir

    def cells(k):
        out = [p_ref[k], s_ref[k]]
        for half in range(2):
            out += [d_ref[d, half, k] for d in range(ndir)]
        for half in range(2):
            out += [w_ref[d, half, k] for d in range(ndir)]
        return out

    def group(flat):
        return (
            flat[0],
            flat[1],
            flat[2 : 2 + ndir],
            flat[2 + ndir : 2 + 2 * ndir],
            flat[2 + 2 * ndir : 2 + 3 * ndir],
            flat[2 + 3 * ndir : 2 + 4 * ndir],
        )

    def col(ref, k, f):
        return jnp.broadcast_to(ref[k, :, pl.ds(f, 1)], (rows, cols))

    def row(ref, k, f):
        return jnp.broadcast_to(ref[k, pl.ds(f, 1), :], (rows, cols))

    def store(k, vals):
        for i in range(nf):
            if i < 2:
                ref, idx, extra = r_out, (i, k), (0, i, k)
            elif i < 2 + 2 * ndir:
                j = i - 2
                ref, idx, extra = jv_out, (j % ndir, j // ndir, k), (1 + j % ndir, j // ndir, k)
            else:
                j = i - 2 - 2 * ndir
                ref, idx, extra = jt_out, (j % ndir, j // ndir, k), (1 + ndir + j % ndir, j // ndir, k)
            ref[idx] = vals[i] + spread_ref[extra]

    def body(k, carry):
        here = cells(k)
        kn = jnp.minimum(k + 1, layers - 1)
        above = cells(kn)
        left = [jnp.where(first_lane, col(hxl_ref, k, f), pltpu.roll(x, 1, 1)) for f, x in enumerate(here)]
        right = [jnp.where(last_lane, col(hxr_ref, k, f), pltpu.roll(x, cols - 1, 1)) for f, x in enumerate(here)]
        down = [jnp.where(first_sub, row(hyd_ref, k, f), pltpu.roll(x, 1, 0)) for f, x in enumerate(here)]
        up_ = [jnp.where(last_sub, row(hyu_ref, k, f), pltpu.roll(x, rows - 1, 0)) for f, x in enumerate(here)]

        tx = tx_ref[k]
        ux = ux_ref[k].astype(jnp.float32)
        ty = ty_ref[k]
        uy = uy_ref[k].astype(jnp.float32)
        tx_f = jnp.where(cut_x, 0.0, tx)
        ty_f = jnp.where(cut_y, 0.0, ty)
        tx_b = jnp.where(first_lane, col(hxl_ref, k, nf), pltpu.roll(tx, 1, 1))
        ux_b = jnp.where(first_lane, col(hxl_ref, k, nf + 1), pltpu.roll(ux, 1, 1))
        ty_b = jnp.where(first_sub, row(hyd_ref, k, nf), pltpu.roll(ty, 1, 0))
        uy_b = jnp.where(first_sub, row(hyd_ref, k, nf + 1), pltpu.roll(uy, 1, 0))
        tz = jnp.where(k < layers - 1, tz_ref[k], 0.0)
        uz = uz_ref[k] == 1

        g_here = group(here)
        acc, _ = face_terms(tx_f, ux > 0.5, g_here, group(right), (0.0, 0.0), ndir)
        _, xb = face_terms(tx_b, ux_b > 0.5, group(left), g_here, (0.0, 0.0), ndir)
        yf, _ = face_terms(ty_f, uy > 0.5, g_here, group(up_), (0.0, 0.0), ndir)
        _, yb = face_terms(ty_b, uy_b > 0.5, group(down), g_here, (0.0, 0.0), ndir)
        zf, zb = face_terms(tz, uz, g_here, group(above), (water_head, oil_head), ndir)
        acc = [a + b + c + e for a, b, c, e in zip(acc, xb, yf, yb)]
        acc = [a + z for a, z in zip(acc, zf)]

        change = here[1] - so_ref[k]
        pore = pore_ref[k]
        acc[0] = acc[0] + pore * change
        acc[1] = acc[1] - pore * change
        for d in range(ndir):
            vs = here[2 + ndir + d]
            acc[2 + d] = acc[2 + d] + pore * vs
            acc[2 + ndir + d] = acc[2 + ndir + d] - pore * vs
            jt_s = 2 + 3 * ndir + d
            acc[jt_s] = acc[jt_s] + pore * (here[2 + 2 * ndir + d] - here[2 + 3 * ndir + d])
        acc = [a + c for a, c in zip(acc, carry)]
        store(k, acc)
        return tuple(zb)

    zero = jnp.zeros((rows, cols), jnp.float32)
    lax.fori_loop(0, layers, body, tuple([zero] * nf))


def body(
    pressure,
    saturation,
    sat_old,
    pore,
    trans_x,
    trans_y,
    trans_z,
    upwind_x,
    upwind_y,
    upwind_z,
    directions,
    adjoint_weights,
    perf_well,
    perf_col,
    perf_top,
    perf_span,
    perf_index,
    bhp,
    target,
):
    layers, rows, cols = pressure.shape
    spatial = (layers, rows, cols)
    ndir = directions.shape[0]
    last_x = lax.axis_index("gx") == lax.axis_size("gx") - 1
    last_y = lax.axis_index(GY_WA) == lax.axis_size(GY_WA) - 1
    edge = jnp.stack([last_x, last_y]).astype(jnp.int32)

    lane_hit = (jnp.arange(cols)[:, None] == (perf_col % cols)[None, :]).astype(jnp.float32)
    row_hit = (jnp.arange(rows)[:, None] == (perf_col // cols)[None, :]).astype(jnp.float32)

    def at_perfs(field):
        by_lane = jnp.dot(field, lane_hit, precision=lax.Precision.HIGHEST)
        return jnp.sum(by_lane * row_hit, axis=-2)

    p_cells = at_perfs(pressure)
    s_cells = at_perfs(saturation)
    dir_cells = at_perfs(directions)
    wts_cells = at_perfs(adjoint_weights)
    depth = jnp.arange(layers)[:, None]
    open_layer = jnp.logical_and(
        depth >= perf_top[None, :], depth < (perf_top + perf_span)[None, :]
    )
    weight = jnp.where(open_layer, perf_index[None, :], 0.0)
    row_bhp = jnp.take(bhp, perf_well)
    drive = p_cells - row_bhp
    mob = mobility(s_cells)
    slope = mobility_slope(s_cells)
    mob_total = mob[0] + mob[1]
    slope_total = slope[0] + slope[1]
    rates = weight * mob * drive
    rate_tangent = weight * (mob * dir_cells[:, 0:1] + slope * drive * dir_cells[:, 1:2])
    grad_p = weight * (mob[0] * wts_cells[:, 0] + mob[1] * wts_cells[:, 1])
    grad_s = weight * drive * (slope[0] * wts_cells[:, 0] + slope[1] * wts_cells[:, 1])
    row_sums = jnp.concatenate(
        [
            jnp.sum(weight * mob_total, axis=0)[None],
            jnp.sum(rates[0] + rates[1], axis=0)[None],
            jnp.sum(rate_tangent[:, 0] + rate_tangent[:, 1], axis=1),
            jnp.sum(grad_p, axis=1),
        ],
        axis=0,
    )
    packed = jnp.concatenate([row_sums, perf_well.astype(jnp.float32)[None]], axis=0)
    everyone = gather_everywhere(packed)

    nf = 2 + 4 * ndir
    vmem = pl.BlockSpec(memory_space=pltpu.VMEM)
    x_low, x_high, y_low, y_high = pl.pallas_call(
        pack_kernel,
        out_shape=[
            jax.ShapeDtypeStruct((layers, rows, nf + 2), jnp.float32),
            jax.ShapeDtypeStruct((layers, rows, nf), jnp.float32),
            jax.ShapeDtypeStruct((layers, nf + 2, cols), jnp.float32),
            jax.ShapeDtypeStruct((layers, nf, cols), jnp.float32),
        ],
        in_specs=[vmem] * 8,
        out_specs=[vmem] * 4,
        cost_estimate=pl.CostEstimate(
            flops=layers * rows * cols * 160,
            transcendentals=0,
            bytes_accessed=(6 + 4 * ndir) * layers * rows * cols * 4,
        ),
    )(pressure, saturation, directions, adjoint_weights, trans_x, upwind_x, trans_y, upwind_y)
    hxl = shift_along(x_low, "gx", True)
    hxr = shift_along(x_high, "gx", False)
    hyd = shift_along(y_low, GY_WA, True)
    hyu = shift_along(y_high, GY_WA, False)

    all_sums = jnp.moveaxis(everyone[:, :-1], 1, 0).reshape(row_sums.shape[0], -1)
    all_wells = everyone[:, -1].reshape(-1)
    same_well = (perf_well.astype(jnp.float32)[:, None] == all_wells[None, :]).astype(jnp.float32)
    row_totals = jnp.dot(all_sums, same_well.T, precision=lax.Precision.HIGHEST)
    row_target = jnp.take(target, perf_well)
    row_factors = well_factors(row_totals, row_target)
    wells_res = rates - weight * mob * row_factors[0]
    wells_fwd = rate_tangent - (weight * mob)[None] * row_factors[1 : 1 + ndir][:, None, None, :]
    out_f = row_factors[1 + ndir :][:, None, :]
    wells_adj = jnp.stack(
        [grad_p - weight * mob_total * out_f, grad_s - weight * slope_total * drive * out_f], axis=1
    )
    combined = jnp.concatenate([wells_res[None], wells_fwd, wells_adj], axis=0)
    by_row = combined[..., None, :] * row_hit
    spread = jnp.dot(by_row, lane_hit.T, precision=lax.Precision.HIGHEST)

    reduced_residual, forward_products, adjoint_products = pl.pallas_call(
        stencil_kernel,
        out_shape=[
            jax.ShapeDtypeStruct((2,) + spatial, jnp.float32),
            jax.ShapeDtypeStruct((ndir, 2) + spatial, jnp.float32),
            jax.ShapeDtypeStruct((ndir, 2) + spatial, jnp.float32),
        ],
        in_specs=[pl.BlockSpec(memory_space=pltpu.SMEM)] + [vmem] * 17,
        out_specs=[vmem] * 3,
        cost_estimate=pl.CostEstimate(
            flops=layers * rows * cols * 1200,
            transcendentals=0,
            bytes_accessed=(10 + 4 * 4 * ndir + 2 + 2 * 2 * ndir) * layers * rows * cols * 4,
        ),
    )(
        edge,
        pressure,
        saturation,
        sat_old,
        pore,
        trans_x,
        trans_y,
        trans_z,
        upwind_x,
        upwind_y,
        upwind_z,
        directions,
        adjoint_weights,
        hxl,
        hxr,
        hyd,
        hyu,
        spread,
    )
    return (reduced_residual, forward_products, adjoint_products)


def solution(mesh):
    split = Mesh(
        mesh.devices.reshape(mesh.shape["gx"], 4, 4, mesh.shape["wa"]), ("gx", "gy_0", "gy_1", "wa")
    )
    return jax.shard_map(
        body,
        mesh=split,
        in_specs=(
            P(None, GY_WA, "gx"),
            P(None, GY_WA, "gx"),
            P(None, GY_WA, "gx"),
            P(None, GY_WA, "gx"),
            P(None, GY_WA, "gx"),
            P(None, GY_WA, "gx"),
            P(None, GY_WA, "gx"),
            P(None, GY_WA, "gx"),
            P(None, GY_WA, "gx"),
            P(None, GY_WA, "gx"),
            P(None, None, None, GY_WA, "gx"),
            P(None, None, None, GY_WA, "gx"),
            P(GX_GY_WA),
            P(GX_GY_WA),
            P(GX_GY_WA),
            P(GX_GY_WA),
            P(GX_GY_WA),
            P(),
            P(),
        ),
        out_specs=(
            P(None, None, GY_WA, "gx"),
            P(None, None, None, GY_WA, "gx"),
            P(None, None, None, GY_WA, "gx"),
        ),
        check_vma=False,
    )
```

```python
import jax
import jax.numpy as jnp
from jax import lax
from jax.experimental import pallas as pl
from jax.experimental.pallas import tpu as pltpu
from jax.sharding import Mesh
from jax.sharding import PartitionSpec as P

GY_WA = ("gy_0", "gy_1", "wa")
GX_GY_WA = ("gx", "gy_0", "gy_1", "wa")


water_visc = 0.5
oil_visc = 2.0
water_head = 0.3
oil_head = 0.2


def gather_everywhere(block):
    held = block[None]
    for axis in ("wa", "gx", "gy_1", "gy_0"):
        size = lax.axis_size(axis)
        step = 1
        while step < size:
            other = lax.ppermute(held, axis, [(i, i ^ step) for i in range(size)])
            held = jnp.concatenate([held, other], axis=0)
            step *= 2
    return held


def shift_along(block, axis, down):
    size = lax.axis_size(axis)
    pairs = [(i, i + 1) for i in range(size - 1)]
    if not down:
        pairs = [(b, a) for a, b in pairs]
    return lax.ppermute(block, axis, pairs)


def mobility(sat):
    return jnp.stack([sat * sat / water_visc, (1.0 - sat) * (1.0 - sat) / oil_visc])


def mobility_slope(sat):
    return jnp.stack([2.0 * sat / water_visc, -2.0 * (1.0 - sat) / oil_visc])


def well_factors(sums, goal):
    return jnp.concatenate([((sums[1] - goal) / sums[0])[None], sums[2:] / sums[0][None]], axis=0)


def face_terms(trans, up, a, b, heads, ndir):
    pa, sa, vpa, vsa, wwa, woa = a
    pb, sb, vpb, vsb, wwb, wob = b
    su = jnp.where(up, sa, sb)
    drop = pa - pb
    pot_w = drop + heads[0]
    pot_o = drop + heads[1]
    tl_w = trans * (su * su / water_visc)
    tl_o = trans * ((1.0 - su) * (1.0 - su) / oil_visc)
    f_w = tl_w * pot_w
    f_o = tl_o * pot_o
    td_w = trans * (2.0 * su / water_visc) * pot_w
    td_o = trans * (-2.0 * (1.0 - su) / oil_visc) * pot_o
    jv_w, jv_o, jt_p, jt_s = [], [], [], []
    for d in range(ndir):
        vsu = jnp.where(up, vsa[d], vsb[d])
        dvp = vpa[d] - vpb[d]
        jv_w.append(td_w * vsu + tl_w * dvp)
        jv_o.append(td_o * vsu + tl_o * dvp)
        dww = wwa[d] - wwb[d]
        dwo = woa[d] - wob[d]
        jt_p.append(dww * tl_w + dwo * tl_o)
        jt_s.append(dww * td_w + dwo * td_o)
    zero = jnp.zeros_like(su)
    as_a = [f_w, f_o] + jv_w + jv_o + jt_p + [jnp.where(up, g, zero) for g in jt_s]
    as_b = [-f_w, -f_o] + [-x for x in jv_w] + [-x for x in jv_o] + [-x for x in jt_p]
    as_b = as_b + [jnp.where(up, zero, g) for g in jt_s]
    return as_a, as_b


def pack_kernel(p_ref, s_ref, d_ref, w_ref, tx_ref, ux_ref, ty_ref, uy_ref, xl_ref, xr_ref, yd_ref, yu_ref):
    ndir = d_ref.shape[0]
    layers, rows, cols = p_ref.shape
    lane = lax.broadcasted_iota(jnp.int32, (rows, cols), 1)
    sub = lax.broadcasted_iota(jnp.int32, (rows, cols), 0)
    nf = 2 + 4 * ndir

    def rolled(x, shift, axis):
        return x if shift == 0 else pltpu.roll(x, shift, axis)

    def rows_into(ref, k, tiles, source_row):
        count = len(tiles)
        for start in range(0, count, rows):
            acc = jnp.zeros((rows, cols), jnp.float32)
            for f in range(start, min(start + rows, count)):
                r = f - start
                acc = jnp.where(sub == r, rolled(tiles[f], (r - source_row) % rows, 0), acc)
            n = min(rows, count - start)
            ref[k, pl.ds(start, n), :] = acc[:n]

    def body(k, carry):
        cells = [p_ref[k], s_ref[k]]
        for half in range(2):
            cells += [d_ref[d, half, k] for d in range(ndir)]
        for half in range(2):
            cells += [w_ref[d, half, k] for d in range(ndir)]
        low_x = cells + [tx_ref[k], ux_ref[k].astype(jnp.float32)]
        low_y = cells + [ty_ref[k], uy_ref[k].astype(jnp.float32)]
        xl = jnp.zeros((rows, cols), jnp.float32)
        for f, t in enumerate(low_x):
            xl = jnp.where(lane == f, rolled(t, (f - (cols - 1)) % cols, 1), xl)
        xr = jnp.zeros((rows, cols), jnp.float32)
        for f, t in enumerate(cells):
            xr = jnp.where(lane == f, rolled(t, f % cols, 1), xr)
        xl_ref[k] = xl[:, : nf + 2]
        xr_ref[k] = xr[:, :nf]
        rows_into(yd_ref, k, low_y, rows - 1)
        rows_into(yu_ref, k, cells, 0)
        return carry

    lax.fori_loop(0, layers, body, 0)


def stencil_kernel(
    edge_ref,
    p_ref,
    s_ref,
    so_ref,
    pore_ref,
    tx_ref,
    ty_ref,
    tz_ref,
    ux_ref,
    uy_ref,
    uz_ref,
    d_ref,
    w_ref,
    hxl_ref,
    hxr_ref,
    hyd_ref,
    hyu_ref,
    spread_ref,
    r_out,
    jv_out,
    jt_out,
):
    ndir = d_ref.shape[0]
    layers, rows, cols = p_ref.shape
    lane = lax.broadcasted_iota(jnp.int32, (rows, cols), 1)
    sub = lax.broadcasted_iota(jnp.int32, (rows, cols), 0)
    first_lane = lane == 0
    last_lane = lane == cols - 1
    first_sub = sub == 0
    last_sub = sub == rows - 1
    cut_x = jnp.logical_and(last_lane, edge_ref[0] == 1)
    cut_y = jnp.logical_and(last_sub, edge_ref[1] == 1)
    nf = 2 + 4 * ndir

    def cells(k):
        out = [p_ref[k], s_ref[k]]
        for half in range(2):
            out += [d_ref[d, half, k] for d in range(ndir)]
        for half in range(2):
            out += [w_ref[d, half, k] for d in range(ndir)]
        return out

    def group(flat):
        return (
            flat[0],
            flat[1],
            flat[2 : 2 + ndir],
            flat[2 + ndir : 2 + 2 * ndir],
            flat[2 + 2 * ndir : 2 + 3 * ndir],
            flat[2 + 3 * ndir : 2 + 4 * ndir],
        )

    def col(ref, k, f):
        return jnp.broadcast_to(ref[k, :, pl.ds(f, 1)], (rows, cols))

    def row(ref, k, f):
        return jnp.broadcast_to(ref[k, pl.ds(f, 1), :], (rows, cols))

    def store(k, vals):
        for i in range(nf):
            if i < 2:
                ref, idx, extra = r_out, (i, k), (0, i, k)
            elif i < 2 + 2 * ndir:
                j = i - 2
                ref, idx, extra = jv_out, (j % ndir, j // ndir, k), (1 + j % ndir, j // ndir, k)
            else:
                j = i - 2 - 2 * ndir
                ref, idx, extra = jt_out, (j % ndir, j // ndir, k), (1 + ndir + j % ndir, j // ndir, k)
            ref[idx] = vals[i] + spread_ref[extra]

    def body(k, carry):
        here = cells(k)
        kn = jnp.minimum(k + 1, layers - 1)
        above = cells(kn)
        left = [jnp.where(first_lane, col(hxl_ref, k, f), pltpu.roll(x, 1, 1)) for f, x in enumerate(here)]
        right = [jnp.where(last_lane, col(hxr_ref, k, f), pltpu.roll(x, cols - 1, 1)) for f, x in enumerate(here)]
        down = [jnp.where(first_sub, row(hyd_ref, k, f), pltpu.roll(x, 1, 0)) for f, x in enumerate(here)]
        up_ = [jnp.where(last_sub, row(hyu_ref, k, f), pltpu.roll(x, rows - 1, 0)) for f, x in enumerate(here)]

        tx = tx_ref[k]
        ux = ux_ref[k].astype(jnp.float32)
        ty = ty_ref[k]
        uy = uy_ref[k].astype(jnp.float32)
        tx_f = jnp.where(cut_x, 0.0, tx)
        ty_f = jnp.where(cut_y, 0.0, ty)
        tx_b = jnp.where(first_lane, col(hxl_ref, k, nf), pltpu.roll(tx, 1, 1))
        ux_b = jnp.where(first_lane, col(hxl_ref, k, nf + 1), pltpu.roll(ux, 1, 1))
        ty_b = jnp.where(first_sub, row(hyd_ref, k, nf), pltpu.roll(ty, 1, 0))
        uy_b = jnp.where(first_sub, row(hyd_ref, k, nf + 1), pltpu.roll(uy, 1, 0))
        tz = jnp.where(k < layers - 1, tz_ref[k], 0.0)
        uz = uz_ref[k] == 1

        g_here = group(here)
        acc, _ = face_terms(tx_f, ux > 0.5, g_here, group(right), (0.0, 0.0), ndir)
        _, xb = face_terms(tx_b, ux_b > 0.5, group(left), g_here, (0.0, 0.0), ndir)
        yf, _ = face_terms(ty_f, uy > 0.5, g_here, group(up_), (0.0, 0.0), ndir)
        _, yb = face_terms(ty_b, uy_b > 0.5, group(down), g_here, (0.0, 0.0), ndir)
        zf, zb = face_terms(tz, uz, g_here, group(above), (water_head, oil_head), ndir)
        acc = [a + b + c + e for a, b, c, e in zip(acc, xb, yf, yb)]
        acc = [a + z for a, z in zip(acc, zf)]

        change = here[1] - so_ref[k]
        pore = pore_ref[k]
        acc[0] = acc[0] + pore * change
        acc[1] = acc[1] - pore * change
        for d in range(ndir):
            vs = here[2 + ndir + d]
            acc[2 + d] = acc[2 + d] + pore * vs
            acc[2 + ndir + d] = acc[2 + ndir + d] - pore * vs
            jt_s = 2 + 3 * ndir + d
            acc[jt_s] = acc[jt_s] + pore * (here[2 + 2 * ndir + d] - here[2 + 3 * ndir + d])
        acc = [a + c for a, c in zip(acc, carry)]
        store(k, acc)
        return tuple(zb)

    zero = jnp.zeros((rows, cols), jnp.float32)
    lax.fori_loop(0, layers, body, tuple([zero] * nf))


def body(
    pressure,
    saturation,
    sat_old,
    pore,
    trans_x,
    trans_y,
    trans_z,
    upwind_x,
    upwind_y,
    upwind_z,
    directions,
    adjoint_weights,
    perf_well,
    perf_col,
    perf_top,
    perf_span,
    perf_index,
    bhp,
    target,
):
    layers, rows, cols = pressure.shape
    spatial = (layers, rows, cols)
    ndir = directions.shape[0]
    last_x = lax.axis_index("gx") == lax.axis_size("gx") - 1
    last_y = lax.axis_index(GY_WA) == lax.axis_size(GY_WA) - 1
    edge = jnp.stack([last_x, last_y]).astype(jnp.int32)

    nf = 2 + 4 * ndir
    vmem = pl.BlockSpec(memory_space=pltpu.VMEM)
    x_low, x_high, y_low, y_high = pl.pallas_call(
        pack_kernel,
        out_shape=[
            jax.ShapeDtypeStruct((layers, rows, nf + 2), jnp.float32),
            jax.ShapeDtypeStruct((layers, rows, nf), jnp.float32),
            jax.ShapeDtypeStruct((layers, nf + 2, cols), jnp.float32),
            jax.ShapeDtypeStruct((layers, nf, cols), jnp.float32),
        ],
        in_specs=[vmem] * 8,
        out_specs=[vmem] * 4,
        cost_estimate=pl.CostEstimate(
            flops=layers * rows * cols * 160,
            transcendentals=0,
            bytes_accessed=(6 + 4 * ndir) * layers * rows * cols * 4,
        ),
    )(pressure, saturation, directions, adjoint_weights, trans_x, upwind_x, trans_y, upwind_y)
    x_low, x_high, y_low, y_high, pressure, saturation, directions, adjoint_weights = lax.optimization_barrier(
        (x_low, x_high, y_low, y_high, pressure, saturation, directions, adjoint_weights)
    )
    hxl = shift_along(x_low, "gx", True)
    hxr = shift_along(x_high, "gx", False)
    hyd = shift_along(y_low, GY_WA, True)
    hyu = shift_along(y_high, GY_WA, False)

    lane_hit = (jnp.arange(cols)[:, None] == (perf_col % cols)[None, :]).astype(jnp.float32)
    row_hit = (jnp.arange(rows)[:, None] == (perf_col // cols)[None, :]).astype(jnp.float32)

    def at_perfs(field):
        by_lane = jnp.dot(field, lane_hit, precision=lax.Precision.HIGHEST)
        return jnp.sum(by_lane * row_hit, axis=-2)

    p_cells = at_perfs(pressure)
    s_cells = at_perfs(saturation)
    dir_cells = at_perfs(directions)
    wts_cells = at_perfs(adjoint_weights)
    depth = jnp.arange(layers)[:, None]
    open_layer = jnp.logical_and(
        depth >= perf_top[None, :], depth < (perf_top + perf_span)[None, :]
    )
    weight = jnp.where(open_layer, perf_index[None, :], 0.0)
    row_bhp = jnp.take(bhp, perf_well)
    drive = p_cells - row_bhp
    mob = mobility(s_cells)
    slope = mobility_slope(s_cells)
    mob_total = mob[0] + mob[1]
    slope_total = slope[0] + slope[1]
    rates = weight * mob * drive
    rate_tangent = weight * (mob * dir_cells[:, 0:1] + slope * drive * dir_cells[:, 1:2])
    grad_p = weight * (mob[0] * wts_cells[:, 0] + mob[1] * wts_cells[:, 1])
    grad_s = weight * drive * (slope[0] * wts_cells[:, 0] + slope[1] * wts_cells[:, 1])
    row_sums = jnp.concatenate(
        [
            jnp.sum(weight * mob_total, axis=0)[None],
            jnp.sum(rates[0] + rates[1], axis=0)[None],
            jnp.sum(rate_tangent[:, 0] + rate_tangent[:, 1], axis=1),
            jnp.sum(grad_p, axis=1),
        ],
        axis=0,
    )
    packed = jnp.concatenate([row_sums, perf_well.astype(jnp.float32)[None]], axis=0)
    packed, hxl, hxr, hyd, hyu = lax.optimization_barrier((packed, hxl, hxr, hyd, hyu))
    everyone = gather_everywhere(packed)


    all_sums = jnp.moveaxis(everyone[:, :-1], 1, 0).reshape(row_sums.shape[0], -1)
    all_wells = everyone[:, -1].reshape(-1)
    same_well = (perf_well.astype(jnp.float32)[:, None] == all_wells[None, :]).astype(jnp.float32)
    row_totals = jnp.dot(all_sums, same_well.T, precision=lax.Precision.HIGHEST)
    row_target = jnp.take(target, perf_well)
    row_factors = well_factors(row_totals, row_target)
    wells_res = rates - weight * mob * row_factors[0]
    wells_fwd = rate_tangent - (weight * mob)[None] * row_factors[1 : 1 + ndir][:, None, None, :]
    out_f = row_factors[1 + ndir :][:, None, :]
    wells_adj = jnp.stack(
        [grad_p - weight * mob_total * out_f, grad_s - weight * slope_total * drive * out_f], axis=1
    )
    combined = jnp.concatenate([wells_res[None], wells_fwd, wells_adj], axis=0)
    by_row = combined[..., None, :] * row_hit
    spread = jnp.dot(by_row, lane_hit.T, precision=lax.Precision.HIGHEST)

    reduced_residual, forward_products, adjoint_products = pl.pallas_call(
        stencil_kernel,
        out_shape=[
            jax.ShapeDtypeStruct((2,) + spatial, jnp.float32),
            jax.ShapeDtypeStruct((ndir, 2) + spatial, jnp.float32),
            jax.ShapeDtypeStruct((ndir, 2) + spatial, jnp.float32),
        ],
        in_specs=[pl.BlockSpec(memory_space=pltpu.SMEM)] + [vmem] * 17,
        out_specs=[vmem] * 3,
        cost_estimate=pl.CostEstimate(
            flops=layers * rows * cols * 1200,
            transcendentals=0,
            bytes_accessed=(10 + 4 * 4 * ndir + 2 + 2 * 2 * ndir) * layers * rows * cols * 4,
        ),
    )(
        edge,
        pressure,
        saturation,
        sat_old,
        pore,
        trans_x,
        trans_y,
        trans_z,
        upwind_x,
        upwind_y,
        upwind_z,
        directions,
        adjoint_weights,
        hxl,
        hxr,
        hyd,
        hyu,
        spread,
    )
    return (reduced_residual, forward_products, adjoint_products)


def solution(mesh):
    split = Mesh(
        mesh.devices.reshape(mesh.shape["gx"], 4, 4, mesh.shape["wa"]), ("gx", "gy_0", "gy_1", "wa")
    )
    return jax.shard_map(
        body,
        mesh=split,
        in_specs=(
            P(None, GY_WA, "gx"),
            P(None, GY_WA, "gx"),
            P(None, GY_WA, "gx"),
            P(None, GY_WA, "gx"),
            P(None, GY_WA, "gx"),
            P(None, GY_WA, "gx"),
            P(None, GY_WA, "gx"),
            P(None, GY_WA, "gx"),
            P(None, GY_WA, "gx"),
            P(None, GY_WA, "gx"),
            P(None, None, None, GY_WA, "gx"),
            P(None, None, None, GY_WA, "gx"),
            P(GX_GY_WA),
            P(GX_GY_WA),
            P(GX_GY_WA),
            P(GX_GY_WA),
            P(GX_GY_WA),
            P(),
            P(),
        ),
        out_specs=(
            P(None, None, GY_WA, "gx"),
            P(None, None, None, GY_WA, "gx"),
            P(None, None, None, GY_WA, "gx"),
        ),
        check_vma=False,
    )
```

```python
import jax
import jax.numpy as jnp
from jax import lax
from jax.experimental import pallas as pl
from jax.experimental.pallas import tpu as pltpu
from jax.sharding import Mesh
from jax.sharding import PartitionSpec as P

GY_WA = ("gy_0", "gy_1", "wa")
GX_GY_WA = ("gx", "gy_0", "gy_1", "wa")


water_visc = 0.5
oil_visc = 2.0
water_head = 0.3
oil_head = 0.2


def gather_everywhere(block):
    peers = lax.axis_size(GX_GY_WA)
    return lax.all_to_all(jnp.broadcast_to(block[None], (peers,) + block.shape), GX_GY_WA, 0, 0)


def shift_along(block, axis, down):
    size = lax.axis_size(axis)
    pairs = [(i, i + 1) for i in range(size - 1)]
    if not down:
        pairs = [(b, a) for a, b in pairs]
    return lax.ppermute(block, axis, pairs)


def mobility(sat):
    return jnp.stack([sat * sat / water_visc, (1.0 - sat) * (1.0 - sat) / oil_visc])


def mobility_slope(sat):
    return jnp.stack([2.0 * sat / water_visc, -2.0 * (1.0 - sat) / oil_visc])


def well_factors(sums, goal):
    return jnp.concatenate([((sums[1] - goal) / sums[0])[None], sums[2:] / sums[0][None]], axis=0)


def face_terms(trans, up, a, b, heads, ndir):
    pa, sa, vpa, vsa, wwa, woa = a
    pb, sb, vpb, vsb, wwb, wob = b
    su = jnp.where(up, sa, sb)
    drop = pa - pb
    pot_w = drop + heads[0]
    pot_o = drop + heads[1]
    tl_w = trans * (su * su / water_visc)
    tl_o = trans * ((1.0 - su) * (1.0 - su) / oil_visc)
    f_w = tl_w * pot_w
    f_o = tl_o * pot_o
    td_w = trans * (2.0 * su / water_visc) * pot_w
    td_o = trans * (-2.0 * (1.0 - su) / oil_visc) * pot_o
    jv_w, jv_o, jt_p, jt_s = [], [], [], []
    for d in range(ndir):
        vsu = jnp.where(up, vsa[d], vsb[d])
        dvp = vpa[d] - vpb[d]
        jv_w.append(td_w * vsu + tl_w * dvp)
        jv_o.append(td_o * vsu + tl_o * dvp)
        dww = wwa[d] - wwb[d]
        dwo = woa[d] - wob[d]
        jt_p.append(dww * tl_w + dwo * tl_o)
        jt_s.append(dww * td_w + dwo * td_o)
    zero = jnp.zeros_like(su)
    as_a = [f_w, f_o] + jv_w + jv_o + jt_p + [jnp.where(up, g, zero) for g in jt_s]
    as_b = [-f_w, -f_o] + [-x for x in jv_w] + [-x for x in jv_o] + [-x for x in jt_p]
    as_b = as_b + [jnp.where(up, zero, g) for g in jt_s]
    return as_a, as_b


def pack_kernel(p_ref, s_ref, d_ref, w_ref, tx_ref, ux_ref, ty_ref, uy_ref, xl_ref, xr_ref, yd_ref, yu_ref):
    ndir = d_ref.shape[0]
    layers, rows, cols = p_ref.shape
    lane = lax.broadcasted_iota(jnp.int32, (rows, cols), 1)
    sub = lax.broadcasted_iota(jnp.int32, (rows, cols), 0)
    nf = 2 + 4 * ndir

    def rolled(x, shift, axis):
        return x if shift == 0 else pltpu.roll(x, shift, axis)

    def rows_into(ref, k, tiles, source_row):
        count = len(tiles)
        for start in range(0, count, rows):
            acc = jnp.zeros((rows, cols), jnp.float32)
            for f in range(start, min(start + rows, count)):
                r = f - start
                acc = jnp.where(sub == r, rolled(tiles[f], (r - source_row) % rows, 0), acc)
            n = min(rows, count - start)
            ref[k, pl.ds(start, n), :] = acc[:n]

    def body(k, carry):
        cells = [p_ref[k], s_ref[k]]
        for half in range(2):
            cells += [d_ref[d, half, k] for d in range(ndir)]
        for half in range(2):
            cells += [w_ref[d, half, k] for d in range(ndir)]
        low_x = cells + [tx_ref[k], ux_ref[k].astype(jnp.float32)]
        low_y = cells + [ty_ref[k], uy_ref[k].astype(jnp.float32)]
        xl = jnp.zeros((rows, cols), jnp.float32)
        for f, t in enumerate(low_x):
            xl = jnp.where(lane == f, rolled(t, (f - (cols - 1)) % cols, 1), xl)
        xr = jnp.zeros((rows, cols), jnp.float32)
        for f, t in enumerate(cells):
            xr = jnp.where(lane == f, rolled(t, f % cols, 1), xr)
        xl_ref[k] = xl[:, : nf + 2]
        xr_ref[k] = xr[:, :nf]
        rows_into(yd_ref, k, low_y, rows - 1)
        rows_into(yu_ref, k, cells, 0)
        return carry

    lax.fori_loop(0, layers, body, 0)


def stencil_kernel(
    edge_ref,
    p_ref,
    s_ref,
    so_ref,
    pore_ref,
    tx_ref,
    ty_ref,
    tz_ref,
    ux_ref,
    uy_ref,
    uz_ref,
    d_ref,
    w_ref,
    hxl_ref,
    hxr_ref,
    hyd_ref,
    hyu_ref,
    spread_ref,
    r_out,
    jv_out,
    jt_out,
):
    ndir = d_ref.shape[0]
    layers, rows, cols = p_ref.shape
    lane = lax.broadcasted_iota(jnp.int32, (rows, cols), 1)
    sub = lax.broadcasted_iota(jnp.int32, (rows, cols), 0)
    first_lane = lane == 0
    last_lane = lane == cols - 1
    first_sub = sub == 0
    last_sub = sub == rows - 1
    cut_x = jnp.logical_and(last_lane, edge_ref[0] == 1)
    cut_y = jnp.logical_and(last_sub, edge_ref[1] == 1)
    nf = 2 + 4 * ndir

    def cells(k):
        out = [p_ref[k], s_ref[k]]
        for half in range(2):
            out += [d_ref[d, half, k] for d in range(ndir)]
        for half in range(2):
            out += [w_ref[d, half, k] for d in range(ndir)]
        return out

    def group(flat):
        return (
            flat[0],
            flat[1],
            flat[2 : 2 + ndir],
            flat[2 + ndir : 2 + 2 * ndir],
            flat[2 + 2 * ndir : 2 + 3 * ndir],
            flat[2 + 3 * ndir : 2 + 4 * ndir],
        )

    def col(ref, k, f):
        return jnp.broadcast_to(ref[k, :, pl.ds(f, 1)], (rows, cols))

    def row(ref, k, f):
        return jnp.broadcast_to(ref[k, pl.ds(f, 1), :], (rows, cols))

    def store(k, vals):
        for i in range(nf):
            if i < 2:
                ref, idx, extra = r_out, (i, k), (0, i, k)
            elif i < 2 + 2 * ndir:
                j = i - 2
                ref, idx, extra = jv_out, (j % ndir, j // ndir, k), (1 + j % ndir, j // ndir, k)
            else:
                j = i - 2 - 2 * ndir
                ref, idx, extra = jt_out, (j % ndir, j // ndir, k), (1 + ndir + j % ndir, j // ndir, k)
            ref[idx] = vals[i] + spread_ref[extra]

    def body(k, carry):
        here = cells(k)
        kn = jnp.minimum(k + 1, layers - 1)
        above = cells(kn)
        left = [jnp.where(first_lane, col(hxl_ref, k, f), pltpu.roll(x, 1, 1)) for f, x in enumerate(here)]
        right = [jnp.where(last_lane, col(hxr_ref, k, f), pltpu.roll(x, cols - 1, 1)) for f, x in enumerate(here)]
        down = [jnp.where(first_sub, row(hyd_ref, k, f), pltpu.roll(x, 1, 0)) for f, x in enumerate(here)]
        up_ = [jnp.where(last_sub, row(hyu_ref, k, f), pltpu.roll(x, rows - 1, 0)) for f, x in enumerate(here)]

        tx = tx_ref[k]
        ux = ux_ref[k].astype(jnp.float32)
        ty = ty_ref[k]
        uy = uy_ref[k].astype(jnp.float32)
        tx_f = jnp.where(cut_x, 0.0, tx)
        ty_f = jnp.where(cut_y, 0.0, ty)
        tx_b = jnp.where(first_lane, col(hxl_ref, k, nf), pltpu.roll(tx, 1, 1))
        ux_b = jnp.where(first_lane, col(hxl_ref, k, nf + 1), pltpu.roll(ux, 1, 1))
        ty_b = jnp.where(first_sub, row(hyd_ref, k, nf), pltpu.roll(ty, 1, 0))
        uy_b = jnp.where(first_sub, row(hyd_ref, k, nf + 1), pltpu.roll(uy, 1, 0))
        tz = jnp.where(k < layers - 1, tz_ref[k], 0.0)
        uz = uz_ref[k] == 1

        g_here = group(here)
        acc, _ = face_terms(tx_f, ux > 0.5, g_here, group(right), (0.0, 0.0), ndir)
        _, xb = face_terms(tx_b, ux_b > 0.5, group(left), g_here, (0.0, 0.0), ndir)
        yf, _ = face_terms(ty_f, uy > 0.5, g_here, group(up_), (0.0, 0.0), ndir)
        _, yb = face_terms(ty_b, uy_b > 0.5, group(down), g_here, (0.0, 0.0), ndir)
        zf, zb = face_terms(tz, uz, g_here, group(above), (water_head, oil_head), ndir)
        acc = [a + b + c + e for a, b, c, e in zip(acc, xb, yf, yb)]
        acc = [a + z for a, z in zip(acc, zf)]

        change = here[1] - so_ref[k]
        pore = pore_ref[k]
        acc[0] = acc[0] + pore * change
        acc[1] = acc[1] - pore * change
        for d in range(ndir):
            vs = here[2 + ndir + d]
            acc[2 + d] = acc[2 + d] + pore * vs
            acc[2 + ndir + d] = acc[2 + ndir + d] - pore * vs
            jt_s = 2 + 3 * ndir + d
            acc[jt_s] = acc[jt_s] + pore * (here[2 + 2 * ndir + d] - here[2 + 3 * ndir + d])
        acc = [a + c for a, c in zip(acc, carry)]
        store(k, acc)
        return tuple(zb)

    zero = jnp.zeros((rows, cols), jnp.float32)
    lax.fori_loop(0, layers, body, tuple([zero] * nf))


def body(
    pressure,
    saturation,
    sat_old,
    pore,
    trans_x,
    trans_y,
    trans_z,
    upwind_x,
    upwind_y,
    upwind_z,
    directions,
    adjoint_weights,
    perf_well,
    perf_col,
    perf_top,
    perf_span,
    perf_index,
    bhp,
    target,
):
    layers, rows, cols = pressure.shape
    spatial = (layers, rows, cols)
    ndir = directions.shape[0]
    last_x = lax.axis_index("gx") == lax.axis_size("gx") - 1
    last_y = lax.axis_index(GY_WA) == lax.axis_size(GY_WA) - 1
    edge = jnp.stack([last_x, last_y]).astype(jnp.int32)

    nf = 2 + 4 * ndir
    vmem = pl.BlockSpec(memory_space=pltpu.VMEM)
    x_low, x_high, y_low, y_high = pl.pallas_call(
        pack_kernel,
        out_shape=[
            jax.ShapeDtypeStruct((layers, rows, nf + 2), jnp.float32),
            jax.ShapeDtypeStruct((layers, rows, nf), jnp.float32),
            jax.ShapeDtypeStruct((layers, nf + 2, cols), jnp.float32),
            jax.ShapeDtypeStruct((layers, nf, cols), jnp.float32),
        ],
        in_specs=[vmem] * 8,
        out_specs=[vmem] * 4,
        cost_estimate=pl.CostEstimate(
            flops=layers * rows * cols * 160,
            transcendentals=0,
            bytes_accessed=(6 + 4 * ndir) * layers * rows * cols * 4,
        ),
    )(pressure, saturation, directions, adjoint_weights, trans_x, upwind_x, trans_y, upwind_y)
    x_low, x_high, y_low, y_high, pressure, saturation, directions, adjoint_weights = lax.optimization_barrier(
        (x_low, x_high, y_low, y_high, pressure, saturation, directions, adjoint_weights)
    )
    hxl = shift_along(x_low, "gx", True)
    hxr = shift_along(x_high, "gx", False)
    hyd = shift_along(y_low, GY_WA, True)
    hyu = shift_along(y_high, GY_WA, False)

    lane_hit = (jnp.arange(cols)[:, None] == (perf_col % cols)[None, :]).astype(jnp.float32)
    row_hit = (jnp.arange(rows)[:, None] == (perf_col // cols)[None, :]).astype(jnp.float32)

    def at_perfs(field):
        by_lane = jnp.dot(field, lane_hit, precision=lax.Precision.HIGHEST)
        return jnp.sum(by_lane * row_hit, axis=-2)

    p_cells = at_perfs(pressure)
    s_cells = at_perfs(saturation)
    dir_cells = at_perfs(directions)
    wts_cells = at_perfs(adjoint_weights)
    depth = jnp.arange(layers)[:, None]
    open_layer = jnp.logical_and(
        depth >= perf_top[None, :], depth < (perf_top + perf_span)[None, :]
    )
    weight = jnp.where(open_layer, perf_index[None, :], 0.0)
    row_bhp = jnp.take(bhp, perf_well)
    drive = p_cells - row_bhp
    mob = mobility(s_cells)
    slope = mobility_slope(s_cells)
    mob_total = mob[0] + mob[1]
    slope_total = slope[0] + slope[1]
    rates = weight * mob * drive
    rate_tangent = weight * (mob * dir_cells[:, 0:1] + slope * drive * dir_cells[:, 1:2])
    grad_p = weight * (mob[0] * wts_cells[:, 0] + mob[1] * wts_cells[:, 1])
    grad_s = weight * drive * (slope[0] * wts_cells[:, 0] + slope[1] * wts_cells[:, 1])
    row_sums = jnp.concatenate(
        [
            jnp.sum(weight * mob_total, axis=0)[None],
            jnp.sum(rates[0] + rates[1], axis=0)[None],
            jnp.sum(rate_tangent[:, 0] + rate_tangent[:, 1], axis=1),
            jnp.sum(grad_p, axis=1),
        ],
        axis=0,
    )
    packed = jnp.concatenate([row_sums, perf_well.astype(jnp.float32)[None]], axis=0)
    everyone = gather_everywhere(packed)


    all_sums = jnp.moveaxis(everyone[:, :-1], 1, 0).reshape(row_sums.shape[0], -1)
    all_wells = everyone[:, -1].reshape(-1)
    same_well = (perf_well.astype(jnp.float32)[:, None] == all_wells[None, :]).astype(jnp.float32)
    row_totals = jnp.dot(all_sums, same_well.T, precision=lax.Precision.HIGHEST)
    row_target = jnp.take(target, perf_well)
    row_factors = well_factors(row_totals, row_target)
    wells_res = rates - weight * mob * row_factors[0]
    wells_fwd = rate_tangent - (weight * mob)[None] * row_factors[1 : 1 + ndir][:, None, None, :]
    out_f = row_factors[1 + ndir :][:, None, :]
    wells_adj = jnp.stack(
        [grad_p - weight * mob_total * out_f, grad_s - weight * slope_total * drive * out_f], axis=1
    )
    combined = jnp.concatenate([wells_res[None], wells_fwd, wells_adj], axis=0)
    by_row = combined[..., None, :] * row_hit
    spread = jnp.dot(by_row, lane_hit.T, precision=lax.Precision.HIGHEST)

    reduced_residual, forward_products, adjoint_products = pl.pallas_call(
        stencil_kernel,
        out_shape=[
            jax.ShapeDtypeStruct((2,) + spatial, jnp.float32),
            jax.ShapeDtypeStruct((ndir, 2) + spatial, jnp.float32),
            jax.ShapeDtypeStruct((ndir, 2) + spatial, jnp.float32),
        ],
        in_specs=[pl.BlockSpec(memory_space=pltpu.SMEM)] + [vmem] * 17,
        out_specs=[vmem] * 3,
        cost_estimate=pl.CostEstimate(
            flops=layers * rows * cols * 1200,
            transcendentals=0,
            bytes_accessed=(10 + 4 * 4 * ndir + 2 + 2 * 2 * ndir) * layers * rows * cols * 4,
        ),
    )(
        edge,
        pressure,
        saturation,
        sat_old,
        pore,
        trans_x,
        trans_y,
        trans_z,
        upwind_x,
        upwind_y,
        upwind_z,
        directions,
        adjoint_weights,
        hxl,
        hxr,
        hyd,
        hyu,
        spread,
    )
    return (reduced_residual, forward_products, adjoint_products)


def solution(mesh):
    split = Mesh(
        mesh.devices.reshape(mesh.shape["gx"], 4, 4, mesh.shape["wa"]), ("gx", "gy_0", "gy_1", "wa")
    )
    return jax.shard_map(
        body,
        mesh=split,
        in_specs=(
            P(None, GY_WA, "gx"),
            P(None, GY_WA, "gx"),
            P(None, GY_WA, "gx"),
            P(None, GY_WA, "gx"),
            P(None, GY_WA, "gx"),
            P(None, GY_WA, "gx"),
            P(None, GY_WA, "gx"),
            P(None, GY_WA, "gx"),
            P(None, GY_WA, "gx"),
            P(None, GY_WA, "gx"),
            P(None, None, None, GY_WA, "gx"),
            P(None, None, None, GY_WA, "gx"),
            P(GX_GY_WA),
            P(GX_GY_WA),
            P(GX_GY_WA),
            P(GX_GY_WA),
            P(GX_GY_WA),
            P(),
            P(),
        ),
        out_specs=(
            P(None, None, GY_WA, "gx"),
            P(None, None, None, GY_WA, "gx"),
            P(None, None, None, GY_WA, "gx"),
        ),
        check_vma=False,
    )
```

```python
import jax
import jax.numpy as jnp
from jax import lax
from jax.experimental import pallas as pl
from jax.experimental.pallas import tpu as pltpu
from jax.sharding import Mesh
from jax.sharding import PartitionSpec as P

GY_WA = ("gy_0", "gy_1", "wa")
GX_GY_WA = ("gx", "gy_0", "gy_1", "wa")


water_visc = 0.5
oil_visc = 2.0
water_head = 0.3
oil_head = 0.2


def gather_everywhere(block):
    peers = lax.axis_size(GX_GY_WA)
    return lax.all_to_all(jnp.broadcast_to(block[None], (peers,) + block.shape), GX_GY_WA, 0, 0)


def shift_along(block, axis, down):
    size = lax.axis_size(axis)
    pairs = [(i, i + 1) for i in range(size - 1)]
    if not down:
        pairs = [(b, a) for a, b in pairs]
    return lax.ppermute(block, axis, pairs)


def mobility(sat):
    return jnp.stack([sat * sat / water_visc, (1.0 - sat) * (1.0 - sat) / oil_visc])


def mobility_slope(sat):
    return jnp.stack([2.0 * sat / water_visc, -2.0 * (1.0 - sat) / oil_visc])


def well_factors(sums, goal):
    return jnp.concatenate([((sums[1] - goal) / sums[0])[None], sums[2:] / sums[0][None]], axis=0)


def face_terms(trans, up, a, b, heads, ndir):
    pa, sa, vpa, vsa, wwa, woa = a
    pb, sb, vpb, vsb, wwb, wob = b
    su = jnp.where(up, sa, sb)
    drop = pa - pb
    pot_w = drop + heads[0]
    pot_o = drop + heads[1]
    tl_w = trans * (su * su / water_visc)
    tl_o = trans * ((1.0 - su) * (1.0 - su) / oil_visc)
    f_w = tl_w * pot_w
    f_o = tl_o * pot_o
    td_w = trans * (2.0 * su / water_visc) * pot_w
    td_o = trans * (-2.0 * (1.0 - su) / oil_visc) * pot_o
    jv_w, jv_o, jt_p, jt_s = [], [], [], []
    for d in range(ndir):
        vsu = jnp.where(up, vsa[d], vsb[d])
        dvp = vpa[d] - vpb[d]
        jv_w.append(td_w * vsu + tl_w * dvp)
        jv_o.append(td_o * vsu + tl_o * dvp)
        dww = wwa[d] - wwb[d]
        dwo = woa[d] - wob[d]
        jt_p.append(dww * tl_w + dwo * tl_o)
        jt_s.append(dww * td_w + dwo * td_o)
    zero = jnp.zeros_like(su)
    as_a = [f_w, f_o] + jv_w + jv_o + jt_p + [jnp.where(up, g, zero) for g in jt_s]
    as_b = [-f_w, -f_o] + [-x for x in jv_w] + [-x for x in jv_o] + [-x for x in jt_p]
    as_b = as_b + [jnp.where(up, zero, g) for g in jt_s]
    return as_a, as_b


def pack_kernel(p_ref, s_ref, d_ref, w_ref, tx_ref, ux_ref, ty_ref, uy_ref, xl_ref, xr_ref, yd_ref, yu_ref):
    ndir = d_ref.shape[0]
    layers, rows, cols = p_ref.shape
    lane = lax.broadcasted_iota(jnp.int32, (rows, cols), 1)
    sub = lax.broadcasted_iota(jnp.int32, (rows, cols), 0)
    nf = 2 + 4 * ndir

    def rolled(x, shift, axis):
        return x if shift == 0 else pltpu.roll(x, shift, axis)

    def rows_into(ref, k, tiles, source_row):
        count = len(tiles)
        for start in range(0, count, rows):
            acc = jnp.zeros((rows, cols), jnp.float32)
            for f in range(start, min(start + rows, count)):
                r = f - start
                acc = jnp.where(sub == r, rolled(tiles[f], (r - source_row) % rows, 0), acc)
            n = min(rows, count - start)
            ref[k, pl.ds(start, n), :] = acc[:n]

    def body(k, carry):
        cells = [p_ref[k], s_ref[k]]
        for half in range(2):
            cells += [d_ref[d, half, k] for d in range(ndir)]
        for half in range(2):
            cells += [w_ref[d, half, k] for d in range(ndir)]
        low_x = cells + [tx_ref[k], ux_ref[k].astype(jnp.float32)]
        low_y = cells + [ty_ref[k], uy_ref[k].astype(jnp.float32)]
        xl = jnp.zeros((rows, cols), jnp.float32)
        for f, t in enumerate(low_x):
            xl = jnp.where(lane == f, rolled(t, (f - (cols - 1)) % cols, 1), xl)
        xr = jnp.zeros((rows, cols), jnp.float32)
        for f, t in enumerate(cells):
            xr = jnp.where(lane == f, rolled(t, f % cols, 1), xr)
        xl_ref[k] = xl[:, : nf + 2]
        xr_ref[k] = xr[:, :nf]
        rows_into(yd_ref, k, low_y, rows - 1)
        rows_into(yu_ref, k, cells, 0)
        return carry

    lax.fori_loop(0, layers, body, 0)


def stencil_kernel(
    edge_ref,
    p_ref,
    s_ref,
    so_ref,
    pore_ref,
    tx_ref,
    ty_ref,
    tz_ref,
    ux_ref,
    uy_ref,
    uz_ref,
    d_ref,
    w_ref,
    pn_ref,
    sn_ref,
    dn_ref,
    wn_ref,
    hxl_ref,
    hxr_ref,
    hyd_ref,
    hyu_ref,
    spread_ref,
    r_out,
    jv_out,
    jt_out,
    carry_ref,
):
    ndir = d_ref.shape[0]
    span, rows, cols = p_ref.shape
    block = pl.program_id(0)
    layers = span * pl.num_programs(0)
    lane = lax.broadcasted_iota(jnp.int32, (rows, cols), 1)
    sub = lax.broadcasted_iota(jnp.int32, (rows, cols), 0)
    first_lane = lane == 0
    last_lane = lane == cols - 1
    first_sub = sub == 0
    last_sub = sub == rows - 1
    cut_x = jnp.logical_and(last_lane, edge_ref[0] == 1)
    cut_y = jnp.logical_and(last_sub, edge_ref[1] == 1)
    nf = 2 + 4 * ndir

    def cells_of(pr, sr, dr, wr, k):
        out = [pr[k], sr[k]]
        for half in range(2):
            out += [dr[d, half, k] for d in range(ndir)]
        for half in range(2):
            out += [wr[d, half, k] for d in range(ndir)]
        return out

    def group(flat):
        return (
            flat[0],
            flat[1],
            flat[2 : 2 + ndir],
            flat[2 + ndir : 2 + 2 * ndir],
            flat[2 + 2 * ndir : 2 + 3 * ndir],
            flat[2 + 3 * ndir : 2 + 4 * ndir],
        )

    def col(ref, k, f):
        return jnp.broadcast_to(ref[k, :, pl.ds(f, 1)], (rows, cols))

    def row(ref, k, f):
        return jnp.broadcast_to(ref[k, pl.ds(f, 1), :], (rows, cols))

    def store(k, vals):
        for i in range(nf):
            if i < 2:
                ref, idx, extra = r_out, (i, k), (0, i, k)
            elif i < 2 + 2 * ndir:
                j = i - 2
                ref, idx, extra = jv_out, (j % ndir, j // ndir, k), (1 + j % ndir, j // ndir, k)
            else:
                j = i - 2 - 2 * ndir
                ref, idx, extra = jt_out, (j % ndir, j // ndir, k), (1 + ndir + j % ndir, j // ndir, k)
            ref[idx] = vals[i] + spread_ref[extra]

    def layer(k, carry, above):
        here = cells_of(p_ref, s_ref, d_ref, w_ref, k)
        left = [jnp.where(first_lane, col(hxl_ref, k, f), pltpu.roll(x, 1, 1)) for f, x in enumerate(here)]
        right = [jnp.where(last_lane, col(hxr_ref, k, f), pltpu.roll(x, cols - 1, 1)) for f, x in enumerate(here)]
        down = [jnp.where(first_sub, row(hyd_ref, k, f), pltpu.roll(x, 1, 0)) for f, x in enumerate(here)]
        up_ = [jnp.where(last_sub, row(hyu_ref, k, f), pltpu.roll(x, rows - 1, 0)) for f, x in enumerate(here)]

        tx = tx_ref[k]
        ux = ux_ref[k].astype(jnp.float32)
        ty = ty_ref[k]
        uy = uy_ref[k].astype(jnp.float32)
        tx_f = jnp.where(cut_x, 0.0, tx)
        ty_f = jnp.where(cut_y, 0.0, ty)
        tx_b = jnp.where(first_lane, col(hxl_ref, k, nf), pltpu.roll(tx, 1, 1))
        ux_b = jnp.where(first_lane, col(hxl_ref, k, nf + 1), pltpu.roll(ux, 1, 1))
        ty_b = jnp.where(first_sub, row(hyd_ref, k, nf), pltpu.roll(ty, 1, 0))
        uy_b = jnp.where(first_sub, row(hyd_ref, k, nf + 1), pltpu.roll(uy, 1, 0))
        tz = jnp.where(block * span + k < layers - 1, tz_ref[k], 0.0)
        uz = uz_ref[k] == 1

        g_here = group(here)
        acc, _ = face_terms(tx_f, ux > 0.5, g_here, group(right), (0.0, 0.0), ndir)
        _, xb = face_terms(tx_b, ux_b > 0.5, group(left), g_here, (0.0, 0.0), ndir)
        yf, _ = face_terms(ty_f, uy > 0.5, g_here, group(up_), (0.0, 0.0), ndir)
        _, yb = face_terms(ty_b, uy_b > 0.5, group(down), g_here, (0.0, 0.0), ndir)
        zf, zb = face_terms(tz, uz, g_here, group(above), (water_head, oil_head), ndir)
        acc = [a + b + c + e for a, b, c, e in zip(acc, xb, yf, yb)]
        acc = [a + z for a, z in zip(acc, zf)]

        change = here[1] - so_ref[k]
        pore = pore_ref[k]
        acc[0] = acc[0] + pore * change
        acc[1] = acc[1] - pore * change
        for d in range(ndir):
            vs = here[2 + ndir + d]
            acc[2 + d] = acc[2 + d] + pore * vs
            acc[2 + ndir + d] = acc[2 + ndir + d] - pore * vs
            jt_s = 2 + 3 * ndir + d
            acc[jt_s] = acc[jt_s] + pore * (here[2 + 2 * ndir + d] - here[2 + 3 * ndir + d])
        acc = [a + c for a, c in zip(acc, carry)]
        store(k, acc)
        return tuple(zb)

    @pl.when(block == 0)
    def _():
        carry_ref[...] = jnp.zeros_like(carry_ref)

    def inner(k, carry):
        return layer(k, carry, cells_of(p_ref, s_ref, d_ref, w_ref, k + 1))

    carry = tuple(carry_ref[i] for i in range(nf))
    carry = lax.fori_loop(0, span - 1, inner, carry)
    carry = layer(span - 1, carry, cells_of(pn_ref, sn_ref, dn_ref, wn_ref, 0))
    for i in range(nf):
        carry_ref[i] = carry[i]


def body(
    pressure,
    saturation,
    sat_old,
    pore,
    trans_x,
    trans_y,
    trans_z,
    upwind_x,
    upwind_y,
    upwind_z,
    directions,
    adjoint_weights,
    perf_well,
    perf_col,
    perf_top,
    perf_span,
    perf_index,
    bhp,
    target,
):
    layers, rows, cols = pressure.shape
    spatial = (layers, rows, cols)
    ndir = directions.shape[0]
    last_x = lax.axis_index("gx") == lax.axis_size("gx") - 1
    last_y = lax.axis_index(GY_WA) == lax.axis_size(GY_WA) - 1
    edge = jnp.stack([last_x, last_y]).astype(jnp.int32)

    nf = 2 + 4 * ndir
    vmem = pl.BlockSpec(memory_space=pltpu.VMEM)
    x_low, x_high, y_low, y_high = pl.pallas_call(
        pack_kernel,
        out_shape=[
            jax.ShapeDtypeStruct((layers, rows, nf + 2), jnp.float32),
            jax.ShapeDtypeStruct((layers, rows, nf), jnp.float32),
            jax.ShapeDtypeStruct((layers, nf + 2, cols), jnp.float32),
            jax.ShapeDtypeStruct((layers, nf, cols), jnp.float32),
        ],
        in_specs=[vmem] * 8,
        out_specs=[vmem] * 4,
        cost_estimate=pl.CostEstimate(
            flops=layers * rows * cols * 160,
            transcendentals=0,
            bytes_accessed=(6 + 4 * ndir) * layers * rows * cols * 4,
        ),
    )(pressure, saturation, directions, adjoint_weights, trans_x, upwind_x, trans_y, upwind_y)
    x_low, x_high, y_low, y_high, pressure, saturation, directions, adjoint_weights = lax.optimization_barrier(
        (x_low, x_high, y_low, y_high, pressure, saturation, directions, adjoint_weights)
    )
    hxl = shift_along(x_low, "gx", True)
    hxr = shift_along(x_high, "gx", False)
    hyd = shift_along(y_low, GY_WA, True)
    hyu = shift_along(y_high, GY_WA, False)

    lane_hit = (jnp.arange(cols)[:, None] == (perf_col % cols)[None, :]).astype(jnp.float32)
    row_hit = (jnp.arange(rows)[:, None] == (perf_col // cols)[None, :]).astype(jnp.float32)

    def at_perfs(field):
        by_lane = jnp.dot(field, lane_hit, precision=lax.Precision.HIGHEST)
        return jnp.sum(by_lane * row_hit, axis=-2)

    p_cells = at_perfs(pressure)
    s_cells = at_perfs(saturation)
    dir_cells = at_perfs(directions)
    wts_cells = at_perfs(adjoint_weights)
    depth = jnp.arange(layers)[:, None]
    open_layer = jnp.logical_and(
        depth >= perf_top[None, :], depth < (perf_top + perf_span)[None, :]
    )
    weight = jnp.where(open_layer, perf_index[None, :], 0.0)
    row_bhp = jnp.take(bhp, perf_well)
    drive = p_cells - row_bhp
    mob = mobility(s_cells)
    slope = mobility_slope(s_cells)
    mob_total = mob[0] + mob[1]
    slope_total = slope[0] + slope[1]
    rates = weight * mob * drive
    rate_tangent = weight * (mob * dir_cells[:, 0:1] + slope * drive * dir_cells[:, 1:2])
    grad_p = weight * (mob[0] * wts_cells[:, 0] + mob[1] * wts_cells[:, 1])
    grad_s = weight * drive * (slope[0] * wts_cells[:, 0] + slope[1] * wts_cells[:, 1])
    row_sums = jnp.concatenate(
        [
            jnp.sum(weight * mob_total, axis=0)[None],
            jnp.sum(rates[0] + rates[1], axis=0)[None],
            jnp.sum(rate_tangent[:, 0] + rate_tangent[:, 1], axis=1),
            jnp.sum(grad_p, axis=1),
        ],
        axis=0,
    )
    packed = jnp.concatenate([row_sums, perf_well.astype(jnp.float32)[None]], axis=0)
    everyone = gather_everywhere(packed)


    all_sums = jnp.moveaxis(everyone[:, :-1], 1, 0).reshape(row_sums.shape[0], -1)
    all_wells = everyone[:, -1].reshape(-1)
    same_well = (perf_well.astype(jnp.float32)[:, None] == all_wells[None, :]).astype(jnp.float32)
    row_totals = jnp.dot(all_sums, same_well.T, precision=lax.Precision.HIGHEST)
    row_target = jnp.take(target, perf_well)
    row_factors = well_factors(row_totals, row_target)
    wells_res = rates - weight * mob * row_factors[0]
    wells_fwd = rate_tangent - (weight * mob)[None] * row_factors[1 : 1 + ndir][:, None, None, :]
    out_f = row_factors[1 + ndir :][:, None, :]
    wells_adj = jnp.stack(
        [grad_p - weight * mob_total * out_f, grad_s - weight * slope_total * drive * out_f], axis=1
    )
    combined = jnp.concatenate([wells_res[None], wells_fwd, wells_adj], axis=0)
    by_row = combined[..., None, :] * row_hit
    spread = jnp.dot(by_row, lane_hit.T, precision=lax.Precision.HIGHEST)

    span = 6 if layers % 6 == 0 else layers
    blocks = layers // span

    def layer_block(*lead):
        return pl.BlockSpec(tuple(lead) + (span, rows, cols), lambda b: (0,) * len(lead) + (b, 0, 0))

    def next_layer(*lead):
        return pl.BlockSpec(
            tuple(lead) + (1, rows, cols),
            lambda b: (0,) * len(lead) + (jnp.minimum((b + 1) * span, layers - 1), 0, 0),
        )

    def halo_block(mid, last):
        return pl.BlockSpec((span, mid, last), lambda b: (b, 0, 0))

    reduced_residual, forward_products, adjoint_products = pl.pallas_call(
        stencil_kernel,
        grid=(blocks,),
        out_shape=[
            jax.ShapeDtypeStruct((2,) + spatial, jnp.float32),
            jax.ShapeDtypeStruct((ndir, 2) + spatial, jnp.float32),
            jax.ShapeDtypeStruct((ndir, 2) + spatial, jnp.float32),
        ],
        in_specs=[pl.BlockSpec(memory_space=pltpu.SMEM)]
        + [layer_block()] * 10
        + [layer_block(ndir, 2)] * 2
        + [next_layer()] * 2
        + [next_layer(ndir, 2)] * 2
        + [
            halo_block(rows, nf + 2),
            halo_block(rows, nf),
            halo_block(nf + 2, cols),
            halo_block(nf, cols),
            layer_block(1 + 2 * ndir, 2),
        ],
        out_specs=[layer_block(2), layer_block(ndir, 2), layer_block(ndir, 2)],
        scratch_shapes=[pltpu.VMEM((nf, rows, cols), jnp.float32)],
        compiler_params=pltpu.CompilerParams(dimension_semantics=("arbitrary",)),
        cost_estimate=pl.CostEstimate(
            flops=layers * rows * cols * 1200,
            transcendentals=0,
            bytes_accessed=(10 + 4 * 4 * ndir + 2 + 2 * 2 * ndir) * layers * rows * cols * 4,
        ),
    )(
        edge,
        pressure,
        saturation,
        sat_old,
        pore,
        trans_x,
        trans_y,
        trans_z,
        upwind_x,
        upwind_y,
        upwind_z,
        directions,
        adjoint_weights,
        pressure,
        saturation,
        directions,
        adjoint_weights,
        hxl,
        hxr,
        hyd,
        hyu,
        spread,
    )
    return (reduced_residual, forward_products, adjoint_products)


def solution(mesh):
    split = Mesh(
        mesh.devices.reshape(mesh.shape["gx"], 4, 4, mesh.shape["wa"]), ("gx", "gy_0", "gy_1", "wa")
    )
    return jax.shard_map(
        body,
        mesh=split,
        in_specs=(
            P(None, GY_WA, "gx"),
            P(None, GY_WA, "gx"),
            P(None, GY_WA, "gx"),
            P(None, GY_WA, "gx"),
            P(None, GY_WA, "gx"),
            P(None, GY_WA, "gx"),
            P(None, GY_WA, "gx"),
            P(None, GY_WA, "gx"),
            P(None, GY_WA, "gx"),
            P(None, GY_WA, "gx"),
            P(None, None, None, GY_WA, "gx"),
            P(None, None, None, GY_WA, "gx"),
            P(GX_GY_WA),
            P(GX_GY_WA),
            P(GX_GY_WA),
            P(GX_GY_WA),
            P(GX_GY_WA),
            P(),
            P(),
        ),
        out_specs=(
            P(None, None, GY_WA, "gx"),
            P(None, None, None, GY_WA, "gx"),
            P(None, None, None, GY_WA, "gx"),
        ),
        check_vma=False,
    )
```

```python
import jax
import jax.numpy as jnp
from jax import lax
from jax.experimental import pallas as pl
from jax.experimental.pallas import tpu as pltpu
from jax.sharding import Mesh
from jax.sharding import PartitionSpec as P

GY_WA = ("gy_0", "gy_1", "wa")
GX_GY_WA = ("gx", "gy_0", "gy_1", "wa")


water_visc = 0.5
oil_visc = 2.0
water_head = 0.3
oil_head = 0.2


def gather_everywhere(block):
    peers = lax.axis_size(GX_GY_WA)
    flat = jnp.broadcast_to(block.reshape(1, -1), (peers, block.size))
    return lax.all_to_all(flat, GX_GY_WA, 0, 0, tiled=True).reshape((peers,) + block.shape)


def shift_along(block, axis, down):
    size = lax.axis_size(axis)
    pairs = [(i, i + 1) for i in range(size - 1)]
    if not down:
        pairs = [(b, a) for a, b in pairs]
    return lax.ppermute(block, axis, pairs)


def mobility(sat):
    return jnp.stack([sat * sat / water_visc, (1.0 - sat) * (1.0 - sat) / oil_visc])


def mobility_slope(sat):
    return jnp.stack([2.0 * sat / water_visc, -2.0 * (1.0 - sat) / oil_visc])


def well_factors(sums, goal):
    return jnp.concatenate([((sums[1] - goal) / sums[0])[None], sums[2:] / sums[0][None]], axis=0)


def face_terms(trans, up, a, b, heads, ndir):
    pa, sa, vpa, vsa, wwa, woa = a
    pb, sb, vpb, vsb, wwb, wob = b
    su = jnp.where(up, sa, sb)
    drop = pa - pb
    pot_w = drop + heads[0]
    pot_o = drop + heads[1]
    tl_w = trans * (su * su / water_visc)
    tl_o = trans * ((1.0 - su) * (1.0 - su) / oil_visc)
    f_w = tl_w * pot_w
    f_o = tl_o * pot_o
    td_w = trans * (2.0 * su / water_visc) * pot_w
    td_o = trans * (-2.0 * (1.0 - su) / oil_visc) * pot_o
    jv_w, jv_o, jt_p, jt_s = [], [], [], []
    for d in range(ndir):
        vsu = jnp.where(up, vsa[d], vsb[d])
        dvp = vpa[d] - vpb[d]
        jv_w.append(td_w * vsu + tl_w * dvp)
        jv_o.append(td_o * vsu + tl_o * dvp)
        dww = wwa[d] - wwb[d]
        dwo = woa[d] - wob[d]
        jt_p.append(dww * tl_w + dwo * tl_o)
        jt_s.append(dww * td_w + dwo * td_o)
    zero = jnp.zeros_like(su)
    as_a = [f_w, f_o] + jv_w + jv_o + jt_p + [jnp.where(up, g, zero) for g in jt_s]
    as_b = [-f_w, -f_o] + [-x for x in jv_w] + [-x for x in jv_o] + [-x for x in jt_p]
    as_b = as_b + [jnp.where(up, zero, g) for g in jt_s]
    return as_a, as_b


def pack_kernel(p_ref, s_ref, d_ref, w_ref, tx_ref, ux_ref, ty_ref, uy_ref, xl_ref, xr_ref, yd_ref, yu_ref):
    ndir = d_ref.shape[0]
    layers, rows, cols = p_ref.shape
    lane = lax.broadcasted_iota(jnp.int32, (rows, cols), 1)
    sub = lax.broadcasted_iota(jnp.int32, (rows, cols), 0)
    nf = 2 + 4 * ndir

    def rolled(x, shift, axis):
        return x if shift == 0 else pltpu.roll(x, shift, axis)

    def rows_into(ref, k, tiles, source_row):
        count = len(tiles)
        for start in range(0, count, rows):
            acc = jnp.zeros((rows, cols), jnp.float32)
            for f in range(start, min(start + rows, count)):
                r = f - start
                acc = jnp.where(sub == r, rolled(tiles[f], (r - source_row) % rows, 0), acc)
            n = min(rows, count - start)
            ref[k, pl.ds(start, n), :] = acc[:n]

    def body(k, carry):
        cells = [p_ref[k], s_ref[k]]
        for half in range(2):
            cells += [d_ref[d, half, k] for d in range(ndir)]
        for half in range(2):
            cells += [w_ref[d, half, k] for d in range(ndir)]
        low_x = cells + [tx_ref[k], ux_ref[k].astype(jnp.float32)]
        low_y = cells + [ty_ref[k], uy_ref[k].astype(jnp.float32)]
        xl = jnp.zeros((rows, cols), jnp.float32)
        for f, t in enumerate(low_x):
            xl = jnp.where(lane == f, rolled(t, (f - (cols - 1)) % cols, 1), xl)
        xr = jnp.zeros((rows, cols), jnp.float32)
        for f, t in enumerate(cells):
            xr = jnp.where(lane == f, rolled(t, f % cols, 1), xr)
        xl_ref[k] = xl[:, : nf + 2]
        xr_ref[k] = xr[:, :nf]
        rows_into(yd_ref, k, low_y, rows - 1)
        rows_into(yu_ref, k, cells, 0)
        return carry

    lax.fori_loop(0, layers, body, 0)


def stencil_kernel(
    edge_ref,
    p_ref,
    s_ref,
    so_ref,
    pore_ref,
    tx_ref,
    ty_ref,
    tz_ref,
    ux_ref,
    uy_ref,
    uz_ref,
    d_ref,
    w_ref,
    pn_ref,
    sn_ref,
    dn_ref,
    wn_ref,
    hxl_ref,
    hxr_ref,
    hyd_ref,
    hyu_ref,
    spread_ref,
    r_out,
    jv_out,
    jt_out,
    carry_ref,
):
    ndir = d_ref.shape[0]
    span, rows, cols = p_ref.shape
    block = pl.program_id(0)
    layers = span * pl.num_programs(0)
    lane = lax.broadcasted_iota(jnp.int32, (rows, cols), 1)
    sub = lax.broadcasted_iota(jnp.int32, (rows, cols), 0)
    first_lane = lane == 0
    last_lane = lane == cols - 1
    first_sub = sub == 0
    last_sub = sub == rows - 1
    cut_x = jnp.logical_and(last_lane, edge_ref[0] == 1)
    cut_y = jnp.logical_and(last_sub, edge_ref[1] == 1)
    nf = 2 + 4 * ndir

    def cells_of(pr, sr, dr, wr, k):
        out = [pr[k], sr[k]]
        for half in range(2):
            out += [dr[d, half, k] for d in range(ndir)]
        for half in range(2):
            out += [wr[d, half, k] for d in range(ndir)]
        return out

    def group(flat):
        return (
            flat[0],
            flat[1],
            flat[2 : 2 + ndir],
            flat[2 + ndir : 2 + 2 * ndir],
            flat[2 + 2 * ndir : 2 + 3 * ndir],
            flat[2 + 3 * ndir : 2 + 4 * ndir],
        )

    def col(ref, k, f):
        return jnp.broadcast_to(ref[k, :, pl.ds(f, 1)], (rows, cols))

    def row(ref, k, f):
        return jnp.broadcast_to(ref[k, pl.ds(f, 1), :], (rows, cols))

    def store(k, vals):
        for i in range(nf):
            if i < 2:
                ref, idx, extra = r_out, (i, k), (0, i, k)
            elif i < 2 + 2 * ndir:
                j = i - 2
                ref, idx, extra = jv_out, (j % ndir, j // ndir, k), (1 + j % ndir, j // ndir, k)
            else:
                j = i - 2 - 2 * ndir
                ref, idx, extra = jt_out, (j % ndir, j // ndir, k), (1 + ndir + j % ndir, j // ndir, k)
            ref[idx] = vals[i] + spread_ref[extra]

    def layer(k, carry, above):
        here = cells_of(p_ref, s_ref, d_ref, w_ref, k)
        left = [jnp.where(first_lane, col(hxl_ref, k, f), pltpu.roll(x, 1, 1)) for f, x in enumerate(here)]
        right = [jnp.where(last_lane, col(hxr_ref, k, f), pltpu.roll(x, cols - 1, 1)) for f, x in enumerate(here)]
        down = [jnp.where(first_sub, row(hyd_ref, k, f), pltpu.roll(x, 1, 0)) for f, x in enumerate(here)]
        up_ = [jnp.where(last_sub, row(hyu_ref, k, f), pltpu.roll(x, rows - 1, 0)) for f, x in enumerate(here)]

        tx = tx_ref[k]
        ux = ux_ref[k].astype(jnp.float32)
        ty = ty_ref[k]
        uy = uy_ref[k].astype(jnp.float32)
        tx_f = jnp.where(cut_x, 0.0, tx)
        ty_f = jnp.where(cut_y, 0.0, ty)
        tx_b = jnp.where(first_lane, col(hxl_ref, k, nf), pltpu.roll(tx, 1, 1))
        ux_b = jnp.where(first_lane, col(hxl_ref, k, nf + 1), pltpu.roll(ux, 1, 1))
        ty_b = jnp.where(first_sub, row(hyd_ref, k, nf), pltpu.roll(ty, 1, 0))
        uy_b = jnp.where(first_sub, row(hyd_ref, k, nf + 1), pltpu.roll(uy, 1, 0))
        tz = jnp.where(block * span + k < layers - 1, tz_ref[k], 0.0)
        uz = uz_ref[k] == 1

        g_here = group(here)
        acc, _ = face_terms(tx_f, ux > 0.5, g_here, group(right), (0.0, 0.0), ndir)
        _, xb = face_terms(tx_b, ux_b > 0.5, group(left), g_here, (0.0, 0.0), ndir)
        yf, _ = face_terms(ty_f, uy > 0.5, g_here, group(up_), (0.0, 0.0), ndir)
        _, yb = face_terms(ty_b, uy_b > 0.5, group(down), g_here, (0.0, 0.0), ndir)
        zf, zb = face_terms(tz, uz, g_here, group(above), (water_head, oil_head), ndir)
        acc = [a + b + c + e for a, b, c, e in zip(acc, xb, yf, yb)]
        acc = [a + z for a, z in zip(acc, zf)]

        change = here[1] - so_ref[k]
        pore = pore_ref[k]
        acc[0] = acc[0] + pore * change
        acc[1] = acc[1] - pore * change
        for d in range(ndir):
            vs = here[2 + ndir + d]
            acc[2 + d] = acc[2 + d] + pore * vs
            acc[2 + ndir + d] = acc[2 + ndir + d] - pore * vs
            jt_s = 2 + 3 * ndir + d
            acc[jt_s] = acc[jt_s] + pore * (here[2 + 2 * ndir + d] - here[2 + 3 * ndir + d])
        acc = [a + c for a, c in zip(acc, carry)]
        store(k, acc)
        return tuple(zb)

    @pl.when(block == 0)
    def _():
        carry_ref[...] = jnp.zeros_like(carry_ref)

    def inner(k, carry):
        return layer(k, carry, cells_of(p_ref, s_ref, d_ref, w_ref, k + 1))

    carry = tuple(carry_ref[i] for i in range(nf))
    carry = lax.fori_loop(0, span - 1, inner, carry)
    carry = layer(span - 1, carry, cells_of(pn_ref, sn_ref, dn_ref, wn_ref, 0))
    for i in range(nf):
        carry_ref[i] = carry[i]


def body(
    pressure,
    saturation,
    sat_old,
    pore,
    trans_x,
    trans_y,
    trans_z,
    upwind_x,
    upwind_y,
    upwind_z,
    directions,
    adjoint_weights,
    perf_well,
    perf_col,
    perf_top,
    perf_span,
    perf_index,
    bhp,
    target,
):
    layers, rows, cols = pressure.shape
    spatial = (layers, rows, cols)
    ndir = directions.shape[0]
    last_x = lax.axis_index("gx") == lax.axis_size("gx") - 1
    last_y = lax.axis_index(GY_WA) == lax.axis_size(GY_WA) - 1
    edge = jnp.stack([last_x, last_y]).astype(jnp.int32)

    nf = 2 + 4 * ndir
    vmem = pl.BlockSpec(memory_space=pltpu.VMEM)
    x_low, x_high, y_low, y_high = pl.pallas_call(
        pack_kernel,
        out_shape=[
            jax.ShapeDtypeStruct((layers, rows, nf + 2), jnp.float32),
            jax.ShapeDtypeStruct((layers, rows, nf), jnp.float32),
            jax.ShapeDtypeStruct((layers, nf + 2, cols), jnp.float32),
            jax.ShapeDtypeStruct((layers, nf, cols), jnp.float32),
        ],
        in_specs=[vmem] * 8,
        out_specs=[vmem] * 4,
        cost_estimate=pl.CostEstimate(
            flops=layers * rows * cols * 160,
            transcendentals=0,
            bytes_accessed=(6 + 4 * ndir) * layers * rows * cols * 4,
        ),
    )(pressure, saturation, directions, adjoint_weights, trans_x, upwind_x, trans_y, upwind_y)
    x_low, x_high, y_low, y_high, pressure, saturation, directions, adjoint_weights = lax.optimization_barrier(
        (x_low, x_high, y_low, y_high, pressure, saturation, directions, adjoint_weights)
    )
    hxl = shift_along(x_low, "gx", True)
    hxr = shift_along(x_high, "gx", False)
    hyd = shift_along(y_low, GY_WA, True)
    hyu = shift_along(y_high, GY_WA, False)

    lane_hit = (jnp.arange(cols)[:, None] == (perf_col % cols)[None, :]).astype(jnp.float32)
    row_hit = (jnp.arange(rows)[:, None] == (perf_col // cols)[None, :]).astype(jnp.float32)

    def at_perfs(field):
        by_lane = jnp.dot(field, lane_hit, precision=lax.Precision.HIGHEST)
        return jnp.sum(by_lane * row_hit, axis=-2)

    p_cells = at_perfs(pressure)
    s_cells = at_perfs(saturation)
    dir_cells = at_perfs(directions)
    wts_cells = at_perfs(adjoint_weights)
    depth = jnp.arange(layers)[:, None]
    open_layer = jnp.logical_and(
        depth >= perf_top[None, :], depth < (perf_top + perf_span)[None, :]
    )
    weight = jnp.where(open_layer, perf_index[None, :], 0.0)
    row_bhp = jnp.take(bhp, perf_well)
    drive = p_cells - row_bhp
    mob = mobility(s_cells)
    slope = mobility_slope(s_cells)
    mob_total = mob[0] + mob[1]
    slope_total = slope[0] + slope[1]
    rates = weight * mob * drive
    rate_tangent = weight * (mob * dir_cells[:, 0:1] + slope * drive * dir_cells[:, 1:2])
    grad_p = weight * (mob[0] * wts_cells[:, 0] + mob[1] * wts_cells[:, 1])
    grad_s = weight * drive * (slope[0] * wts_cells[:, 0] + slope[1] * wts_cells[:, 1])
    row_sums = jnp.concatenate(
        [
            jnp.sum(weight * mob_total, axis=0)[None],
            jnp.sum(rates[0] + rates[1], axis=0)[None],
            jnp.sum(rate_tangent[:, 0] + rate_tangent[:, 1], axis=1),
            jnp.sum(grad_p, axis=1),
        ],
        axis=0,
    )
    packed = jnp.concatenate([row_sums, perf_well.astype(jnp.float32)[None]], axis=0)
    everyone = gather_everywhere(packed)


    all_sums = jnp.moveaxis(everyone[:, :-1], 1, 0).reshape(row_sums.shape[0], -1)
    all_wells = everyone[:, -1].reshape(-1)
    same_well = (perf_well.astype(jnp.float32)[:, None] == all_wells[None, :]).astype(jnp.float32)
    row_totals = jnp.dot(all_sums, same_well.T, precision=lax.Precision.HIGHEST)
    row_target = jnp.take(target, perf_well)
    row_factors = well_factors(row_totals, row_target)
    wells_res = rates - weight * mob * row_factors[0]
    wells_fwd = rate_tangent - (weight * mob)[None] * row_factors[1 : 1 + ndir][:, None, None, :]
    out_f = row_factors[1 + ndir :][:, None, :]
    wells_adj = jnp.stack(
        [grad_p - weight * mob_total * out_f, grad_s - weight * slope_total * drive * out_f], axis=1
    )
    combined = jnp.concatenate([wells_res[None], wells_fwd, wells_adj], axis=0)
    by_row = combined[..., None, :] * row_hit
    spread = jnp.dot(by_row, lane_hit.T, precision=lax.Precision.HIGHEST)

    span = 6 if layers % 6 == 0 else layers
    blocks = layers // span

    def layer_block(*lead):
        return pl.BlockSpec(tuple(lead) + (span, rows, cols), lambda b: (0,) * len(lead) + (b, 0, 0))

    def next_layer(*lead):
        return pl.BlockSpec(
            tuple(lead) + (1, rows, cols),
            lambda b: (0,) * len(lead) + (jnp.minimum((b + 1) * span, layers - 1), 0, 0),
        )

    def halo_block(mid, last):
        return pl.BlockSpec((span, mid, last), lambda b: (b, 0, 0))

    reduced_residual, forward_products, adjoint_products = pl.pallas_call(
        stencil_kernel,
        grid=(blocks,),
        out_shape=[
            jax.ShapeDtypeStruct((2,) + spatial, jnp.float32),
            jax.ShapeDtypeStruct((ndir, 2) + spatial, jnp.float32),
            jax.ShapeDtypeStruct((ndir, 2) + spatial, jnp.float32),
        ],
        in_specs=[pl.BlockSpec(memory_space=pltpu.SMEM)]
        + [layer_block()] * 10
        + [layer_block(ndir, 2)] * 2
        + [next_layer()] * 2
        + [next_layer(ndir, 2)] * 2
        + [
            halo_block(rows, nf + 2),
            halo_block(rows, nf),
            halo_block(nf + 2, cols),
            halo_block(nf, cols),
            layer_block(1 + 2 * ndir, 2),
        ],
        out_specs=[layer_block(2), layer_block(ndir, 2), layer_block(ndir, 2)],
        scratch_shapes=[pltpu.VMEM((nf, rows, cols), jnp.float32)],
        compiler_params=pltpu.CompilerParams(dimension_semantics=("arbitrary",)),
        cost_estimate=pl.CostEstimate(
            flops=layers * rows * cols * 1200,
            transcendentals=0,
            bytes_accessed=(10 + 4 * 4 * ndir + 2 + 2 * 2 * ndir) * layers * rows * cols * 4,
        ),
    )(
        edge,
        pressure,
        saturation,
        sat_old,
        pore,
        trans_x,
        trans_y,
        trans_z,
        upwind_x,
        upwind_y,
        upwind_z,
        directions,
        adjoint_weights,
        pressure,
        saturation,
        directions,
        adjoint_weights,
        hxl,
        hxr,
        hyd,
        hyu,
        spread,
    )
    return (reduced_residual, forward_products, adjoint_products)


def solution(mesh):
    split = Mesh(
        mesh.devices.reshape(mesh.shape["gx"], 4, 4, mesh.shape["wa"]), ("gx", "gy_0", "gy_1", "wa")
    )
    return jax.shard_map(
        body,
        mesh=split,
        in_specs=(
            P(None, GY_WA, "gx"),
            P(None, GY_WA, "gx"),
            P(None, GY_WA, "gx"),
            P(None, GY_WA, "gx"),
            P(None, GY_WA, "gx"),
            P(None, GY_WA, "gx"),
            P(None, GY_WA, "gx"),
            P(None, GY_WA, "gx"),
            P(None, GY_WA, "gx"),
            P(None, GY_WA, "gx"),
            P(None, None, None, GY_WA, "gx"),
            P(None, None, None, GY_WA, "gx"),
            P(GX_GY_WA),
            P(GX_GY_WA),
            P(GX_GY_WA),
            P(GX_GY_WA),
            P(GX_GY_WA),
            P(),
            P(),
        ),
        out_specs=(
            P(None, None, GY_WA, "gx"),
            P(None, None, None, GY_WA, "gx"),
            P(None, None, None, GY_WA, "gx"),
        ),
        check_vma=False,
    )
```

```python
import jax
import jax.numpy as jnp
from jax import lax
from jax.experimental import pallas as pl
from jax.experimental.pallas import tpu as pltpu
from jax.sharding import Mesh
from jax.sharding import PartitionSpec as P

GY_WA = ("gy_0", "gy_1", "wa")
GX_GY_WA = ("gx", "gy_0", "gy_1", "wa")


water_visc = 0.5
oil_visc = 2.0
water_head = 0.3
oil_head = 0.2


def gather_everywhere(block):
    peers = lax.axis_size(GX_GY_WA)
    flat = jnp.broadcast_to(block.reshape(1, -1), (peers, block.size))
    return lax.all_to_all(flat, GX_GY_WA, 0, 0, tiled=True).reshape((peers,) + block.shape)


def shift_along(block, axis, down):
    size = lax.axis_size(axis)
    pairs = [(i, i + 1) for i in range(size - 1)]
    if not down:
        pairs = [(b, a) for a, b in pairs]
    return lax.ppermute(block, axis, pairs)


def mobility(sat):
    return jnp.stack([sat * sat / water_visc, (1.0 - sat) * (1.0 - sat) / oil_visc])


def mobility_slope(sat):
    return jnp.stack([2.0 * sat / water_visc, -2.0 * (1.0 - sat) / oil_visc])


def well_factors(sums, goal):
    return jnp.concatenate([((sums[1] - goal) / sums[0])[None], sums[2:] / sums[0][None]], axis=0)


def face_terms(trans, up, a, b, heads, ndir):
    pa, sa, vpa, vsa, wwa, woa = a
    pb, sb, vpb, vsb, wwb, wob = b
    su = jnp.where(up, sa, sb)
    drop = pa - pb
    pot_w = drop + heads[0]
    pot_o = drop + heads[1]
    tl_w = trans * (su * su / water_visc)
    tl_o = trans * ((1.0 - su) * (1.0 - su) / oil_visc)
    f_w = tl_w * pot_w
    f_o = tl_o * pot_o
    td_w = trans * (2.0 * su / water_visc) * pot_w
    td_o = trans * (-2.0 * (1.0 - su) / oil_visc) * pot_o
    jv_w, jv_o, jt_p, jt_s = [], [], [], []
    for d in range(ndir):
        vsu = jnp.where(up, vsa[d], vsb[d])
        dvp = vpa[d] - vpb[d]
        jv_w.append(td_w * vsu + tl_w * dvp)
        jv_o.append(td_o * vsu + tl_o * dvp)
        dww = wwa[d] - wwb[d]
        dwo = woa[d] - wob[d]
        jt_p.append(dww * tl_w + dwo * tl_o)
        jt_s.append(dww * td_w + dwo * td_o)
    zero = jnp.zeros_like(su)
    as_a = [f_w, f_o] + jv_w + jv_o + jt_p + [jnp.where(up, g, zero) for g in jt_s]
    as_b = [-f_w, -f_o] + [-x for x in jv_w] + [-x for x in jv_o] + [-x for x in jt_p]
    as_b = as_b + [jnp.where(up, zero, g) for g in jt_s]
    return as_a, as_b


def pack_kernel(p_ref, s_ref, d_ref, w_ref, tx_ref, ux_ref, ty_ref, uy_ref, xl_ref, xr_ref, yd_ref, yu_ref):
    ndir = d_ref.shape[0]
    layers, rows, cols = p_ref.shape
    lane = lax.broadcasted_iota(jnp.int32, (rows, cols), 1)
    sub = lax.broadcasted_iota(jnp.int32, (rows, cols), 0)
    nf = 2 + 4 * ndir

    def rolled(x, shift, axis):
        return x if shift == 0 else pltpu.roll(x, shift, axis)

    def rows_into(ref, k, tiles, source_row):
        count = len(tiles)
        for start in range(0, count, rows):
            acc = jnp.zeros((rows, cols), jnp.float32)
            for f in range(start, min(start + rows, count)):
                r = f - start
                acc = jnp.where(sub == r, rolled(tiles[f], (r - source_row) % rows, 0), acc)
            n = min(rows, count - start)
            ref[k, pl.ds(start, n), :] = acc[:n]

    def body(k, carry):
        cells = [p_ref[k], s_ref[k]]
        for half in range(2):
            cells += [d_ref[d, half, k] for d in range(ndir)]
        for half in range(2):
            cells += [w_ref[d, half, k] for d in range(ndir)]
        low_x = cells + [tx_ref[k], ux_ref[k].astype(jnp.float32)]
        low_y = cells + [ty_ref[k], uy_ref[k].astype(jnp.float32)]
        xl = jnp.zeros((rows, cols), jnp.float32)
        for f, t in enumerate(low_x):
            xl = jnp.where(lane == f, rolled(t, (f - (cols - 1)) % cols, 1), xl)
        xr = jnp.zeros((rows, cols), jnp.float32)
        for f, t in enumerate(cells):
            xr = jnp.where(lane == f, rolled(t, f % cols, 1), xr)
        xl_ref[k] = xl[:, : nf + 2]
        xr_ref[k] = xr[:, :nf]
        rows_into(yd_ref, k, low_y, rows - 1)
        rows_into(yu_ref, k, cells, 0)
        return carry

    lax.fori_loop(0, layers, body, 0)


def stencil_kernel(
    p_ref,
    s_ref,
    so_ref,
    pore_ref,
    tx_ref,
    ty_ref,
    tz_ref,
    ux_ref,
    uy_ref,
    uz_ref,
    d_ref,
    w_ref,
    pn_ref,
    sn_ref,
    dn_ref,
    wn_ref,
    hxl_ref,
    hxr_ref,
    hyd_ref,
    hyu_ref,
    spread_ref,
    r_out,
    jv_out,
    jt_out,
    carry_ref,
):
    ndir = d_ref.shape[0]
    span, rows, cols = p_ref.shape
    block = pl.program_id(0)
    layers = span * pl.num_programs(0)
    lane = lax.broadcasted_iota(jnp.int32, (rows, cols), 1)
    sub = lax.broadcasted_iota(jnp.int32, (rows, cols), 0)
    first_lane = lane == 0
    last_lane = lane == cols - 1
    first_sub = sub == 0
    last_sub = sub == rows - 1
    last_x = lax.axis_index("gx") == lax.axis_size("gx") - 1
    last_y = lax.axis_index(GY_WA) == lax.axis_size(GY_WA) - 1
    cut_x = jnp.logical_and(last_lane, last_x)
    cut_y = jnp.logical_and(last_sub, last_y)
    nf = 2 + 4 * ndir

    def cells_of(pr, sr, dr, wr, k):
        out = [pr[k], sr[k]]
        for half in range(2):
            out += [dr[d, half, k] for d in range(ndir)]
        for half in range(2):
            out += [wr[d, half, k] for d in range(ndir)]
        return out

    def group(flat):
        return (
            flat[0],
            flat[1],
            flat[2 : 2 + ndir],
            flat[2 + ndir : 2 + 2 * ndir],
            flat[2 + 2 * ndir : 2 + 3 * ndir],
            flat[2 + 3 * ndir : 2 + 4 * ndir],
        )

    def col(ref, k, f):
        return jnp.broadcast_to(ref[k, :, pl.ds(f, 1)], (rows, cols))

    def row(ref, k, f):
        return jnp.broadcast_to(ref[k, pl.ds(f, 1), :], (rows, cols))

    def store(k, vals):
        for i in range(nf):
            if i < 2:
                ref, idx, extra = r_out, (i, k), (0, i, k)
            elif i < 2 + 2 * ndir:
                j = i - 2
                ref, idx, extra = jv_out, (j % ndir, j // ndir, k), (1 + j % ndir, j // ndir, k)
            else:
                j = i - 2 - 2 * ndir
                ref, idx, extra = jt_out, (j % ndir, j // ndir, k), (1 + ndir + j % ndir, j // ndir, k)
            ref[idx] = vals[i] + spread_ref[extra]

    def layer(k, carry, above):
        here = cells_of(p_ref, s_ref, d_ref, w_ref, k)
        left = [jnp.where(first_lane, col(hxl_ref, k, f), pltpu.roll(x, 1, 1)) for f, x in enumerate(here)]
        right = [jnp.where(last_lane, col(hxr_ref, k, f), pltpu.roll(x, cols - 1, 1)) for f, x in enumerate(here)]
        down = [jnp.where(first_sub, row(hyd_ref, k, f), pltpu.roll(x, 1, 0)) for f, x in enumerate(here)]
        up_ = [jnp.where(last_sub, row(hyu_ref, k, f), pltpu.roll(x, rows - 1, 0)) for f, x in enumerate(here)]

        tx = tx_ref[k]
        ux = ux_ref[k].astype(jnp.float32)
        ty = ty_ref[k]
        uy = uy_ref[k].astype(jnp.float32)
        tx_f = jnp.where(cut_x, 0.0, tx)
        ty_f = jnp.where(cut_y, 0.0, ty)
        tx_b = jnp.where(first_lane, col(hxl_ref, k, nf), pltpu.roll(tx, 1, 1))
        ux_b = jnp.where(first_lane, col(hxl_ref, k, nf + 1), pltpu.roll(ux, 1, 1))
        ty_b = jnp.where(first_sub, row(hyd_ref, k, nf), pltpu.roll(ty, 1, 0))
        uy_b = jnp.where(first_sub, row(hyd_ref, k, nf + 1), pltpu.roll(uy, 1, 0))
        tz = jnp.where(block * span + k < layers - 1, tz_ref[k], 0.0)
        uz = uz_ref[k] == 1

        g_here = group(here)
        acc, _ = face_terms(tx_f, ux > 0.5, g_here, group(right), (0.0, 0.0), ndir)
        _, xb = face_terms(tx_b, ux_b > 0.5, group(left), g_here, (0.0, 0.0), ndir)
        yf, _ = face_terms(ty_f, uy > 0.5, g_here, group(up_), (0.0, 0.0), ndir)
        _, yb = face_terms(ty_b, uy_b > 0.5, group(down), g_here, (0.0, 0.0), ndir)
        zf, zb = face_terms(tz, uz, g_here, group(above), (water_head, oil_head), ndir)
        acc = [a + b + c + e for a, b, c, e in zip(acc, xb, yf, yb)]
        acc = [a + z for a, z in zip(acc, zf)]

        change = here[1] - so_ref[k]
        pore = pore_ref[k]
        acc[0] = acc[0] + pore * change
        acc[1] = acc[1] - pore * change
        for d in range(ndir):
            vs = here[2 + ndir + d]
            acc[2 + d] = acc[2 + d] + pore * vs
            acc[2 + ndir + d] = acc[2 + ndir + d] - pore * vs
            jt_s = 2 + 3 * ndir + d
            acc[jt_s] = acc[jt_s] + pore * (here[2 + 2 * ndir + d] - here[2 + 3 * ndir + d])
        acc = [a + c for a, c in zip(acc, carry)]
        store(k, acc)
        return tuple(zb)

    @pl.when(block == 0)
    def _():
        carry_ref[...] = jnp.zeros_like(carry_ref)

    def inner(k, carry):
        return layer(k, carry, cells_of(p_ref, s_ref, d_ref, w_ref, k + 1))

    carry = tuple(carry_ref[i] for i in range(nf))
    carry = lax.fori_loop(0, span - 1, inner, carry)
    carry = layer(span - 1, carry, cells_of(pn_ref, sn_ref, dn_ref, wn_ref, 0))
    for i in range(nf):
        carry_ref[i] = carry[i]


def body(
    pressure,
    saturation,
    sat_old,
    pore,
    trans_x,
    trans_y,
    trans_z,
    upwind_x,
    upwind_y,
    upwind_z,
    directions,
    adjoint_weights,
    perf_well,
    perf_col,
    perf_top,
    perf_span,
    perf_index,
    bhp,
    target,
):
    layers, rows, cols = pressure.shape
    spatial = (layers, rows, cols)
    ndir = directions.shape[0]

    nf = 2 + 4 * ndir
    vmem = pl.BlockSpec(memory_space=pltpu.VMEM)
    x_low, x_high, y_low, y_high = pl.pallas_call(
        pack_kernel,
        out_shape=[
            jax.ShapeDtypeStruct((layers, rows, nf + 2), jnp.float32),
            jax.ShapeDtypeStruct((layers, rows, nf), jnp.float32),
            jax.ShapeDtypeStruct((layers, nf + 2, cols), jnp.float32),
            jax.ShapeDtypeStruct((layers, nf, cols), jnp.float32),
        ],
        in_specs=[vmem] * 8,
        out_specs=[vmem] * 4,
        cost_estimate=pl.CostEstimate(
            flops=layers * rows * cols * 160,
            transcendentals=0,
            bytes_accessed=(6 + 4 * ndir) * layers * rows * cols * 4,
        ),
    )(pressure, saturation, directions, adjoint_weights, trans_x, upwind_x, trans_y, upwind_y)
    x_low, x_high, y_low, y_high, pressure, saturation, directions, adjoint_weights = lax.optimization_barrier(
        (x_low, x_high, y_low, y_high, pressure, saturation, directions, adjoint_weights)
    )
    hxl = shift_along(x_low, "gx", True)
    hxr = shift_along(x_high, "gx", False)
    hyd = shift_along(y_low, GY_WA, True)
    hyu = shift_along(y_high, GY_WA, False)

    lane_hit = (jnp.arange(cols)[:, None] == (perf_col % cols)[None, :]).astype(jnp.float32)
    row_hit = (jnp.arange(rows)[:, None] == (perf_col // cols)[None, :]).astype(jnp.float32)

    def at_perfs(field):
        by_lane = jnp.dot(field, lane_hit, precision=lax.Precision.HIGHEST)
        return jnp.sum(by_lane * row_hit, axis=-2)

    p_cells = at_perfs(pressure)
    s_cells = at_perfs(saturation)
    dir_cells = at_perfs(directions)
    wts_cells = at_perfs(adjoint_weights)
    depth = jnp.arange(layers)[:, None]
    open_layer = jnp.logical_and(
        depth >= perf_top[None, :], depth < (perf_top + perf_span)[None, :]
    )
    weight = jnp.where(open_layer, perf_index[None, :], 0.0)
    row_bhp, row_target = jnp.take(jnp.stack([bhp, target]), perf_well, axis=1)
    drive = p_cells - row_bhp
    mob = mobility(s_cells)
    slope = mobility_slope(s_cells)
    mob_total = mob[0] + mob[1]
    slope_total = slope[0] + slope[1]
    rates = weight * mob * drive
    rate_tangent = weight * (mob * dir_cells[:, 0:1] + slope * drive * dir_cells[:, 1:2])
    grad_p = weight * (mob[0] * wts_cells[:, 0] + mob[1] * wts_cells[:, 1])
    grad_s = weight * drive * (slope[0] * wts_cells[:, 0] + slope[1] * wts_cells[:, 1])
    row_sums = jnp.concatenate(
        [
            jnp.sum(weight * mob_total, axis=0)[None],
            jnp.sum(rates[0] + rates[1], axis=0)[None],
            jnp.sum(rate_tangent[:, 0] + rate_tangent[:, 1], axis=1),
            jnp.sum(grad_p, axis=1),
        ],
        axis=0,
    )
    packed = jnp.concatenate([row_sums, perf_well.astype(jnp.float32)[None]], axis=0)
    everyone = gather_everywhere(packed)


    all_sums = jnp.moveaxis(everyone[:, :-1], 1, 0).reshape(row_sums.shape[0], -1)
    all_wells = everyone[:, -1].reshape(-1)
    same_well = (perf_well.astype(jnp.float32)[:, None] == all_wells[None, :]).astype(jnp.float32)
    row_totals = jnp.dot(all_sums, same_well.T, precision=lax.Precision.HIGHEST)
    row_factors = well_factors(row_totals, row_target)
    wells_res = rates - weight * mob * row_factors[0]
    wells_fwd = rate_tangent - (weight * mob)[None] * row_factors[1 : 1 + ndir][:, None, None, :]
    out_f = row_factors[1 + ndir :][:, None, :]
    wells_adj = jnp.stack(
        [grad_p - weight * mob_total * out_f, grad_s - weight * slope_total * drive * out_f], axis=1
    )
    combined = jnp.concatenate([wells_res[None], wells_fwd, wells_adj], axis=0)
    by_row = combined[..., None, :] * row_hit
    spread = jnp.dot(by_row, lane_hit.T, precision=lax.Precision.HIGHEST)

    span = 6 if layers % 6 == 0 else layers
    blocks = layers // span

    def layer_block(*lead):
        return pl.BlockSpec(tuple(lead) + (span, rows, cols), lambda b: (0,) * len(lead) + (b, 0, 0))

    def next_layer(*lead):
        return pl.BlockSpec(
            tuple(lead) + (1, rows, cols),
            lambda b: (0,) * len(lead) + (jnp.minimum((b + 1) * span, layers - 1), 0, 0),
        )

    def halo_block(mid, last):
        return pl.BlockSpec((span, mid, last), lambda b: (b, 0, 0))

    reduced_residual, forward_products, adjoint_products = pl.pallas_call(
        stencil_kernel,
        grid=(blocks,),
        out_shape=[
            jax.ShapeDtypeStruct((2,) + spatial, jnp.float32),
            jax.ShapeDtypeStruct((ndir, 2) + spatial, jnp.float32),
            jax.ShapeDtypeStruct((ndir, 2) + spatial, jnp.float32),
        ],
        in_specs=[layer_block()] * 10
        + [layer_block(ndir, 2)] * 2
        + [next_layer()] * 2
        + [next_layer(ndir, 2)] * 2
        + [
            halo_block(rows, nf + 2),
            halo_block(rows, nf),
            halo_block(nf + 2, cols),
            halo_block(nf, cols),
            layer_block(1 + 2 * ndir, 2),
        ],
        out_specs=[layer_block(2), layer_block(ndir, 2), layer_block(ndir, 2)],
        scratch_shapes=[pltpu.VMEM((nf, rows, cols), jnp.float32)],
        compiler_params=pltpu.CompilerParams(dimension_semantics=("arbitrary",)),
        cost_estimate=pl.CostEstimate(
            flops=layers * rows * cols * 1200,
            transcendentals=0,
            bytes_accessed=(10 + 4 * 4 * ndir + 2 + 2 * 2 * ndir) * layers * rows * cols * 4,
        ),
    )(
        pressure,
        saturation,
        sat_old,
        pore,
        trans_x,
        trans_y,
        trans_z,
        upwind_x,
        upwind_y,
        upwind_z,
        directions,
        adjoint_weights,
        pressure,
        saturation,
        directions,
        adjoint_weights,
        hxl,
        hxr,
        hyd,
        hyu,
        spread,
    )
    return (reduced_residual, forward_products, adjoint_products)


def solution(mesh):
    split = Mesh(
        mesh.devices.reshape(mesh.shape["gx"], 4, 4, mesh.shape["wa"]), ("gx", "gy_0", "gy_1", "wa")
    )
    return jax.shard_map(
        body,
        mesh=split,
        in_specs=(
            P(None, GY_WA, "gx"),
            P(None, GY_WA, "gx"),
            P(None, GY_WA, "gx"),
            P(None, GY_WA, "gx"),
            P(None, GY_WA, "gx"),
            P(None, GY_WA, "gx"),
            P(None, GY_WA, "gx"),
            P(None, GY_WA, "gx"),
            P(None, GY_WA, "gx"),
            P(None, GY_WA, "gx"),
            P(None, None, None, GY_WA, "gx"),
            P(None, None, None, GY_WA, "gx"),
            P(GX_GY_WA),
            P(GX_GY_WA),
            P(GX_GY_WA),
            P(GX_GY_WA),
            P(GX_GY_WA),
            P(),
            P(),
        ),
        out_specs=(
            P(None, None, GY_WA, "gx"),
            P(None, None, None, GY_WA, "gx"),
            P(None, None, None, GY_WA, "gx"),
        ),
        check_vma=False,
    )
```

```python
import jax
import jax.numpy as jnp
from jax import lax
from jax.experimental import pallas as pl
from jax.experimental.pallas import tpu as pltpu
from jax.sharding import Mesh
from jax.sharding import PartitionSpec as P


GY_WA = ("gy_0", "gy_1", "wa")
GX_GY_WA = ("gx", "gy_0", "gy_1", "wa")


water_visc = 0.5
oil_visc = 2.0
water_head = 0.3
oil_head = 0.2


def gather_everywhere(block):
    peers = lax.axis_size(GX_GY_WA)
    flat = jnp.broadcast_to(block.reshape(1, -1), (peers, block.size))
    return lax.all_to_all(flat, GX_GY_WA, 0, 0, tiled=True).reshape((peers,) + block.shape)


def shift_along(block, axis, down):
    size = lax.axis_size(axis)
    pairs = [(i, i + 1) for i in range(size - 1)]
    if not down:
        pairs = [(b, a) for a, b in pairs]
    return lax.ppermute(block, axis, pairs)


def mobility(sat):
    return jnp.stack([sat * sat / water_visc, (1.0 - sat) * (1.0 - sat) / oil_visc])


def mobility_slope(sat):
    return jnp.stack([2.0 * sat / water_visc, -2.0 * (1.0 - sat) / oil_visc])


def well_factors(sums, goal):
    return jnp.concatenate([((sums[1] - goal) / sums[0])[None], sums[2:] / sums[0][None]], axis=0)


def face_terms(trans, up, a, b, heads, ndir):
    pa, sa, vpa, vsa, wwa, woa = a
    pb, sb, vpb, vsb, wwb, wob = b
    su = jnp.where(up, sa, sb)
    drop = pa - pb
    pot_w = drop + heads[0]
    pot_o = drop + heads[1]
    tl_w = trans * (su * su / water_visc)
    tl_o = trans * ((1.0 - su) * (1.0 - su) / oil_visc)
    f_w = tl_w * pot_w
    f_o = tl_o * pot_o
    td_w = trans * (2.0 * su / water_visc) * pot_w
    td_o = trans * (-2.0 * (1.0 - su) / oil_visc) * pot_o
    jv_w, jv_o, jt_p, jt_s = [], [], [], []
    for d in range(ndir):
        vsu = jnp.where(up, vsa[d], vsb[d])
        dvp = vpa[d] - vpb[d]
        jv_w.append(td_w * vsu + tl_w * dvp)
        jv_o.append(td_o * vsu + tl_o * dvp)
        dww = wwa[d] - wwb[d]
        dwo = woa[d] - wob[d]
        jt_p.append(dww * tl_w + dwo * tl_o)
        jt_s.append(dww * td_w + dwo * td_o)
    zero = jnp.zeros_like(su)
    as_a = [f_w, f_o] + jv_w + jv_o + jt_p + [jnp.where(up, g, zero) for g in jt_s]
    as_b = [-f_w, -f_o] + [-x for x in jv_w] + [-x for x in jv_o] + [-x for x in jt_p]
    as_b = as_b + [jnp.where(up, zero, g) for g in jt_s]
    return as_a, as_b


def pack_kernel(p_ref, s_ref, d_ref, w_ref, tx_ref, ux_ref, ty_ref, uy_ref, xl_ref, xr_ref, yd_ref, yu_ref):
    ndir = d_ref.shape[0]
    layers, rows, cols = p_ref.shape
    lane = lax.broadcasted_iota(jnp.int32, (rows, cols), 1)
    sub = lax.broadcasted_iota(jnp.int32, (rows, cols), 0)
    nf = 2 + 4 * ndir

    def rolled(x, shift, axis):
        return x if shift == 0 else pltpu.roll(x, shift, axis)

    def rows_into(ref, k, tiles, source_row):
        count = len(tiles)
        for start in range(0, count, rows):
            acc = jnp.zeros((rows, cols), jnp.float32)
            for f in range(start, min(start + rows, count)):
                r = f - start
                acc = jnp.where(sub == r, rolled(tiles[f], (r - source_row) % rows, 0), acc)
            n = min(rows, count - start)
            ref[k, pl.ds(start, n), :] = acc[:n]

    def body(k, carry):
        cells = [p_ref[k], s_ref[k]]
        for half in range(2):
            cells += [d_ref[d, half, k] for d in range(ndir)]
        for half in range(2):
            cells += [w_ref[d, half, k] for d in range(ndir)]
        low_x = cells + [tx_ref[k], ux_ref[k].astype(jnp.float32)]
        low_y = cells + [ty_ref[k], uy_ref[k].astype(jnp.float32)]
        xl = jnp.zeros((rows, cols), jnp.float32)
        for f, t in enumerate(low_x):
            xl = jnp.where(lane == f, rolled(t, (f - (cols - 1)) % cols, 1), xl)
        xr = jnp.zeros((rows, cols), jnp.float32)
        for f, t in enumerate(cells):
            xr = jnp.where(lane == f, rolled(t, f % cols, 1), xr)
        xl_ref[k] = xl[:, : nf + 2]
        xr_ref[k] = xr[:, :nf]
        rows_into(yd_ref, k, low_y, rows - 1)
        rows_into(yu_ref, k, cells, 0)
        return carry

    lax.fori_loop(0, layers, body, 0)


def stencil_kernel(
    p_ref,
    s_ref,
    so_ref,
    pore_ref,
    tx_ref,
    ty_ref,
    tz_ref,
    ux_ref,
    uy_ref,
    uz_ref,
    d_ref,
    w_ref,
    pn_ref,
    sn_ref,
    dn_ref,
    wn_ref,
    hxl_ref,
    hxr_ref,
    hyd_ref,
    hyu_ref,
    r_out,
    jv_out,
    jt_out,
    carry_ref,
):
    ndir = d_ref.shape[0]
    span, rows, cols = p_ref.shape
    block = pl.program_id(0)
    layers = span * pl.num_programs(0)
    lane = lax.broadcasted_iota(jnp.int32, (rows, cols), 1)
    sub = lax.broadcasted_iota(jnp.int32, (rows, cols), 0)
    first_lane = lane == 0
    last_lane = lane == cols - 1
    first_sub = sub == 0
    last_sub = sub == rows - 1
    last_x = lax.axis_index("gx") == lax.axis_size("gx") - 1
    last_y = lax.axis_index(GY_WA) == lax.axis_size(GY_WA) - 1
    cut_x = jnp.logical_and(last_lane, last_x)
    cut_y = jnp.logical_and(last_sub, last_y)
    nf = 2 + 4 * ndir

    def cells_of(pr, sr, dr, wr, k):
        out = [pr[k], sr[k]]
        for half in range(2):
            out += [dr[d, half, k] for d in range(ndir)]
        for half in range(2):
            out += [wr[d, half, k] for d in range(ndir)]
        return out

    def group(flat):
        return (
            flat[0],
            flat[1],
            flat[2 : 2 + ndir],
            flat[2 + ndir : 2 + 2 * ndir],
            flat[2 + 2 * ndir : 2 + 3 * ndir],
            flat[2 + 3 * ndir : 2 + 4 * ndir],
        )

    def col(ref, k, f):
        return jnp.broadcast_to(ref[k, :, pl.ds(f, 1)], (rows, cols))

    def row(ref, k, f):
        return jnp.broadcast_to(ref[k, pl.ds(f, 1), :], (rows, cols))

    def store(k, vals):
        for i in range(nf):
            if i < 2:
                ref, idx = r_out, (i, k)
            elif i < 2 + 2 * ndir:
                j = i - 2
                ref, idx = jv_out, (j % ndir, j // ndir, k)
            else:
                j = i - 2 - 2 * ndir
                ref, idx = jt_out, (j % ndir, j // ndir, k)
            ref[idx] = vals[i]

    def layer(k, carry, above):
        here = cells_of(p_ref, s_ref, d_ref, w_ref, k)
        left = [jnp.where(first_lane, col(hxl_ref, k, f), pltpu.roll(x, 1, 1)) for f, x in enumerate(here)]
        right = [jnp.where(last_lane, col(hxr_ref, k, f), pltpu.roll(x, cols - 1, 1)) for f, x in enumerate(here)]
        down = [jnp.where(first_sub, row(hyd_ref, k, f), pltpu.roll(x, 1, 0)) for f, x in enumerate(here)]
        up_ = [jnp.where(last_sub, row(hyu_ref, k, f), pltpu.roll(x, rows - 1, 0)) for f, x in enumerate(here)]

        tx = tx_ref[k]
        ux = ux_ref[k].astype(jnp.float32)
        ty = ty_ref[k]
        uy = uy_ref[k].astype(jnp.float32)
        tx_f = jnp.where(cut_x, 0.0, tx)
        ty_f = jnp.where(cut_y, 0.0, ty)
        tx_b = jnp.where(first_lane, col(hxl_ref, k, nf), pltpu.roll(tx, 1, 1))
        ux_b = jnp.where(first_lane, col(hxl_ref, k, nf + 1), pltpu.roll(ux, 1, 1))
        ty_b = jnp.where(first_sub, row(hyd_ref, k, nf), pltpu.roll(ty, 1, 0))
        uy_b = jnp.where(first_sub, row(hyd_ref, k, nf + 1), pltpu.roll(uy, 1, 0))
        tz = jnp.where(block * span + k < layers - 1, tz_ref[k], 0.0)
        uz = uz_ref[k] == 1

        g_here = group(here)
        acc, _ = face_terms(tx_f, ux > 0.5, g_here, group(right), (0.0, 0.0), ndir)
        _, xb = face_terms(tx_b, ux_b > 0.5, group(left), g_here, (0.0, 0.0), ndir)
        yf, _ = face_terms(ty_f, uy > 0.5, g_here, group(up_), (0.0, 0.0), ndir)
        _, yb = face_terms(ty_b, uy_b > 0.5, group(down), g_here, (0.0, 0.0), ndir)
        zf, zb = face_terms(tz, uz, g_here, group(above), (water_head, oil_head), ndir)
        acc = [a + b + c + e for a, b, c, e in zip(acc, xb, yf, yb)]
        acc = [a + z for a, z in zip(acc, zf)]

        change = here[1] - so_ref[k]
        pore = pore_ref[k]
        acc[0] = acc[0] + pore * change
        acc[1] = acc[1] - pore * change
        for d in range(ndir):
            vs = here[2 + ndir + d]
            acc[2 + d] = acc[2 + d] + pore * vs
            acc[2 + ndir + d] = acc[2 + ndir + d] - pore * vs
            jt_s = 2 + 3 * ndir + d
            acc[jt_s] = acc[jt_s] + pore * (here[2 + 2 * ndir + d] - here[2 + 3 * ndir + d])
        acc = [a + c for a, c in zip(acc, carry)]
        store(k, acc)
        return tuple(zb)

    @pl.when(block == 0)
    def _():
        carry_ref[...] = jnp.zeros_like(carry_ref)

    def inner(k, carry):
        return layer(k, carry, cells_of(p_ref, s_ref, d_ref, w_ref, k + 1))

    carry = tuple(carry_ref[i] for i in range(nf))
    carry = lax.fori_loop(0, span - 1, inner, carry)
    carry = layer(span - 1, carry, cells_of(pn_ref, sn_ref, dn_ref, wn_ref, 0))
    for i in range(nf):
        carry_ref[i] = carry[i]


def layer_body(
    pressure,
    saturation,
    sat_old,
    pore,
    trans_x,
    trans_y,
    trans_z,
    upwind_x,
    upwind_y,
    upwind_z,
    directions,
    adjoint_weights,
    perf_well,
    perf_col,
    perf_top,
    perf_span,
    perf_index,
    bhp,
    target,
):
    layers, rows, cols = pressure.shape
    spatial = (layers, rows, cols)
    ndir = directions.shape[0]

    nf = 2 + 4 * ndir
    vmem = pl.BlockSpec(memory_space=pltpu.VMEM)
    x_low, x_high, y_low, y_high = pl.pallas_call(
        pack_kernel,
        out_shape=[
            jax.ShapeDtypeStruct((layers, rows, nf + 2), jnp.float32),
            jax.ShapeDtypeStruct((layers, rows, nf), jnp.float32),
            jax.ShapeDtypeStruct((layers, nf + 2, cols), jnp.float32),
            jax.ShapeDtypeStruct((layers, nf, cols), jnp.float32),
        ],
        in_specs=[vmem] * 8,
        out_specs=[vmem] * 4,
        cost_estimate=pl.CostEstimate(
            flops=layers * rows * cols * 160,
            transcendentals=0,
            bytes_accessed=(6 + 4 * ndir) * layers * rows * cols * 4,
        ),
    )(pressure, saturation, directions, adjoint_weights, trans_x, upwind_x, trans_y, upwind_y)
    x_low, x_high, y_low, y_high, pressure, saturation, directions, adjoint_weights = lax.optimization_barrier(
        (x_low, x_high, y_low, y_high, pressure, saturation, directions, adjoint_weights)
    )
    hxl = shift_along(x_low, "gx", True)
    hxr = shift_along(x_high, "gx", False)
    hyd = shift_along(y_low, GY_WA, True)
    hyu = shift_along(y_high, GY_WA, False)

    lane_hit = (jnp.arange(cols)[:, None] == (perf_col % cols)[None, :]).astype(jnp.float32)
    row_hit = (jnp.arange(rows)[:, None] == (perf_col // cols)[None, :]).astype(jnp.float32)

    def at_perfs(field):
        by_lane = jnp.dot(field, lane_hit, precision=lax.Precision.HIGHEST)
        return jnp.sum(by_lane * row_hit, axis=-2)

    p_cells = at_perfs(pressure)
    s_cells = at_perfs(saturation)
    dir_cells = at_perfs(directions)
    wts_cells = at_perfs(adjoint_weights)
    depth = jnp.arange(layers)[:, None]
    open_layer = jnp.logical_and(
        depth >= perf_top[None, :], depth < (perf_top + perf_span)[None, :]
    )
    weight = jnp.where(open_layer, perf_index[None, :], 0.0)
    row_bhp, row_target = jnp.take(jnp.stack([bhp, target]), perf_well, axis=1)
    drive = p_cells - row_bhp
    mob = mobility(s_cells)
    slope = mobility_slope(s_cells)
    mob_total = mob[0] + mob[1]
    slope_total = slope[0] + slope[1]
    rates = weight * mob * drive
    rate_tangent = weight * (mob * dir_cells[:, 0:1] + slope * drive * dir_cells[:, 1:2])
    grad_p = weight * (mob[0] * wts_cells[:, 0] + mob[1] * wts_cells[:, 1])
    grad_s = weight * drive * (slope[0] * wts_cells[:, 0] + slope[1] * wts_cells[:, 1])
    row_sums = jnp.concatenate(
        [
            jnp.sum(weight * mob_total, axis=0)[None],
            jnp.sum(rates[0] + rates[1], axis=0)[None],
            jnp.sum(rate_tangent[:, 0] + rate_tangent[:, 1], axis=1),
            jnp.sum(grad_p, axis=1),
        ],
        axis=0,
    )
    packed = jnp.concatenate([row_sums, perf_well.astype(jnp.float32)[None]], axis=0)
    everyone = gather_everywhere(packed)


    all_sums = jnp.moveaxis(everyone[:, :-1], 1, 0).reshape(row_sums.shape[0], -1)
    all_wells = everyone[:, -1].reshape(-1)
    same_well = (perf_well.astype(jnp.float32)[:, None] == all_wells[None, :]).astype(jnp.float32)
    row_totals = jnp.dot(all_sums, same_well.T, precision=lax.Precision.HIGHEST)
    row_factors = well_factors(row_totals, row_target)
    wells_res = rates - weight * mob * row_factors[0]
    wells_fwd = rate_tangent - (weight * mob)[None] * row_factors[1 : 1 + ndir][:, None, None, :]
    out_f = row_factors[1 + ndir :][:, None, :]
    wells_adj = jnp.stack(
        [grad_p - weight * mob_total * out_f, grad_s - weight * slope_total * drive * out_f], axis=1
    )
    combined = jnp.concatenate([wells_res[None], wells_fwd, wells_adj], axis=0)
    by_row = combined[..., None, :] * row_hit
    spread = jnp.dot(by_row, lane_hit.T, precision=lax.Precision.HIGHEST)

    span = 6 if layers % 6 == 0 else layers
    blocks = layers // span

    def layer_block(*lead):
        return pl.BlockSpec(tuple(lead) + (span, rows, cols), lambda b: (0,) * len(lead) + (b, 0, 0))

    def next_layer(*lead):
        return pl.BlockSpec(
            tuple(lead) + (1, rows, cols),
            lambda b: (0,) * len(lead) + (jnp.minimum((b + 1) * span, layers - 1), 0, 0),
        )

    def halo_block(mid, last):
        return pl.BlockSpec((span, mid, last), lambda b: (b, 0, 0))

    flux = pl.pallas_call(
        stencil_kernel,
        grid=(blocks,),
        out_shape=[
            jax.ShapeDtypeStruct((2,) + spatial, jnp.float32),
            jax.ShapeDtypeStruct((ndir, 2) + spatial, jnp.float32),
            jax.ShapeDtypeStruct((ndir, 2) + spatial, jnp.float32),
        ],
        in_specs=[layer_block()] * 10
        + [layer_block(ndir, 2)] * 2
        + [next_layer()] * 2
        + [next_layer(ndir, 2)] * 2
        + [
            halo_block(rows, nf + 2),
            halo_block(rows, nf),
            halo_block(nf + 2, cols),
            halo_block(nf, cols),
        ],
        out_specs=[layer_block(2), layer_block(ndir, 2), layer_block(ndir, 2)],
        scratch_shapes=[pltpu.VMEM((nf, rows, cols), jnp.float32)],
        compiler_params=pltpu.CompilerParams(dimension_semantics=("arbitrary",)),
        cost_estimate=pl.CostEstimate(
            flops=layers * rows * cols * 1200,
            transcendentals=0,
            bytes_accessed=(10 + 4 * 4 * ndir + 2 + 2 * 2 * ndir) * layers * rows * cols * 4,
        ),
    )(
        pressure,
        saturation,
        sat_old,
        pore,
        trans_x,
        trans_y,
        trans_z,
        upwind_x,
        upwind_y,
        upwind_z,
        directions,
        adjoint_weights,
        pressure,
        saturation,
        directions,
        adjoint_weights,
        hxl,
        hxr,
        hyd,
        hyu,
    )
    reduced_residual, forward_products, adjoint_products = flux
    reduced_residual = reduced_residual + spread[0]
    forward_products = forward_products + spread[1 : 1 + ndir]
    adjoint_products = adjoint_products + spread[1 + ndir :]
    return (reduced_residual, forward_products, adjoint_products)


def solution(mesh):
    split = Mesh(
        mesh.devices.reshape(mesh.shape["gx"], 4, 4, mesh.shape["wa"]), ("gx", "gy_0", "gy_1", "wa")
    )
    return jax.shard_map(
        layer_body,
        mesh=split,
        in_specs=(
            P(None, GY_WA, "gx"),
            P(None, GY_WA, "gx"),
            P(None, GY_WA, "gx"),
            P(None, GY_WA, "gx"),
            P(None, GY_WA, "gx"),
            P(None, GY_WA, "gx"),
            P(None, GY_WA, "gx"),
            P(None, GY_WA, "gx"),
            P(None, GY_WA, "gx"),
            P(None, GY_WA, "gx"),
            P(None, None, None, GY_WA, "gx"),
            P(None, None, None, GY_WA, "gx"),
            P(GX_GY_WA),
            P(GX_GY_WA),
            P(GX_GY_WA),
            P(GX_GY_WA),
            P(GX_GY_WA),
            P(),
            P(),
        ),
        out_specs=(
            P(None, None, GY_WA, "gx"),
            P(None, None, None, GY_WA, "gx"),
            P(None, None, None, GY_WA, "gx"),
        ),
        check_vma=False,
    )
```

```python
import jax
import jax.numpy as jnp
from jax import lax
from jax.experimental import pallas as pl
from jax.experimental.pallas import tpu as pltpu
from jax.sharding import Mesh
from jax.sharding import PartitionSpec as P


GY_WA = ("gy_0", "gy_1", "wa")
GX_GY_WA = ("gx", "gy_0", "gy_1", "wa")


water_visc = 0.5
oil_visc = 2.0
water_head = 0.3
oil_head = 0.2


def gather_everywhere(block):
    peers = lax.axis_size(GX_GY_WA)
    flat = jnp.broadcast_to(block.reshape(1, -1), (peers, block.size))
    return lax.all_to_all(flat, GX_GY_WA, 0, 0, tiled=True).reshape((peers,) + block.shape)


def shift_along(block, axis, down):
    size = lax.axis_size(axis)
    pairs = [(i, i + 1) for i in range(size - 1)]
    if not down:
        pairs = [(b, a) for a, b in pairs]
    return lax.ppermute(block, axis, pairs)


def mobility(sat):
    return jnp.stack([sat * sat / water_visc, (1.0 - sat) * (1.0 - sat) / oil_visc])


def mobility_slope(sat):
    return jnp.stack([2.0 * sat / water_visc, -2.0 * (1.0 - sat) / oil_visc])


def well_factors(sums, goal):
    return jnp.concatenate([((sums[1] - goal) / sums[0])[None], sums[2:] / sums[0][None]], axis=0)


def face_terms(trans, up, a, b, heads, ndir):
    pa, sa, vpa, vsa, wwa, woa = a
    pb, sb, vpb, vsb, wwb, wob = b
    su = jnp.where(up, sa, sb)
    drop = pa - pb
    pot_w = drop + heads[0]
    pot_o = drop + heads[1]
    tl_w = trans * (su * su / water_visc)
    tl_o = trans * ((1.0 - su) * (1.0 - su) / oil_visc)
    f_w = tl_w * pot_w
    f_o = tl_o * pot_o
    td_w = trans * (2.0 * su / water_visc) * pot_w
    td_o = trans * (-2.0 * (1.0 - su) / oil_visc) * pot_o
    jv_w, jv_o, jt_p, jt_s = [], [], [], []
    for d in range(ndir):
        vsu = jnp.where(up, vsa[d], vsb[d])
        dvp = vpa[d] - vpb[d]
        jv_w.append(td_w * vsu + tl_w * dvp)
        jv_o.append(td_o * vsu + tl_o * dvp)
        dww = wwa[d] - wwb[d]
        dwo = woa[d] - wob[d]
        jt_p.append(dww * tl_w + dwo * tl_o)
        jt_s.append(dww * td_w + dwo * td_o)
    zero = jnp.zeros_like(su)
    as_a = [f_w, f_o] + jv_w + jv_o + jt_p + [jnp.where(up, g, zero) for g in jt_s]
    as_b = [-f_w, -f_o] + [-x for x in jv_w] + [-x for x in jv_o] + [-x for x in jt_p]
    as_b = as_b + [jnp.where(up, zero, g) for g in jt_s]
    return as_a, as_b


def pack_kernel(p_ref, s_ref, d_ref, w_ref, tx_ref, ux_ref, ty_ref, uy_ref, xl_ref, xr_ref, yd_ref, yu_ref):
    ndir = d_ref.shape[0]
    layers, rows, cols = p_ref.shape
    lane = lax.broadcasted_iota(jnp.int32, (rows, cols), 1)
    sub = lax.broadcasted_iota(jnp.int32, (rows, cols), 0)
    nf = 2 + 4 * ndir

    def rolled(x, shift, axis):
        return x if shift == 0 else pltpu.roll(x, shift, axis)

    def rows_into(ref, k, tiles, source_row):
        count = len(tiles)
        for start in range(0, count, rows):
            acc = jnp.zeros((rows, cols), jnp.float32)
            for f in range(start, min(start + rows, count)):
                r = f - start
                acc = jnp.where(sub == r, rolled(tiles[f], (r - source_row) % rows, 0), acc)
            n = min(rows, count - start)
            ref[k, pl.ds(start, n), :] = acc[:n]

    def body(k, carry):
        cells = [p_ref[k], s_ref[k]]
        for half in range(2):
            cells += [d_ref[d, half, k] for d in range(ndir)]
        for half in range(2):
            cells += [w_ref[d, half, k] for d in range(ndir)]
        low_x = cells + [tx_ref[k], ux_ref[k].astype(jnp.float32)]
        low_y = cells + [ty_ref[k], uy_ref[k].astype(jnp.float32)]
        xl = jnp.zeros((rows, cols), jnp.float32)
        for f, t in enumerate(low_x):
            xl = jnp.where(lane == f, rolled(t, (f - (cols - 1)) % cols, 1), xl)
        xr = jnp.zeros((rows, cols), jnp.float32)
        for f, t in enumerate(cells):
            xr = jnp.where(lane == f, rolled(t, f % cols, 1), xr)
        xl_ref[k] = xl[:, : nf + 2]
        xr_ref[k] = xr[:, :nf]
        rows_into(yd_ref, k, low_y, rows - 1)
        rows_into(yu_ref, k, cells, 0)
        return carry

    lax.fori_loop(0, layers, body, 0)


def stencil_kernel(
    p_ref,
    s_ref,
    so_ref,
    pore_ref,
    tx_ref,
    ty_ref,
    tz_ref,
    ux_ref,
    uy_ref,
    uz_ref,
    d_ref,
    w_ref,
    pn_ref,
    sn_ref,
    dn_ref,
    wn_ref,
    hxl_ref,
    hxr_ref,
    hyd_ref,
    hyu_ref,
    r_out,
    jv_out,
    jt_out,
    carry_ref,
):
    ndir = d_ref.shape[0]
    span, rows, cols = p_ref.shape
    block = pl.program_id(0)
    layers = span * pl.num_programs(0)
    lane = lax.broadcasted_iota(jnp.int32, (rows, cols), 1)
    sub = lax.broadcasted_iota(jnp.int32, (rows, cols), 0)
    first_lane = lane == 0
    last_lane = lane == cols - 1
    first_sub = sub == 0
    last_sub = sub == rows - 1
    last_x = lax.axis_index("gx") == lax.axis_size("gx") - 1
    last_y = lax.axis_index(GY_WA) == lax.axis_size(GY_WA) - 1
    cut_x = jnp.logical_and(last_lane, last_x)
    cut_y = jnp.logical_and(last_sub, last_y)
    nf = 2 + 4 * ndir

    def cells_of(pr, sr, dr, wr, k):
        out = [pr[k], sr[k]]
        for half in range(2):
            out += [dr[d, half, k] for d in range(ndir)]
        for half in range(2):
            out += [wr[d, half, k] for d in range(ndir)]
        return out

    def group(flat):
        return (
            flat[0],
            flat[1],
            flat[2 : 2 + ndir],
            flat[2 + ndir : 2 + 2 * ndir],
            flat[2 + 2 * ndir : 2 + 3 * ndir],
            flat[2 + 3 * ndir : 2 + 4 * ndir],
        )

    def col(ref, k, f):
        return jnp.broadcast_to(ref[k, :, pl.ds(f, 1)], (rows, cols))

    def row(ref, k, f):
        return jnp.broadcast_to(ref[k, pl.ds(f, 1), :], (rows, cols))

    def store(k, vals):
        for i in range(nf):
            if i < 2:
                ref, idx = r_out, (i, k)
            elif i < 2 + 2 * ndir:
                j = i - 2
                ref, idx = jv_out, (j % ndir, j // ndir, k)
            else:
                j = i - 2 - 2 * ndir
                ref, idx = jt_out, (j % ndir, j // ndir, k)
            ref[idx] = vals[i]

    def layer(k, carry, above):
        here = cells_of(p_ref, s_ref, d_ref, w_ref, k)
        left = [jnp.where(first_lane, col(hxl_ref, k, f), pltpu.roll(x, 1, 1)) for f, x in enumerate(here)]
        right = [jnp.where(last_lane, col(hxr_ref, k, f), pltpu.roll(x, cols - 1, 1)) for f, x in enumerate(here)]
        down = [jnp.where(first_sub, row(hyd_ref, k, f), pltpu.roll(x, 1, 0)) for f, x in enumerate(here)]
        up_ = [jnp.where(last_sub, row(hyu_ref, k, f), pltpu.roll(x, rows - 1, 0)) for f, x in enumerate(here)]

        tx = tx_ref[k]
        ux = ux_ref[k].astype(jnp.float32)
        ty = ty_ref[k]
        uy = uy_ref[k].astype(jnp.float32)
        tx_f = jnp.where(cut_x, 0.0, tx)
        ty_f = jnp.where(cut_y, 0.0, ty)
        tx_b = jnp.where(first_lane, col(hxl_ref, k, nf), pltpu.roll(tx, 1, 1))
        ux_b = jnp.where(first_lane, col(hxl_ref, k, nf + 1), pltpu.roll(ux, 1, 1))
        ty_b = jnp.where(first_sub, row(hyd_ref, k, nf), pltpu.roll(ty, 1, 0))
        uy_b = jnp.where(first_sub, row(hyd_ref, k, nf + 1), pltpu.roll(uy, 1, 0))
        tz = jnp.where(block * span + k < layers - 1, tz_ref[k], 0.0)
        uz = uz_ref[k] == 1

        g_here = group(here)
        acc, _ = face_terms(tx_f, ux > 0.5, g_here, group(right), (0.0, 0.0), ndir)
        _, xb = face_terms(tx_b, ux_b > 0.5, group(left), g_here, (0.0, 0.0), ndir)
        yf, _ = face_terms(ty_f, uy > 0.5, g_here, group(up_), (0.0, 0.0), ndir)
        _, yb = face_terms(ty_b, uy_b > 0.5, group(down), g_here, (0.0, 0.0), ndir)
        zf, zb = face_terms(tz, uz, g_here, group(above), (water_head, oil_head), ndir)
        acc = [a + b + c + e for a, b, c, e in zip(acc, xb, yf, yb)]
        acc = [a + z for a, z in zip(acc, zf)]

        change = here[1] - so_ref[k]
        pore = pore_ref[k]
        acc[0] = acc[0] + pore * change
        acc[1] = acc[1] - pore * change
        for d in range(ndir):
            vs = here[2 + ndir + d]
            acc[2 + d] = acc[2 + d] + pore * vs
            acc[2 + ndir + d] = acc[2 + ndir + d] - pore * vs
            jt_s = 2 + 3 * ndir + d
            acc[jt_s] = acc[jt_s] + pore * (here[2 + 2 * ndir + d] - here[2 + 3 * ndir + d])
        acc = [a + c for a, c in zip(acc, carry)]
        store(k, acc)
        return tuple(zb)

    @pl.when(block == 0)
    def _():
        carry_ref[...] = jnp.zeros_like(carry_ref)

    def inner(k, carry):
        return layer(k, carry, cells_of(p_ref, s_ref, d_ref, w_ref, k + 1))

    carry = tuple(carry_ref[i] for i in range(nf))
    carry = lax.fori_loop(0, span - 1, inner, carry)
    carry = layer(span - 1, carry, cells_of(pn_ref, sn_ref, dn_ref, wn_ref, 0))
    for i in range(nf):
        carry_ref[i] = carry[i]


def layer_body(
    pressure,
    saturation,
    sat_old,
    pore,
    trans_x,
    trans_y,
    trans_z,
    upwind_x,
    upwind_y,
    upwind_z,
    directions,
    adjoint_weights,
    perf_well,
    perf_col,
    perf_top,
    perf_span,
    perf_index,
    bhp,
    target,
):
    layers, rows, cols = pressure.shape
    spatial = (layers, rows, cols)
    ndir = directions.shape[0]

    nf = 2 + 4 * ndir
    vmem = pl.BlockSpec(memory_space=pltpu.VMEM)
    packs = pl.pallas_call(
        pack_kernel,
        out_shape=[
            jax.ShapeDtypeStruct((layers, rows, nf + 2), jnp.float32),
            jax.ShapeDtypeStruct((layers, rows, nf), jnp.float32),
            jax.ShapeDtypeStruct((layers, nf + 2, cols), jnp.float32),
            jax.ShapeDtypeStruct((layers, nf, cols), jnp.float32),
        ],
        in_specs=[vmem] * 8,
        out_specs=[vmem] * 4,
        cost_estimate=pl.CostEstimate(
            flops=layers * rows * cols * 160,
            transcendentals=0,
            bytes_accessed=(6 + 4 * ndir) * layers * rows * cols * 4,
        ),
    )(pressure, saturation, directions, adjoint_weights, trans_x, upwind_x, trans_y, upwind_y)
    x_low, x_high, y_low, y_high = packs
    hxl = shift_along(x_low, "gx", True)
    hxr = shift_along(x_high, "gx", False)
    hyd = shift_along(y_low, GY_WA, True)
    hyu = shift_along(y_high, GY_WA, False)

    lane_hit = (jnp.arange(cols)[:, None] == (perf_col % cols)[None, :]).astype(jnp.float32)
    row_hit = (jnp.arange(rows)[:, None] == (perf_col // cols)[None, :]).astype(jnp.float32)

    def at_perfs(field):
        by_lane = jnp.dot(field, lane_hit, precision=lax.Precision.HIGHEST)
        return jnp.sum(by_lane * row_hit, axis=-2)

    p_cells = at_perfs(pressure)
    s_cells = at_perfs(saturation)
    dir_cells = at_perfs(directions)
    wts_cells = at_perfs(adjoint_weights)
    depth = jnp.arange(layers)[:, None]
    open_layer = jnp.logical_and(
        depth >= perf_top[None, :], depth < (perf_top + perf_span)[None, :]
    )
    weight = jnp.where(open_layer, perf_index[None, :], 0.0)
    row_bhp, row_target = jnp.take(jnp.stack([bhp, target]), perf_well, axis=1)
    drive = p_cells - row_bhp
    mob = mobility(s_cells)
    slope = mobility_slope(s_cells)
    mob_total = mob[0] + mob[1]
    slope_total = slope[0] + slope[1]
    rates = weight * mob * drive
    rate_tangent = weight * (mob * dir_cells[:, 0:1] + slope * drive * dir_cells[:, 1:2])
    grad_p = weight * (mob[0] * wts_cells[:, 0] + mob[1] * wts_cells[:, 1])
    grad_s = weight * drive * (slope[0] * wts_cells[:, 0] + slope[1] * wts_cells[:, 1])
    row_sums = jnp.concatenate(
        [
            jnp.sum(weight * mob_total, axis=0)[None],
            jnp.sum(rates[0] + rates[1], axis=0)[None],
            jnp.sum(rate_tangent[:, 0] + rate_tangent[:, 1], axis=1),
            jnp.sum(grad_p, axis=1),
        ],
        axis=0,
    )
    packed = jnp.concatenate([row_sums, perf_well.astype(jnp.float32)[None]], axis=0)
    everyone = gather_everywhere(packed)


    all_sums = jnp.moveaxis(everyone[:, :-1], 1, 0).reshape(row_sums.shape[0], -1)
    all_wells = everyone[:, -1].reshape(-1)
    same_well = (perf_well.astype(jnp.float32)[:, None] == all_wells[None, :]).astype(jnp.float32)
    row_totals = jnp.dot(all_sums, same_well.T, precision=lax.Precision.HIGHEST)
    row_factors = well_factors(row_totals, row_target)
    wells_res = rates - weight * mob * row_factors[0]
    wells_fwd = rate_tangent - (weight * mob)[None] * row_factors[1 : 1 + ndir][:, None, None, :]
    out_f = row_factors[1 + ndir :][:, None, :]
    wells_adj = jnp.stack(
        [grad_p - weight * mob_total * out_f, grad_s - weight * slope_total * drive * out_f], axis=1
    )
    combined = jnp.concatenate([wells_res[None], wells_fwd, wells_adj], axis=0)
    by_row = combined[..., None, :] * row_hit
    spread = jnp.dot(by_row, lane_hit.T, precision=lax.Precision.HIGHEST)

    span = 6 if layers % 6 == 0 else layers
    blocks = layers // span

    def layer_block(*lead):
        return pl.BlockSpec(tuple(lead) + (span, rows, cols), lambda b: (0,) * len(lead) + (b, 0, 0))

    def next_layer(*lead):
        return pl.BlockSpec(
            tuple(lead) + (1, rows, cols),
            lambda b: (0,) * len(lead) + (jnp.minimum((b + 1) * span, layers - 1), 0, 0),
        )

    def halo_block(mid, last):
        return pl.BlockSpec((span, mid, last), lambda b: (b, 0, 0))

    flux = pl.pallas_call(
        stencil_kernel,
        grid=(blocks,),
        out_shape=[
            jax.ShapeDtypeStruct((2,) + spatial, jnp.float32),
            jax.ShapeDtypeStruct((ndir, 2) + spatial, jnp.float32),
            jax.ShapeDtypeStruct((ndir, 2) + spatial, jnp.float32),
        ],
        in_specs=[layer_block()] * 10
        + [layer_block(ndir, 2)] * 2
        + [next_layer()] * 2
        + [next_layer(ndir, 2)] * 2
        + [
            halo_block(rows, nf + 2),
            halo_block(rows, nf),
            halo_block(nf + 2, cols),
            halo_block(nf, cols),
        ],
        out_specs=[layer_block(2), layer_block(ndir, 2), layer_block(ndir, 2)],
        scratch_shapes=[pltpu.VMEM((nf, rows, cols), jnp.float32)],
        compiler_params=pltpu.CompilerParams(dimension_semantics=("arbitrary",)),
        cost_estimate=pl.CostEstimate(
            flops=layers * rows * cols * 1200,
            transcendentals=0,
            bytes_accessed=(10 + 4 * 4 * ndir + 2 + 2 * 2 * ndir) * layers * rows * cols * 4,
        ),
    )(
        pressure,
        saturation,
        sat_old,
        pore,
        trans_x,
        trans_y,
        trans_z,
        upwind_x,
        upwind_y,
        upwind_z,
        directions,
        adjoint_weights,
        pressure,
        saturation,
        directions,
        adjoint_weights,
        hxl,
        hxr,
        hyd,
        hyu,
    )
    reduced_residual, forward_products, adjoint_products = flux
    reduced_residual = reduced_residual + spread[0]
    forward_products = forward_products + spread[1 : 1 + ndir]
    adjoint_products = adjoint_products + spread[1 + ndir :]
    return (reduced_residual, forward_products, adjoint_products)


def solution(mesh):
    split = Mesh(
        mesh.devices.reshape(mesh.shape["gx"], 4, 4, mesh.shape["wa"]), ("gx", "gy_0", "gy_1", "wa")
    )
    return jax.shard_map(
        layer_body,
        mesh=split,
        in_specs=(
            P(None, GY_WA, "gx"),
            P(None, GY_WA, "gx"),
            P(None, GY_WA, "gx"),
            P(None, GY_WA, "gx"),
            P(None, GY_WA, "gx"),
            P(None, GY_WA, "gx"),
            P(None, GY_WA, "gx"),
            P(None, GY_WA, "gx"),
            P(None, GY_WA, "gx"),
            P(None, GY_WA, "gx"),
            P(None, None, None, GY_WA, "gx"),
            P(None, None, None, GY_WA, "gx"),
            P(GX_GY_WA),
            P(GX_GY_WA),
            P(GX_GY_WA),
            P(GX_GY_WA),
            P(GX_GY_WA),
            P(),
            P(),
        ),
        out_specs=(
            P(None, None, GY_WA, "gx"),
            P(None, None, None, GY_WA, "gx"),
            P(None, None, None, GY_WA, "gx"),
        ),
        check_vma=False,
    )
```

```python
import jax
import jax.numpy as jnp
from jax import lax
from jax.experimental import pallas as pl
from jax.experimental.pallas import tpu as pltpu
from jax.sharding import Mesh
from jax.sharding import PartitionSpec as P


GY_WA = ("gy_0", "gy_1", "wa")
GX_GY_WA = ("gx", "gy_0", "gy_1", "wa")


water_visc = 0.5
oil_visc = 2.0
water_head = 0.3
oil_head = 0.2


def gather_everywhere(block):
    peers = lax.axis_size(GX_GY_WA)
    flat = jnp.broadcast_to(block.reshape(1, -1), (peers, block.size))
    return lax.all_to_all(flat, GX_GY_WA, 0, 0, tiled=True).reshape((peers,) + block.shape)


def shift_along(block, axis, down):
    size = lax.axis_size(axis)
    pairs = [(i, i + 1) for i in range(size - 1)]
    if not down:
        pairs = [(b, a) for a, b in pairs]
    return lax.ppermute(block, axis, pairs)


def mobility(sat):
    return jnp.stack([sat * sat / water_visc, (1.0 - sat) * (1.0 - sat) / oil_visc])


def mobility_slope(sat):
    return jnp.stack([2.0 * sat / water_visc, -2.0 * (1.0 - sat) / oil_visc])


def well_factors(sums, goal):
    return jnp.concatenate([((sums[1] - goal) / sums[0])[None], sums[2:] / sums[0][None]], axis=0)


def face_terms(trans, up, a, b, heads, ndir):
    pa, sa, vpa, vsa, wwa, woa = a
    pb, sb, vpb, vsb, wwb, wob = b
    su = jnp.where(up, sa, sb)
    drop = pa - pb
    pot_w = drop + heads[0]
    pot_o = drop + heads[1]
    tl_w = trans * (su * su / water_visc)
    tl_o = trans * ((1.0 - su) * (1.0 - su) / oil_visc)
    f_w = tl_w * pot_w
    f_o = tl_o * pot_o
    td_w = trans * (2.0 * su / water_visc) * pot_w
    td_o = trans * (-2.0 * (1.0 - su) / oil_visc) * pot_o
    jv_w, jv_o, jt_p, jt_s = [], [], [], []
    for d in range(ndir):
        vsu = jnp.where(up, vsa[d], vsb[d])
        dvp = vpa[d] - vpb[d]
        jv_w.append(td_w * vsu + tl_w * dvp)
        jv_o.append(td_o * vsu + tl_o * dvp)
        dww = wwa[d] - wwb[d]
        dwo = woa[d] - wob[d]
        jt_p.append(dww * tl_w + dwo * tl_o)
        jt_s.append(dww * td_w + dwo * td_o)
    zero = jnp.zeros_like(su)
    as_a = [f_w, f_o] + jv_w + jv_o + jt_p + [jnp.where(up, g, zero) for g in jt_s]
    as_b = [-f_w, -f_o] + [-x for x in jv_w] + [-x for x in jv_o] + [-x for x in jt_p]
    as_b = as_b + [jnp.where(up, zero, g) for g in jt_s]
    return as_a, as_b


def pack_kernel(p_ref, s_ref, d_ref, w_ref, tx_ref, ux_ref, ty_ref, uy_ref, xl_ref, xr_ref, yd_ref, yu_ref):
    ndir = d_ref.shape[0]
    layers, rows, cols = p_ref.shape
    lane = lax.broadcasted_iota(jnp.int32, (rows, cols), 1)
    sub = lax.broadcasted_iota(jnp.int32, (rows, cols), 0)
    nf = 2 + 4 * ndir

    def rolled(x, shift, axis):
        return x if shift == 0 else pltpu.roll(x, shift, axis)

    def rows_into(ref, k, tiles, source_row):
        count = len(tiles)
        for start in range(0, count, rows):
            acc = jnp.zeros((rows, cols), jnp.float32)
            for f in range(start, min(start + rows, count)):
                r = f - start
                acc = jnp.where(sub == r, rolled(tiles[f], (r - source_row) % rows, 0), acc)
            n = min(rows, count - start)
            ref[k, pl.ds(start, n), :] = acc[:n]

    def body(k, carry):
        cells = [p_ref[k], s_ref[k]]
        for half in range(2):
            cells += [d_ref[d, half, k] for d in range(ndir)]
        for half in range(2):
            cells += [w_ref[d, half, k] for d in range(ndir)]
        low_x = cells + [tx_ref[k], ux_ref[k].astype(jnp.float32)]
        low_y = cells + [ty_ref[k], uy_ref[k].astype(jnp.float32)]
        xl = jnp.zeros((rows, cols), jnp.float32)
        for f, t in enumerate(low_x):
            xl = jnp.where(lane == f, rolled(t, (f - (cols - 1)) % cols, 1), xl)
        xr = jnp.zeros((rows, cols), jnp.float32)
        for f, t in enumerate(cells):
            xr = jnp.where(lane == f, rolled(t, f % cols, 1), xr)
        xl_ref[k] = xl[:, : nf + 2]
        xr_ref[k] = xr[:, :nf]
        rows_into(yd_ref, k, low_y, rows - 1)
        rows_into(yu_ref, k, cells, 0)
        return carry

    lax.fori_loop(0, layers, body, 0)


def stencil_kernel(
    p_ref,
    s_ref,
    so_ref,
    pore_ref,
    tx_ref,
    ty_ref,
    tz_ref,
    ux_ref,
    uy_ref,
    uz_ref,
    d_ref,
    w_ref,
    pn_ref,
    sn_ref,
    dn_ref,
    wn_ref,
    hxl_ref,
    hxr_ref,
    hyd_ref,
    hyu_ref,
    r_out,
    jv_out,
    jt_out,
    carry_ref,
):
    ndir = d_ref.shape[0]
    span, rows, cols = p_ref.shape
    block = pl.program_id(0)
    layers = span * pl.num_programs(0)
    lane = lax.broadcasted_iota(jnp.int32, (rows, cols), 1)
    sub = lax.broadcasted_iota(jnp.int32, (rows, cols), 0)
    first_lane = lane == 0
    last_lane = lane == cols - 1
    first_sub = sub == 0
    last_sub = sub == rows - 1
    last_x = lax.axis_index("gx") == lax.axis_size("gx") - 1
    last_y = lax.axis_index(GY_WA) == lax.axis_size(GY_WA) - 1
    cut_x = jnp.logical_and(last_lane, last_x)
    cut_y = jnp.logical_and(last_sub, last_y)
    nf = 2 + 4 * ndir

    def cells_of(pr, sr, dr, wr, k):
        out = [pr[k], sr[k]]
        for half in range(2):
            out += [dr[d, half, k] for d in range(ndir)]
        for half in range(2):
            out += [wr[d, half, k] for d in range(ndir)]
        return out

    def group(flat):
        return (
            flat[0],
            flat[1],
            flat[2 : 2 + ndir],
            flat[2 + ndir : 2 + 2 * ndir],
            flat[2 + 2 * ndir : 2 + 3 * ndir],
            flat[2 + 3 * ndir : 2 + 4 * ndir],
        )

    def col(ref, k, f):
        return jnp.broadcast_to(ref[k, :, pl.ds(f, 1)], (rows, cols))

    def row(ref, k, f):
        return jnp.broadcast_to(ref[k, pl.ds(f, 1), :], (rows, cols))

    def store(k, vals):
        for i in range(nf):
            if i < 2:
                ref, idx = r_out, (i, k)
            elif i < 2 + 2 * ndir:
                j = i - 2
                ref, idx = jv_out, (j % ndir, j // ndir, k)
            else:
                j = i - 2 - 2 * ndir
                ref, idx = jt_out, (j % ndir, j // ndir, k)
            ref[idx] = vals[i]

    def layer(k, carry, above):
        here = cells_of(p_ref, s_ref, d_ref, w_ref, k)
        left = [jnp.where(first_lane, col(hxl_ref, k, f), pltpu.roll(x, 1, 1)) for f, x in enumerate(here)]
        right = [jnp.where(last_lane, col(hxr_ref, k, f), pltpu.roll(x, cols - 1, 1)) for f, x in enumerate(here)]
        down = [jnp.where(first_sub, row(hyd_ref, k, f), pltpu.roll(x, 1, 0)) for f, x in enumerate(here)]
        up_ = [jnp.where(last_sub, row(hyu_ref, k, f), pltpu.roll(x, rows - 1, 0)) for f, x in enumerate(here)]

        tx = tx_ref[k]
        ux = ux_ref[k].astype(jnp.float32)
        ty = ty_ref[k]
        uy = uy_ref[k].astype(jnp.float32)
        tx_f = jnp.where(cut_x, 0.0, tx)
        ty_f = jnp.where(cut_y, 0.0, ty)
        tx_b = jnp.where(first_lane, col(hxl_ref, k, nf), pltpu.roll(tx, 1, 1))
        ux_b = jnp.where(first_lane, col(hxl_ref, k, nf + 1), pltpu.roll(ux, 1, 1))
        ty_b = jnp.where(first_sub, row(hyd_ref, k, nf), pltpu.roll(ty, 1, 0))
        uy_b = jnp.where(first_sub, row(hyd_ref, k, nf + 1), pltpu.roll(uy, 1, 0))
        tz = jnp.where(block * span + k < layers - 1, tz_ref[k], 0.0)
        uz = uz_ref[k] == 1

        g_here = group(here)
        acc, _ = face_terms(tx_f, ux > 0.5, g_here, group(right), (0.0, 0.0), ndir)
        _, xb = face_terms(tx_b, ux_b > 0.5, group(left), g_here, (0.0, 0.0), ndir)
        yf, _ = face_terms(ty_f, uy > 0.5, g_here, group(up_), (0.0, 0.0), ndir)
        _, yb = face_terms(ty_b, uy_b > 0.5, group(down), g_here, (0.0, 0.0), ndir)
        zf, zb = face_terms(tz, uz, g_here, group(above), (water_head, oil_head), ndir)
        acc = [a + b + c + e for a, b, c, e in zip(acc, xb, yf, yb)]
        acc = [a + z for a, z in zip(acc, zf)]

        change = here[1] - so_ref[k]
        pore = pore_ref[k]
        acc[0] = acc[0] + pore * change
        acc[1] = acc[1] - pore * change
        for d in range(ndir):
            vs = here[2 + ndir + d]
            acc[2 + d] = acc[2 + d] + pore * vs
            acc[2 + ndir + d] = acc[2 + ndir + d] - pore * vs
            jt_s = 2 + 3 * ndir + d
            acc[jt_s] = acc[jt_s] + pore * (here[2 + 2 * ndir + d] - here[2 + 3 * ndir + d])
        acc = [a + c for a, c in zip(acc, carry)]
        store(k, acc)
        return tuple(zb)

    @pl.when(block == 0)
    def _():
        carry_ref[...] = jnp.zeros_like(carry_ref)

    def inner(k, carry):
        return layer(k, carry, cells_of(p_ref, s_ref, d_ref, w_ref, k + 1))

    carry = tuple(carry_ref[i] for i in range(nf))
    carry = lax.fori_loop(0, span - 1, inner, carry)
    carry = layer(span - 1, carry, cells_of(pn_ref, sn_ref, dn_ref, wn_ref, 0))
    for i in range(nf):
        carry_ref[i] = carry[i]


def layer_body(
    pressure,
    saturation,
    sat_old,
    pore,
    trans_x,
    trans_y,
    trans_z,
    upwind_x,
    upwind_y,
    upwind_z,
    directions,
    adjoint_weights,
    perf_well,
    perf_col,
    perf_top,
    perf_span,
    perf_index,
    bhp,
    target,
):
    layers, rows, cols = pressure.shape
    spatial = (layers, rows, cols)
    ndir = directions.shape[0]

    nf = 2 + 4 * ndir
    vmem = pl.BlockSpec(memory_space=pltpu.VMEM)
    pack_span = 6 if layers % 6 == 0 else layers

    def pack_block(*lead, mid=rows, last=cols):
        return pl.BlockSpec(tuple(lead) + (pack_span, mid, last), lambda b: (0,) * len(lead) + (b, 0, 0))

    x_low, x_high, y_low, y_high = pl.pallas_call(
        pack_kernel,
        grid=(layers // pack_span,),
        out_shape=[
            jax.ShapeDtypeStruct((layers, rows, nf + 2), jnp.float32),
            jax.ShapeDtypeStruct((layers, rows, nf), jnp.float32),
            jax.ShapeDtypeStruct((layers, nf + 2, cols), jnp.float32),
            jax.ShapeDtypeStruct((layers, nf, cols), jnp.float32),
        ],
        in_specs=[pack_block(), pack_block(), pack_block(ndir, 2), pack_block(ndir, 2)] + [pack_block()] * 4,
        out_specs=[
            pack_block(last=nf + 2),
            pack_block(last=nf),
            pack_block(mid=nf + 2),
            pack_block(mid=nf),
        ],
        compiler_params=pltpu.CompilerParams(dimension_semantics=("arbitrary",)),
        cost_estimate=pl.CostEstimate(
            flops=layers * rows * cols * 160,
            transcendentals=0,
            bytes_accessed=(6 + 4 * ndir) * layers * rows * cols * 4,
        ),
    )(pressure, saturation, directions, adjoint_weights, trans_x, upwind_x, trans_y, upwind_y)
    x_low, x_high, y_low, y_high, pressure, saturation, directions, adjoint_weights = lax.optimization_barrier(
        (x_low, x_high, y_low, y_high, pressure, saturation, directions, adjoint_weights)
    )
    hxl = shift_along(x_low, "gx", True)
    hxr = shift_along(x_high, "gx", False)
    hyd = shift_along(y_low, GY_WA, True)
    hyu = shift_along(y_high, GY_WA, False)

    lane_hit = (jnp.arange(cols)[:, None] == (perf_col % cols)[None, :]).astype(jnp.float32)
    row_hit = (jnp.arange(rows)[:, None] == (perf_col // cols)[None, :]).astype(jnp.float32)

    def at_perfs(field):
        by_lane = jnp.dot(field, lane_hit, precision=lax.Precision.HIGHEST)
        return jnp.sum(by_lane * row_hit, axis=-2)

    p_cells = at_perfs(pressure)
    s_cells = at_perfs(saturation)
    dir_cells = at_perfs(directions)
    wts_cells = at_perfs(adjoint_weights)
    depth = jnp.arange(layers)[:, None]
    open_layer = jnp.logical_and(
        depth >= perf_top[None, :], depth < (perf_top + perf_span)[None, :]
    )
    weight = jnp.where(open_layer, perf_index[None, :], 0.0)
    row_bhp, row_target = jnp.take(jnp.stack([bhp, target]), perf_well, axis=1)
    drive = p_cells - row_bhp
    mob = mobility(s_cells)
    slope = mobility_slope(s_cells)
    mob_total = mob[0] + mob[1]
    slope_total = slope[0] + slope[1]
    rates = weight * mob * drive
    rate_tangent = weight * (mob * dir_cells[:, 0:1] + slope * drive * dir_cells[:, 1:2])
    grad_p = weight * (mob[0] * wts_cells[:, 0] + mob[1] * wts_cells[:, 1])
    grad_s = weight * drive * (slope[0] * wts_cells[:, 0] + slope[1] * wts_cells[:, 1])
    row_sums = jnp.concatenate(
        [
            jnp.sum(weight * mob_total, axis=0)[None],
            jnp.sum(rates[0] + rates[1], axis=0)[None],
            jnp.sum(rate_tangent[:, 0] + rate_tangent[:, 1], axis=1),
            jnp.sum(grad_p, axis=1),
        ],
        axis=0,
    )
    packed = jnp.concatenate([row_sums, perf_well.astype(jnp.float32)[None]], axis=0)
    everyone = gather_everywhere(packed)


    all_sums = jnp.moveaxis(everyone[:, :-1], 1, 0).reshape(row_sums.shape[0], -1)
    all_wells = everyone[:, -1].reshape(-1)
    same_well = (perf_well.astype(jnp.float32)[:, None] == all_wells[None, :]).astype(jnp.float32)
    row_totals = jnp.dot(all_sums, same_well.T, precision=lax.Precision.HIGHEST)
    row_factors = well_factors(row_totals, row_target)
    wells_res = rates - weight * mob * row_factors[0]
    wells_fwd = rate_tangent - (weight * mob)[None] * row_factors[1 : 1 + ndir][:, None, None, :]
    out_f = row_factors[1 + ndir :][:, None, :]
    wells_adj = jnp.stack(
        [grad_p - weight * mob_total * out_f, grad_s - weight * slope_total * drive * out_f], axis=1
    )
    combined = jnp.concatenate([wells_res[None], wells_fwd, wells_adj], axis=0)
    by_row = combined[..., None, :] * row_hit
    spread = jnp.dot(by_row, lane_hit.T, precision=lax.Precision.HIGHEST)

    span = 6 if layers % 6 == 0 else layers
    blocks = layers // span

    def layer_block(*lead):
        return pl.BlockSpec(tuple(lead) + (span, rows, cols), lambda b: (0,) * len(lead) + (b, 0, 0))

    def next_layer(*lead):
        return pl.BlockSpec(
            tuple(lead) + (1, rows, cols),
            lambda b: (0,) * len(lead) + (jnp.minimum((b + 1) * span, layers - 1), 0, 0),
        )

    def halo_block(mid, last):
        return pl.BlockSpec((span, mid, last), lambda b: (b, 0, 0))

    flux = pl.pallas_call(
        stencil_kernel,
        grid=(blocks,),
        out_shape=[
            jax.ShapeDtypeStruct((2,) + spatial, jnp.float32),
            jax.ShapeDtypeStruct((ndir, 2) + spatial, jnp.float32),
            jax.ShapeDtypeStruct((ndir, 2) + spatial, jnp.float32),
        ],
        in_specs=[layer_block()] * 10
        + [layer_block(ndir, 2)] * 2
        + [next_layer()] * 2
        + [next_layer(ndir, 2)] * 2
        + [
            halo_block(rows, nf + 2),
            halo_block(rows, nf),
            halo_block(nf + 2, cols),
            halo_block(nf, cols),
        ],
        out_specs=[layer_block(2), layer_block(ndir, 2), layer_block(ndir, 2)],
        scratch_shapes=[pltpu.VMEM((nf, rows, cols), jnp.float32)],
        compiler_params=pltpu.CompilerParams(dimension_semantics=("arbitrary",)),
        cost_estimate=pl.CostEstimate(
            flops=layers * rows * cols * 1200,
            transcendentals=0,
            bytes_accessed=(10 + 4 * 4 * ndir + 2 + 2 * 2 * ndir) * layers * rows * cols * 4,
        ),
    )(
        pressure,
        saturation,
        sat_old,
        pore,
        trans_x,
        trans_y,
        trans_z,
        upwind_x,
        upwind_y,
        upwind_z,
        directions,
        adjoint_weights,
        pressure,
        saturation,
        directions,
        adjoint_weights,
        hxl,
        hxr,
        hyd,
        hyu,
    )
    reduced_residual, forward_products, adjoint_products = flux
    reduced_residual = reduced_residual + spread[0]
    forward_products = forward_products + spread[1 : 1 + ndir]
    adjoint_products = adjoint_products + spread[1 + ndir :]
    return (reduced_residual, forward_products, adjoint_products)


def solution(mesh):
    split = Mesh(
        mesh.devices.reshape(mesh.shape["gx"], 4, 4, mesh.shape["wa"]), ("gx", "gy_0", "gy_1", "wa")
    )
    return jax.shard_map(
        layer_body,
        mesh=split,
        in_specs=(
            P(None, GY_WA, "gx"),
            P(None, GY_WA, "gx"),
            P(None, GY_WA, "gx"),
            P(None, GY_WA, "gx"),
            P(None, GY_WA, "gx"),
            P(None, GY_WA, "gx"),
            P(None, GY_WA, "gx"),
            P(None, GY_WA, "gx"),
            P(None, GY_WA, "gx"),
            P(None, GY_WA, "gx"),
            P(None, None, None, GY_WA, "gx"),
            P(None, None, None, GY_WA, "gx"),
            P(GX_GY_WA),
            P(GX_GY_WA),
            P(GX_GY_WA),
            P(GX_GY_WA),
            P(GX_GY_WA),
            P(),
            P(),
        ),
        out_specs=(
            P(None, None, GY_WA, "gx"),
            P(None, None, None, GY_WA, "gx"),
            P(None, None, None, GY_WA, "gx"),
        ),
        check_vma=False,
    )
```

```python
import jax
import jax.numpy as jnp
from jax import lax
from jax.experimental import pallas as pl
from jax.experimental.pallas import tpu as pltpu
from jax.sharding import Mesh
from jax.sharding import PartitionSpec as P


GY_WA = ("gy_0", "gy_1", "wa")
GX_GY_WA = ("gx", "gy_0", "gy_1", "wa")


water_visc = 0.5
oil_visc = 2.0
water_head = 0.3
oil_head = 0.2


def gather_everywhere(block):
    peers = lax.axis_size(GX_GY_WA)
    flat = jnp.broadcast_to(block.reshape(1, -1), (peers, block.size))
    return lax.all_to_all(flat, GX_GY_WA, 0, 0, tiled=True).reshape((peers,) + block.shape)


def shift_along(block, axis, down):
    size = lax.axis_size(axis)
    pairs = [(i, i + 1) for i in range(size - 1)]
    if not down:
        pairs = [(b, a) for a, b in pairs]
    return lax.ppermute(block, axis, pairs)


def mobility(sat):
    return jnp.stack([sat * sat / water_visc, (1.0 - sat) * (1.0 - sat) / oil_visc])


def mobility_slope(sat):
    return jnp.stack([2.0 * sat / water_visc, -2.0 * (1.0 - sat) / oil_visc])


def well_factors(sums, goal):
    return jnp.concatenate([((sums[1] - goal) / sums[0])[None], sums[2:] / sums[0][None]], axis=0)


def face_terms(trans, up, a, b, heads, ndir):
    pa, sa, vpa, vsa, wwa, woa = a
    pb, sb, vpb, vsb, wwb, wob = b
    su = jnp.where(up, sa, sb)
    drop = pa - pb
    pot_w = drop + heads[0]
    pot_o = drop + heads[1]
    tl_w = trans * (su * su / water_visc)
    tl_o = trans * ((1.0 - su) * (1.0 - su) / oil_visc)
    f_w = tl_w * pot_w
    f_o = tl_o * pot_o
    td_w = trans * (2.0 * su / water_visc) * pot_w
    td_o = trans * (-2.0 * (1.0 - su) / oil_visc) * pot_o
    jv_w, jv_o, jt_p, jt_s = [], [], [], []
    for d in range(ndir):
        vsu = jnp.where(up, vsa[d], vsb[d])
        dvp = vpa[d] - vpb[d]
        jv_w.append(td_w * vsu + tl_w * dvp)
        jv_o.append(td_o * vsu + tl_o * dvp)
        dww = wwa[d] - wwb[d]
        dwo = woa[d] - wob[d]
        jt_p.append(dww * tl_w + dwo * tl_o)
        jt_s.append(dww * td_w + dwo * td_o)
    zero = jnp.zeros_like(su)
    as_a = [f_w, f_o] + jv_w + jv_o + jt_p + [jnp.where(up, g, zero) for g in jt_s]
    as_b = [-f_w, -f_o] + [-x for x in jv_w] + [-x for x in jv_o] + [-x for x in jt_p]
    as_b = as_b + [jnp.where(up, zero, g) for g in jt_s]
    return as_a, as_b


def pack_kernel(p_ref, s_ref, d_ref, w_ref, tx_ref, ux_ref, ty_ref, uy_ref, xl_ref, xr_ref, yd_ref, yu_ref):
    ndir = d_ref.shape[0]
    layers, rows, cols = p_ref.shape
    lane = lax.broadcasted_iota(jnp.int32, (rows, cols), 1)
    sub = lax.broadcasted_iota(jnp.int32, (rows, cols), 0)
    nf = 2 + 4 * ndir

    def rolled(x, shift, axis):
        return x if shift == 0 else pltpu.roll(x, shift, axis)

    def row_of(ref, lead, r):
        v = ref[lead + (pl.ds(r, 1), slice(None))]
        return jnp.broadcast_to(v.astype(jnp.float32), (rows, cols))

    def rows_into(ref, k, sources, source_row):
        count = len(sources)
        for start in range(0, count, rows):
            acc = jnp.zeros((rows, cols), jnp.float32)
            for f in range(start, min(start + rows, count)):
                src, lead = sources[f]
                acc = jnp.where(sub == f - start, row_of(src, lead, source_row), acc)
            n = min(rows, count - start)
            ref[k, pl.ds(start, n), :] = acc[:n]

    def body(k, carry):
        cells = [p_ref[k], s_ref[k]]
        for half in range(2):
            cells += [d_ref[d, half, k] for d in range(ndir)]
        for half in range(2):
            cells += [w_ref[d, half, k] for d in range(ndir)]
        sources = [(p_ref, (k,)), (s_ref, (k,))]
        for half in range(2):
            sources += [(d_ref, (d, half, k)) for d in range(ndir)]
        for half in range(2):
            sources += [(w_ref, (d, half, k)) for d in range(ndir)]
        low_x = cells + [tx_ref[k], ux_ref[k].astype(jnp.float32)]
        xl = jnp.zeros((rows, cols), jnp.float32)
        for f, t in enumerate(low_x):
            xl = jnp.where(lane == f, rolled(t, (f - (cols - 1)) % cols, 1), xl)
        xr = jnp.zeros((rows, cols), jnp.float32)
        for f, t in enumerate(cells):
            xr = jnp.where(lane == f, rolled(t, f % cols, 1), xr)
        xl_ref[k] = xl[:, : nf + 2]
        xr_ref[k] = xr[:, :nf]
        rows_into(yd_ref, k, sources + [(ty_ref, (k,)), (uy_ref, (k,))], rows - 1)
        rows_into(yu_ref, k, sources, 0)
        return carry

    lax.fori_loop(0, layers, body, 0)


def stencil_kernel(
    p_ref,
    s_ref,
    so_ref,
    pore_ref,
    tx_ref,
    ty_ref,
    tz_ref,
    ux_ref,
    uy_ref,
    uz_ref,
    d_ref,
    w_ref,
    pn_ref,
    sn_ref,
    dn_ref,
    wn_ref,
    hxl_ref,
    hxr_ref,
    hyd_ref,
    hyu_ref,
    r_out,
    jv_out,
    jt_out,
    carry_ref,
):
    ndir = d_ref.shape[0]
    span, rows, cols = p_ref.shape
    block = pl.program_id(0)
    layers = span * pl.num_programs(0)
    lane = lax.broadcasted_iota(jnp.int32, (rows, cols), 1)
    sub = lax.broadcasted_iota(jnp.int32, (rows, cols), 0)
    first_lane = lane == 0
    last_lane = lane == cols - 1
    first_sub = sub == 0
    last_sub = sub == rows - 1
    last_x = lax.axis_index("gx") == lax.axis_size("gx") - 1
    last_y = lax.axis_index(GY_WA) == lax.axis_size(GY_WA) - 1
    cut_x = jnp.logical_and(last_lane, last_x)
    cut_y = jnp.logical_and(last_sub, last_y)
    nf = 2 + 4 * ndir

    def cells_of(pr, sr, dr, wr, k):
        out = [pr[k], sr[k]]
        for half in range(2):
            out += [dr[d, half, k] for d in range(ndir)]
        for half in range(2):
            out += [wr[d, half, k] for d in range(ndir)]
        return out

    def group(flat):
        return (
            flat[0],
            flat[1],
            flat[2 : 2 + ndir],
            flat[2 + ndir : 2 + 2 * ndir],
            flat[2 + 2 * ndir : 2 + 3 * ndir],
            flat[2 + 3 * ndir : 2 + 4 * ndir],
        )

    def col(ref, k, f):
        return jnp.broadcast_to(ref[k, :, pl.ds(f, 1)], (rows, cols))

    def row(ref, k, f):
        return jnp.broadcast_to(ref[k, pl.ds(f, 1), :], (rows, cols))

    def store(k, vals):
        for i in range(nf):
            if i < 2:
                ref, idx = r_out, (i, k)
            elif i < 2 + 2 * ndir:
                j = i - 2
                ref, idx = jv_out, (j % ndir, j // ndir, k)
            else:
                j = i - 2 - 2 * ndir
                ref, idx = jt_out, (j % ndir, j // ndir, k)
            ref[idx] = vals[i]

    def layer(k, carry, above):
        here = cells_of(p_ref, s_ref, d_ref, w_ref, k)
        left = [jnp.where(first_lane, col(hxl_ref, k, f), pltpu.roll(x, 1, 1)) for f, x in enumerate(here)]
        right = [jnp.where(last_lane, col(hxr_ref, k, f), pltpu.roll(x, cols - 1, 1)) for f, x in enumerate(here)]
        down = [jnp.where(first_sub, row(hyd_ref, k, f), pltpu.roll(x, 1, 0)) for f, x in enumerate(here)]
        up_ = [jnp.where(last_sub, row(hyu_ref, k, f), pltpu.roll(x, rows - 1, 0)) for f, x in enumerate(here)]

        tx = tx_ref[k]
        ux = ux_ref[k].astype(jnp.float32)
        ty = ty_ref[k]
        uy = uy_ref[k].astype(jnp.float32)
        tx_f = jnp.where(cut_x, 0.0, tx)
        ty_f = jnp.where(cut_y, 0.0, ty)
        tx_b = jnp.where(first_lane, col(hxl_ref, k, nf), pltpu.roll(tx, 1, 1))
        ux_b = jnp.where(first_lane, col(hxl_ref, k, nf + 1), pltpu.roll(ux, 1, 1))
        ty_b = jnp.where(first_sub, row(hyd_ref, k, nf), pltpu.roll(ty, 1, 0))
        uy_b = jnp.where(first_sub, row(hyd_ref, k, nf + 1), pltpu.roll(uy, 1, 0))
        tz = jnp.where(block * span + k < layers - 1, tz_ref[k], 0.0)
        uz = uz_ref[k] == 1

        g_here = group(here)
        acc, _ = face_terms(tx_f, ux > 0.5, g_here, group(right), (0.0, 0.0), ndir)
        _, xb = face_terms(tx_b, ux_b > 0.5, group(left), g_here, (0.0, 0.0), ndir)
        yf, _ = face_terms(ty_f, uy > 0.5, g_here, group(up_), (0.0, 0.0), ndir)
        _, yb = face_terms(ty_b, uy_b > 0.5, group(down), g_here, (0.0, 0.0), ndir)
        zf, zb = face_terms(tz, uz, g_here, group(above), (water_head, oil_head), ndir)
        acc = [a + b + c + e for a, b, c, e in zip(acc, xb, yf, yb)]
        acc = [a + z for a, z in zip(acc, zf)]

        change = here[1] - so_ref[k]
        pore = pore_ref[k]
        acc[0] = acc[0] + pore * change
        acc[1] = acc[1] - pore * change
        for d in range(ndir):
            vs = here[2 + ndir + d]
            acc[2 + d] = acc[2 + d] + pore * vs
            acc[2 + ndir + d] = acc[2 + ndir + d] - pore * vs
            jt_s = 2 + 3 * ndir + d
            acc[jt_s] = acc[jt_s] + pore * (here[2 + 2 * ndir + d] - here[2 + 3 * ndir + d])
        acc = [a + c for a, c in zip(acc, carry)]
        store(k, acc)
        return tuple(zb)

    @pl.when(block == 0)
    def _():
        carry_ref[...] = jnp.zeros_like(carry_ref)

    def inner(k, carry):
        return layer(k, carry, cells_of(p_ref, s_ref, d_ref, w_ref, k + 1))

    carry = tuple(carry_ref[i] for i in range(nf))
    carry = lax.fori_loop(0, span - 1, inner, carry)
    carry = layer(span - 1, carry, cells_of(pn_ref, sn_ref, dn_ref, wn_ref, 0))
    for i in range(nf):
        carry_ref[i] = carry[i]


def layer_body(
    pressure,
    saturation,
    sat_old,
    pore,
    trans_x,
    trans_y,
    trans_z,
    upwind_x,
    upwind_y,
    upwind_z,
    directions,
    adjoint_weights,
    perf_well,
    perf_col,
    perf_top,
    perf_span,
    perf_index,
    bhp,
    target,
):
    layers, rows, cols = pressure.shape
    spatial = (layers, rows, cols)
    ndir = directions.shape[0]

    nf = 2 + 4 * ndir
    vmem = pl.BlockSpec(memory_space=pltpu.VMEM)
    pack_span = 6 if layers % 6 == 0 else layers

    def pack_block(*lead, mid=rows, last=cols):
        return pl.BlockSpec(tuple(lead) + (pack_span, mid, last), lambda b: (0,) * len(lead) + (b, 0, 0))

    x_low, x_high, y_low, y_high = pl.pallas_call(
        pack_kernel,
        grid=(layers // pack_span,),
        out_shape=[
            jax.ShapeDtypeStruct((layers, rows, nf + 2), jnp.float32),
            jax.ShapeDtypeStruct((layers, rows, nf), jnp.float32),
            jax.ShapeDtypeStruct((layers, nf + 2, cols), jnp.float32),
            jax.ShapeDtypeStruct((layers, nf, cols), jnp.float32),
        ],
        in_specs=[pack_block(), pack_block(), pack_block(ndir, 2), pack_block(ndir, 2)] + [pack_block()] * 4,
        out_specs=[
            pack_block(last=nf + 2),
            pack_block(last=nf),
            pack_block(mid=nf + 2),
            pack_block(mid=nf),
        ],
        compiler_params=pltpu.CompilerParams(dimension_semantics=("arbitrary",)),
        cost_estimate=pl.CostEstimate(
            flops=layers * rows * cols * 160,
            transcendentals=0,
            bytes_accessed=(6 + 4 * ndir) * layers * rows * cols * 4,
        ),
    )(pressure, saturation, directions, adjoint_weights, trans_x, upwind_x, trans_y, upwind_y)
    x_low, x_high, y_low, y_high, pressure, saturation, directions, adjoint_weights = lax.optimization_barrier(
        (x_low, x_high, y_low, y_high, pressure, saturation, directions, adjoint_weights)
    )
    hxl = shift_along(x_low, "gx", True)
    hxr = shift_along(x_high, "gx", False)
    hyd = shift_along(y_low, GY_WA, True)
    hyu = shift_along(y_high, GY_WA, False)

    lane_hit = (jnp.arange(cols)[:, None] == (perf_col % cols)[None, :]).astype(jnp.float32)
    row_hit = (jnp.arange(rows)[:, None] == (perf_col // cols)[None, :]).astype(jnp.float32)

    def at_perfs(field):
        by_lane = jnp.dot(field, lane_hit, precision=lax.Precision.HIGHEST)
        return jnp.sum(by_lane * row_hit, axis=-2)

    p_cells = at_perfs(pressure)
    s_cells = at_perfs(saturation)
    dir_cells = at_perfs(directions)
    wts_cells = at_perfs(adjoint_weights)
    depth = jnp.arange(layers)[:, None]
    open_layer = jnp.logical_and(
        depth >= perf_top[None, :], depth < (perf_top + perf_span)[None, :]
    )
    weight = jnp.where(open_layer, perf_index[None, :], 0.0)
    row_bhp, row_target = jnp.take(jnp.stack([bhp, target]), perf_well, axis=1)
    drive = p_cells - row_bhp
    mob = mobility(s_cells)
    slope = mobility_slope(s_cells)
    mob_total = mob[0] + mob[1]
    slope_total = slope[0] + slope[1]
    rates = weight * mob * drive
    rate_tangent = weight * (mob * dir_cells[:, 0:1] + slope * drive * dir_cells[:, 1:2])
    grad_p = weight * (mob[0] * wts_cells[:, 0] + mob[1] * wts_cells[:, 1])
    grad_s = weight * drive * (slope[0] * wts_cells[:, 0] + slope[1] * wts_cells[:, 1])
    row_sums = jnp.concatenate(
        [
            jnp.sum(weight * mob_total, axis=0)[None],
            jnp.sum(rates[0] + rates[1], axis=0)[None],
            jnp.sum(rate_tangent[:, 0] + rate_tangent[:, 1], axis=1),
            jnp.sum(grad_p, axis=1),
        ],
        axis=0,
    )
    packed = jnp.concatenate([row_sums, perf_well.astype(jnp.float32)[None]], axis=0)
    everyone = gather_everywhere(packed)


    all_sums = jnp.moveaxis(everyone[:, :-1], 1, 0).reshape(row_sums.shape[0], -1)
    all_wells = everyone[:, -1].reshape(-1)
    same_well = (perf_well.astype(jnp.float32)[:, None] == all_wells[None, :]).astype(jnp.float32)
    row_totals = jnp.dot(all_sums, same_well.T, precision=lax.Precision.HIGHEST)
    row_factors = well_factors(row_totals, row_target)
    wells_res = rates - weight * mob * row_factors[0]
    wells_fwd = rate_tangent - (weight * mob)[None] * row_factors[1 : 1 + ndir][:, None, None, :]
    out_f = row_factors[1 + ndir :][:, None, :]
    wells_adj = jnp.stack(
        [grad_p - weight * mob_total * out_f, grad_s - weight * slope_total * drive * out_f], axis=1
    )
    combined = jnp.concatenate([wells_res[None], wells_fwd, wells_adj], axis=0)
    by_row = combined[..., None, :] * row_hit
    spread = jnp.dot(by_row, lane_hit.T, precision=lax.Precision.HIGHEST)

    span = 6 if layers % 6 == 0 else layers
    blocks = layers // span

    def layer_block(*lead):
        return pl.BlockSpec(tuple(lead) + (span, rows, cols), lambda b: (0,) * len(lead) + (b, 0, 0))

    def next_layer(*lead):
        return pl.BlockSpec(
            tuple(lead) + (1, rows, cols),
            lambda b: (0,) * len(lead) + (jnp.minimum((b + 1) * span, layers - 1), 0, 0),
        )

    def halo_block(mid, last):
        return pl.BlockSpec((span, mid, last), lambda b: (b, 0, 0))

    flux = pl.pallas_call(
        stencil_kernel,
        grid=(blocks,),
        out_shape=[
            jax.ShapeDtypeStruct((2,) + spatial, jnp.float32),
            jax.ShapeDtypeStruct((ndir, 2) + spatial, jnp.float32),
            jax.ShapeDtypeStruct((ndir, 2) + spatial, jnp.float32),
        ],
        in_specs=[layer_block()] * 10
        + [layer_block(ndir, 2)] * 2
        + [next_layer()] * 2
        + [next_layer(ndir, 2)] * 2
        + [
            halo_block(rows, nf + 2),
            halo_block(rows, nf),
            halo_block(nf + 2, cols),
            halo_block(nf, cols),
        ],
        out_specs=[layer_block(2), layer_block(ndir, 2), layer_block(ndir, 2)],
        scratch_shapes=[pltpu.VMEM((nf, rows, cols), jnp.float32)],
        compiler_params=pltpu.CompilerParams(dimension_semantics=("arbitrary",)),
        cost_estimate=pl.CostEstimate(
            flops=layers * rows * cols * 1200,
            transcendentals=0,
            bytes_accessed=(10 + 4 * 4 * ndir + 2 + 2 * 2 * ndir) * layers * rows * cols * 4,
        ),
    )(
        pressure,
        saturation,
        sat_old,
        pore,
        trans_x,
        trans_y,
        trans_z,
        upwind_x,
        upwind_y,
        upwind_z,
        directions,
        adjoint_weights,
        pressure,
        saturation,
        directions,
        adjoint_weights,
        hxl,
        hxr,
        hyd,
        hyu,
    )
    reduced_residual, forward_products, adjoint_products = flux
    reduced_residual = reduced_residual + spread[0]
    forward_products = forward_products + spread[1 : 1 + ndir]
    adjoint_products = adjoint_products + spread[1 + ndir :]
    return (reduced_residual, forward_products, adjoint_products)


def solution(mesh):
    split = Mesh(
        mesh.devices.reshape(mesh.shape["gx"], 4, 4, mesh.shape["wa"]), ("gx", "gy_0", "gy_1", "wa")
    )
    return jax.shard_map(
        layer_body,
        mesh=split,
        in_specs=(
            P(None, GY_WA, "gx"),
            P(None, GY_WA, "gx"),
            P(None, GY_WA, "gx"),
            P(None, GY_WA, "gx"),
            P(None, GY_WA, "gx"),
            P(None, GY_WA, "gx"),
            P(None, GY_WA, "gx"),
            P(None, GY_WA, "gx"),
            P(None, GY_WA, "gx"),
            P(None, GY_WA, "gx"),
            P(None, None, None, GY_WA, "gx"),
            P(None, None, None, GY_WA, "gx"),
            P(GX_GY_WA),
            P(GX_GY_WA),
            P(GX_GY_WA),
            P(GX_GY_WA),
            P(GX_GY_WA),
            P(),
            P(),
        ),
        out_specs=(
            P(None, None, GY_WA, "gx"),
            P(None, None, None, GY_WA, "gx"),
            P(None, None, None, GY_WA, "gx"),
        ),
        check_vma=False,
    )
```

```python
import jax
import jax.numpy as jnp
from jax import lax
from jax.experimental import pallas as pl
from jax.experimental.pallas import tpu as pltpu
from jax.sharding import Mesh
from jax.sharding import PartitionSpec as P


GY_WA = ("gy_0", "gy_1", "wa")
GX_GY_WA = ("gx", "gy_0", "gy_1", "wa")


water_visc = 0.5
oil_visc = 2.0
water_head = 0.3
oil_head = 0.2


def gather_everywhere(block):
    peers = lax.axis_size(GX_GY_WA)
    flat = jnp.broadcast_to(block.reshape(1, -1), (peers, block.size))
    return lax.all_to_all(flat, GX_GY_WA, 0, 0, tiled=True).reshape((peers,) + block.shape)


def shift_along(block, axis, down):
    size = lax.axis_size(axis)
    pairs = [(i, i + 1) for i in range(size - 1)]
    if not down:
        pairs = [(b, a) for a, b in pairs]
    return lax.ppermute(block, axis, pairs)


def mobility(sat):
    return jnp.stack([sat * sat / water_visc, (1.0 - sat) * (1.0 - sat) / oil_visc])


def mobility_slope(sat):
    return jnp.stack([2.0 * sat / water_visc, -2.0 * (1.0 - sat) / oil_visc])


def well_factors(sums, goal):
    return jnp.concatenate([((sums[1] - goal) / sums[0])[None], sums[2:] / sums[0][None]], axis=0)


def face_terms(trans, up, a, b, heads, ndir):
    pa, sa, vpa, vsa, wwa, woa = a
    pb, sb, vpb, vsb, wwb, wob = b
    su = jnp.where(up, sa, sb)
    drop = pa - pb
    pot_w = drop + heads[0]
    pot_o = drop + heads[1]
    tl_w = trans * (su * su / water_visc)
    tl_o = trans * ((1.0 - su) * (1.0 - su) / oil_visc)
    f_w = tl_w * pot_w
    f_o = tl_o * pot_o
    td_w = trans * (2.0 * su / water_visc) * pot_w
    td_o = trans * (-2.0 * (1.0 - su) / oil_visc) * pot_o
    jv_w, jv_o, jt_p, jt_s = [], [], [], []
    for d in range(ndir):
        vsu = jnp.where(up, vsa[d], vsb[d])
        dvp = vpa[d] - vpb[d]
        jv_w.append(td_w * vsu + tl_w * dvp)
        jv_o.append(td_o * vsu + tl_o * dvp)
        dww = wwa[d] - wwb[d]
        dwo = woa[d] - wob[d]
        jt_p.append(dww * tl_w + dwo * tl_o)
        jt_s.append(dww * td_w + dwo * td_o)
    zero = jnp.zeros_like(su)
    as_a = [f_w, f_o] + jv_w + jv_o + jt_p + [jnp.where(up, g, zero) for g in jt_s]
    as_b = [-f_w, -f_o] + [-x for x in jv_w] + [-x for x in jv_o] + [-x for x in jt_p]
    as_b = as_b + [jnp.where(up, zero, g) for g in jt_s]
    return as_a, as_b


def pack_kernel(p_ref, s_ref, d_ref, w_ref, tx_ref, ux_ref, ty_ref, uy_ref, xl_ref, xr_ref, yd_ref, yu_ref):
    ndir = d_ref.shape[0]
    layers, rows, cols = p_ref.shape
    lane = lax.broadcasted_iota(jnp.int32, (rows, cols), 1)
    sub = lax.broadcasted_iota(jnp.int32, (rows, cols), 0)
    nf = 2 + 4 * ndir

    def rolled(x, shift, axis):
        return x if shift == 0 else pltpu.roll(x, shift, axis)

    def rows_into(ref, k, tiles, source_row):
        count = len(tiles)
        for start in range(0, count, rows):
            acc = jnp.zeros((rows, cols), jnp.float32)
            for f in range(start, min(start + rows, count)):
                r = f - start
                acc = jnp.where(sub == r, rolled(tiles[f], (r - source_row) % rows, 0), acc)
            n = min(rows, count - start)
            ref[k, pl.ds(start, n), :] = acc[:n]

    def body(k, carry):
        cells = [p_ref[k], s_ref[k]]
        for half in range(2):
            cells += [d_ref[d, half, k] for d in range(ndir)]
        for half in range(2):
            cells += [w_ref[d, half, k] for d in range(ndir)]
        low_x = cells + [tx_ref[k], ux_ref[k].astype(jnp.float32)]
        low_y = cells + [ty_ref[k], uy_ref[k].astype(jnp.float32)]
        xl = jnp.zeros((rows, cols), jnp.float32)
        for f, t in enumerate(low_x):
            xl = jnp.where(lane == f, rolled(t, (f - (cols - 1)) % cols, 1), xl)
        xr = jnp.zeros((rows, cols), jnp.float32)
        for f, t in enumerate(cells):
            xr = jnp.where(lane == f, rolled(t, f % cols, 1), xr)
        xl_ref[k] = xl[:, : nf + 2]
        xr_ref[k] = xr[:, :nf]
        rows_into(yd_ref, k, low_y, rows - 1)
        rows_into(yu_ref, k, cells, 0)
        return carry

    lax.fori_loop(0, layers, body, 0)


def stencil_kernel(
    p_ref,
    s_ref,
    so_ref,
    pore_ref,
    tx_ref,
    ty_ref,
    tz_ref,
    ux_ref,
    uy_ref,
    uz_ref,
    d_ref,
    w_ref,
    pn_ref,
    sn_ref,
    dn_ref,
    wn_ref,
    hxl_ref,
    hxr_ref,
    hyd_ref,
    hyu_ref,
    r_out,
    jv_out,
    jt_out,
    carry_ref,
):
    ndir = d_ref.shape[0]
    span, rows, cols = p_ref.shape
    block = pl.program_id(0)
    layers = span * pl.num_programs(0)
    lane = lax.broadcasted_iota(jnp.int32, (rows, cols), 1)
    sub = lax.broadcasted_iota(jnp.int32, (rows, cols), 0)
    first_lane = lane == 0
    last_lane = lane == cols - 1
    first_sub = sub == 0
    last_sub = sub == rows - 1
    last_x = lax.axis_index("gx") == lax.axis_size("gx") - 1
    last_y = lax.axis_index(GY_WA) == lax.axis_size(GY_WA) - 1
    cut_x = jnp.logical_and(last_lane, last_x)
    cut_y = jnp.logical_and(last_sub, last_y)
    nf = 2 + 4 * ndir

    def cells_of(pr, sr, dr, wr, k):
        out = [pr[k], sr[k]]
        for half in range(2):
            out += [dr[d, half, k] for d in range(ndir)]
        for half in range(2):
            out += [wr[d, half, k] for d in range(ndir)]
        return out

    def group(flat):
        return (
            flat[0],
            flat[1],
            flat[2 : 2 + ndir],
            flat[2 + ndir : 2 + 2 * ndir],
            flat[2 + 2 * ndir : 2 + 3 * ndir],
            flat[2 + 3 * ndir : 2 + 4 * ndir],
        )

    def col(ref, k, f):
        return jnp.broadcast_to(ref[k, :, pl.ds(f, 1)], (rows, cols))

    def row(ref, k, f):
        return jnp.broadcast_to(ref[k, pl.ds(f, 1), :], (rows, cols))

    def store(k, vals):
        for i in range(nf):
            if i < 2:
                ref, idx = r_out, (i, k)
            elif i < 2 + 2 * ndir:
                j = i - 2
                ref, idx = jv_out, (j % ndir, j // ndir, k)
            else:
                j = i - 2 - 2 * ndir
                ref, idx = jt_out, (j % ndir, j // ndir, k)
            ref[idx] = vals[i]

    def layer(k, carry, above):
        here = cells_of(p_ref, s_ref, d_ref, w_ref, k)
        left = [jnp.where(first_lane, col(hxl_ref, k, f), pltpu.roll(x, 1, 1)) for f, x in enumerate(here)]
        right = [jnp.where(last_lane, col(hxr_ref, k, f), pltpu.roll(x, cols - 1, 1)) for f, x in enumerate(here)]
        down = [jnp.where(first_sub, row(hyd_ref, k, f), pltpu.roll(x, 1, 0)) for f, x in enumerate(here)]
        up_ = [jnp.where(last_sub, row(hyu_ref, k, f), pltpu.roll(x, rows - 1, 0)) for f, x in enumerate(here)]

        tx = tx_ref[k]
        ux = ux_ref[k].astype(jnp.float32)
        ty = ty_ref[k]
        uy = uy_ref[k].astype(jnp.float32)
        tx_f = jnp.where(cut_x, 0.0, tx)
        ty_f = jnp.where(cut_y, 0.0, ty)
        tx_b = jnp.where(first_lane, col(hxl_ref, k, nf), pltpu.roll(tx, 1, 1))
        ux_b = jnp.where(first_lane, col(hxl_ref, k, nf + 1), pltpu.roll(ux, 1, 1))
        ty_b = jnp.where(first_sub, row(hyd_ref, k, nf), pltpu.roll(ty, 1, 0))
        uy_b = jnp.where(first_sub, row(hyd_ref, k, nf + 1), pltpu.roll(uy, 1, 0))
        tz = jnp.where(block * span + k < layers - 1, tz_ref[k], 0.0)
        uz = uz_ref[k] == 1

        g_here = group(here)
        acc, _ = face_terms(tx_f, ux > 0.5, g_here, group(right), (0.0, 0.0), ndir)
        _, xb = face_terms(tx_b, ux_b > 0.5, group(left), g_here, (0.0, 0.0), ndir)
        yf, _ = face_terms(ty_f, uy > 0.5, g_here, group(up_), (0.0, 0.0), ndir)
        _, yb = face_terms(ty_b, uy_b > 0.5, group(down), g_here, (0.0, 0.0), ndir)
        zf, zb = face_terms(tz, uz, g_here, group(above), (water_head, oil_head), ndir)
        acc = [a + b + c + e for a, b, c, e in zip(acc, xb, yf, yb)]
        acc = [a + z for a, z in zip(acc, zf)]

        change = here[1] - so_ref[k]
        pore = pore_ref[k]
        acc[0] = acc[0] + pore * change
        acc[1] = acc[1] - pore * change
        for d in range(ndir):
            vs = here[2 + ndir + d]
            acc[2 + d] = acc[2 + d] + pore * vs
            acc[2 + ndir + d] = acc[2 + ndir + d] - pore * vs
            jt_s = 2 + 3 * ndir + d
            acc[jt_s] = acc[jt_s] + pore * (here[2 + 2 * ndir + d] - here[2 + 3 * ndir + d])
        acc = [a + c for a, c in zip(acc, carry)]
        store(k, acc)
        return tuple(zb)

    @pl.when(block == 0)
    def _():
        carry_ref[...] = jnp.zeros_like(carry_ref)

    def inner(k, carry):
        return layer(k, carry, cells_of(p_ref, s_ref, d_ref, w_ref, k + 1))

    carry = tuple(carry_ref[i] for i in range(nf))
    carry = lax.fori_loop(0, span - 1, inner, carry)
    carry = layer(span - 1, carry, cells_of(pn_ref, sn_ref, dn_ref, wn_ref, 0))
    for i in range(nf):
        carry_ref[i] = carry[i]


def layer_body(
    pressure,
    saturation,
    sat_old,
    pore,
    trans_x,
    trans_y,
    trans_z,
    upwind_x,
    upwind_y,
    upwind_z,
    directions,
    adjoint_weights,
    perf_well,
    perf_col,
    perf_top,
    perf_span,
    perf_index,
    bhp,
    target,
):
    layers, rows, cols = pressure.shape
    spatial = (layers, rows, cols)
    ndir = directions.shape[0]

    nf = 2 + 4 * ndir
    vmem = pl.BlockSpec(memory_space=pltpu.VMEM)
    x_low, x_high, y_low, y_high = pl.pallas_call(
        pack_kernel,
        out_shape=[
            jax.ShapeDtypeStruct((layers, rows, nf + 2), jnp.float32),
            jax.ShapeDtypeStruct((layers, rows, nf), jnp.float32),
            jax.ShapeDtypeStruct((layers, nf + 2, cols), jnp.float32),
            jax.ShapeDtypeStruct((layers, nf, cols), jnp.float32),
        ],
        in_specs=[vmem] * 8,
        out_specs=[vmem] * 4,
        cost_estimate=pl.CostEstimate(
            flops=layers * rows * cols * 160,
            transcendentals=0,
            bytes_accessed=(6 + 4 * ndir) * layers * rows * cols * 4,
        ),
    )(pressure, saturation, directions, adjoint_weights, trans_x, upwind_x, trans_y, upwind_y)
    x_low, x_high, y_low, y_high, pressure, saturation, directions, adjoint_weights = lax.optimization_barrier(
        (x_low, x_high, y_low, y_high, pressure, saturation, directions, adjoint_weights)
    )
    hxl = shift_along(x_low, "gx", True)
    hxr = shift_along(x_high, "gx", False)
    hyd = shift_along(y_low, GY_WA, True)
    hyu = shift_along(y_high, GY_WA, False)

    lane_hit = (jnp.arange(cols)[:, None] == (perf_col % cols)[None, :]).astype(jnp.float32)
    row_hit = (jnp.arange(rows)[:, None] == (perf_col // cols)[None, :]).astype(jnp.float32)

    def at_perfs(field):
        by_lane = jnp.dot(field, lane_hit, precision=lax.Precision.HIGHEST)
        return jnp.sum(by_lane * row_hit, axis=-2)

    p_cells = at_perfs(pressure)
    s_cells = at_perfs(saturation)
    dir_cells = at_perfs(directions)
    wts_cells = at_perfs(adjoint_weights)
    depth = jnp.arange(layers)[:, None]
    open_layer = jnp.logical_and(
        depth >= perf_top[None, :], depth < (perf_top + perf_span)[None, :]
    )
    weight = jnp.where(open_layer, perf_index[None, :], 0.0)
    row_bhp, row_target = jnp.take(jnp.stack([bhp, target]), perf_well, axis=1)
    drive = p_cells - row_bhp
    mob = mobility(s_cells)
    slope = mobility_slope(s_cells)
    mob_total = mob[0] + mob[1]
    slope_total = slope[0] + slope[1]
    rates = weight * mob * drive
    rate_tangent = weight * (mob * dir_cells[:, 0:1] + slope * drive * dir_cells[:, 1:2])
    grad_p = weight * (mob[0] * wts_cells[:, 0] + mob[1] * wts_cells[:, 1])
    grad_s = weight * drive * (slope[0] * wts_cells[:, 0] + slope[1] * wts_cells[:, 1])
    row_sums = jnp.concatenate(
        [
            jnp.sum(weight * mob_total, axis=0)[None],
            jnp.sum(rates[0] + rates[1], axis=0)[None],
            jnp.sum(rate_tangent[:, 0] + rate_tangent[:, 1], axis=1),
            jnp.sum(grad_p, axis=1),
        ],
        axis=0,
    )
    packed = jnp.concatenate([row_sums, perf_well.astype(jnp.float32)[None]], axis=0)
    everyone = gather_everywhere(packed)


    same_well = (perf_well.astype(jnp.float32)[:, None, None] == everyone[None, :, -1, :]).astype(jnp.float32)
    row_totals = jnp.einsum("dqc,rdc->qr", everyone[:, :-1], same_well, precision=lax.Precision.HIGHEST)
    row_factors = well_factors(row_totals, row_target)
    wells_res = rates - weight * mob * row_factors[0]
    wells_fwd = rate_tangent - (weight * mob)[None] * row_factors[1 : 1 + ndir][:, None, None, :]
    out_f = row_factors[1 + ndir :][:, None, :]
    wells_adj = jnp.stack(
        [grad_p - weight * mob_total * out_f, grad_s - weight * slope_total * drive * out_f], axis=1
    )
    combined = jnp.concatenate([wells_res[None], wells_fwd, wells_adj], axis=0)
    by_row = combined[..., None, :] * row_hit
    spread = jnp.dot(by_row, lane_hit.T, precision=lax.Precision.HIGHEST)

    span = 6 if layers % 6 == 0 else layers
    blocks = layers // span

    def layer_block(*lead):
        return pl.BlockSpec(tuple(lead) + (span, rows, cols), lambda b: (0,) * len(lead) + (b, 0, 0))

    def next_layer(*lead):
        return pl.BlockSpec(
            tuple(lead) + (1, rows, cols),
            lambda b: (0,) * len(lead) + (jnp.minimum((b + 1) * span, layers - 1), 0, 0),
        )

    def halo_block(mid, last):
        return pl.BlockSpec((span, mid, last), lambda b: (b, 0, 0))

    flux = pl.pallas_call(
        stencil_kernel,
        grid=(blocks,),
        out_shape=[
            jax.ShapeDtypeStruct((2,) + spatial, jnp.float32),
            jax.ShapeDtypeStruct((ndir, 2) + spatial, jnp.float32),
            jax.ShapeDtypeStruct((ndir, 2) + spatial, jnp.float32),
        ],
        in_specs=[layer_block()] * 10
        + [layer_block(ndir, 2)] * 2
        + [next_layer()] * 2
        + [next_layer(ndir, 2)] * 2
        + [
            halo_block(rows, nf + 2),
            halo_block(rows, nf),
            halo_block(nf + 2, cols),
            halo_block(nf, cols),
        ],
        out_specs=[layer_block(2), layer_block(ndir, 2), layer_block(ndir, 2)],
        scratch_shapes=[pltpu.VMEM((nf, rows, cols), jnp.float32)],
        compiler_params=pltpu.CompilerParams(dimension_semantics=("arbitrary",)),
        cost_estimate=pl.CostEstimate(
            flops=layers * rows * cols * 1200,
            transcendentals=0,
            bytes_accessed=(10 + 4 * 4 * ndir + 2 + 2 * 2 * ndir) * layers * rows * cols * 4,
        ),
    )(
        pressure,
        saturation,
        sat_old,
        pore,
        trans_x,
        trans_y,
        trans_z,
        upwind_x,
        upwind_y,
        upwind_z,
        directions,
        adjoint_weights,
        pressure,
        saturation,
        directions,
        adjoint_weights,
        hxl,
        hxr,
        hyd,
        hyu,
    )
    reduced_residual, forward_products, adjoint_products = flux
    cell_row = perf_col // cols
    cell_lane = perf_col % cols
    reduced_residual = reduced_residual.at[..., cell_row, cell_lane].add(wells_res)
    forward_products = forward_products.at[..., cell_row, cell_lane].add(wells_fwd)
    adjoint_products = adjoint_products.at[..., cell_row, cell_lane].add(wells_adj)
    return (reduced_residual, forward_products, adjoint_products)


def solution(mesh):
    split = Mesh(
        mesh.devices.reshape(mesh.shape["gx"], 4, 4, mesh.shape["wa"]), ("gx", "gy_0", "gy_1", "wa")
    )
    return jax.shard_map(
        layer_body,
        mesh=split,
        in_specs=(
            P(None, GY_WA, "gx"),
            P(None, GY_WA, "gx"),
            P(None, GY_WA, "gx"),
            P(None, GY_WA, "gx"),
            P(None, GY_WA, "gx"),
            P(None, GY_WA, "gx"),
            P(None, GY_WA, "gx"),
            P(None, GY_WA, "gx"),
            P(None, GY_WA, "gx"),
            P(None, GY_WA, "gx"),
            P(None, None, None, GY_WA, "gx"),
            P(None, None, None, GY_WA, "gx"),
            P(GX_GY_WA),
            P(GX_GY_WA),
            P(GX_GY_WA),
            P(GX_GY_WA),
            P(GX_GY_WA),
            P(),
            P(),
        ),
        out_specs=(
            P(None, None, GY_WA, "gx"),
            P(None, None, None, GY_WA, "gx"),
            P(None, None, None, GY_WA, "gx"),
        ),
        check_vma=False,
    )
```

```python
import jax
import jax.numpy as jnp
from jax import lax
from jax.experimental import pallas as pl
from jax.experimental.pallas import tpu as pltpu
from jax.sharding import Mesh
from jax.sharding import PartitionSpec as P


GY_WA = ("gy_0", "gy_1", "wa")
GX_GY_WA = ("gx", "gy_0", "gy_1", "wa")


water_visc = 0.5
oil_visc = 2.0
water_head = 0.3
oil_head = 0.2


def gather_everywhere(block):
    peers = lax.axis_size(GX_GY_WA)
    flat = jnp.broadcast_to(block.reshape(1, -1), (peers, block.size))
    return lax.all_to_all(flat, GX_GY_WA, 0, 0, tiled=True).reshape((peers,) + block.shape)


def shift_along(block, axis, down):
    size = lax.axis_size(axis)
    pairs = [(i, i + 1) for i in range(size - 1)]
    if not down:
        pairs = [(b, a) for a, b in pairs]
    return lax.ppermute(block, axis, pairs)


def mobility(sat):
    return jnp.stack([sat * sat / water_visc, (1.0 - sat) * (1.0 - sat) / oil_visc])


def mobility_slope(sat):
    return jnp.stack([2.0 * sat / water_visc, -2.0 * (1.0 - sat) / oil_visc])


def well_factors(sums, goal):
    return jnp.concatenate([((sums[1] - goal) / sums[0])[None], sums[2:] / sums[0][None]], axis=0)


def face_terms(trans, up, a, b, heads, ndir):
    pa, sa, vpa, vsa, wwa, woa = a
    pb, sb, vpb, vsb, wwb, wob = b
    su = jnp.where(up, sa, sb)
    drop = pa - pb
    pot_w = drop + heads[0]
    pot_o = drop + heads[1]
    tl_w = trans * (su * su / water_visc)
    tl_o = trans * ((1.0 - su) * (1.0 - su) / oil_visc)
    f_w = tl_w * pot_w
    f_o = tl_o * pot_o
    td_w = trans * (2.0 * su / water_visc) * pot_w
    td_o = trans * (-2.0 * (1.0 - su) / oil_visc) * pot_o
    jv_w, jv_o, jt_p, jt_s = [], [], [], []
    for d in range(ndir):
        vsu = jnp.where(up, vsa[d], vsb[d])
        dvp = vpa[d] - vpb[d]
        jv_w.append(td_w * vsu + tl_w * dvp)
        jv_o.append(td_o * vsu + tl_o * dvp)
        dww = wwa[d] - wwb[d]
        dwo = woa[d] - wob[d]
        jt_p.append(dww * tl_w + dwo * tl_o)
        jt_s.append(dww * td_w + dwo * td_o)
    zero = jnp.zeros_like(su)
    as_a = [f_w, f_o] + jv_w + jv_o + jt_p + [jnp.where(up, g, zero) for g in jt_s]
    as_b = [-f_w, -f_o] + [-x for x in jv_w] + [-x for x in jv_o] + [-x for x in jt_p]
    as_b = as_b + [jnp.where(up, zero, g) for g in jt_s]
    return as_a, as_b


def pack_kernel(p_ref, s_ref, d_ref, w_ref, tx_ref, ux_ref, ty_ref, uy_ref, xl_ref, xr_ref, yd_ref, yu_ref):
    ndir = d_ref.shape[0]
    layers, rows, cols = p_ref.shape
    lane = lax.broadcasted_iota(jnp.int32, (rows, cols), 1)
    sub = lax.broadcasted_iota(jnp.int32, (rows, cols), 0)
    nf = 2 + 4 * ndir

    def rolled(x, shift, axis):
        return x if shift == 0 else pltpu.roll(x, shift, axis)

    def rows_into(ref, k, tiles, source_row):
        count = len(tiles)
        for start in range(0, count, rows):
            acc = jnp.zeros((rows, cols), jnp.float32)
            for f in range(start, min(start + rows, count)):
                r = f - start
                acc = jnp.where(sub == r, rolled(tiles[f], (r - source_row) % rows, 0), acc)
            n = min(rows, count - start)
            ref[k, pl.ds(start, n), :] = acc[:n]

    def body(k, carry):
        cells = [p_ref[k], s_ref[k]]
        for half in range(2):
            cells += [d_ref[d, half, k] for d in range(ndir)]
        for half in range(2):
            cells += [w_ref[d, half, k] for d in range(ndir)]
        low_x = cells + [tx_ref[k], ux_ref[k].astype(jnp.float32)]
        low_y = cells + [ty_ref[k], uy_ref[k].astype(jnp.float32)]
        xl = jnp.zeros((rows, cols), jnp.float32)
        for f, t in enumerate(low_x):
            xl = jnp.where(lane == f, rolled(t, (f - (cols - 1)) % cols, 1), xl)
        xr = jnp.zeros((rows, cols), jnp.float32)
        for f, t in enumerate(cells):
            xr = jnp.where(lane == f, rolled(t, f % cols, 1), xr)
        xl_ref[k] = xl[:, : nf + 2]
        xr_ref[k] = xr[:, :nf]
        rows_into(yd_ref, k, low_y, rows - 1)
        rows_into(yu_ref, k, cells, 0)
        return carry

    lax.fori_loop(0, layers, body, 0)


def stencil_kernel(
    p_ref,
    s_ref,
    so_ref,
    pore_ref,
    tx_ref,
    ty_ref,
    tz_ref,
    ux_ref,
    uy_ref,
    uz_ref,
    d_ref,
    w_ref,
    pn_ref,
    sn_ref,
    dn_ref,
    wn_ref,
    hxl_ref,
    hxr_ref,
    hyd_ref,
    hyu_ref,
    r_out,
    jv_out,
    jt_out,
    carry_ref,
):
    ndir = d_ref.shape[0]
    span, rows, cols = p_ref.shape
    block = pl.program_id(0)
    layers = span * pl.num_programs(0)
    lane = lax.broadcasted_iota(jnp.int32, (rows, cols), 1)
    sub = lax.broadcasted_iota(jnp.int32, (rows, cols), 0)
    first_lane = lane == 0
    last_lane = lane == cols - 1
    first_sub = sub == 0
    last_sub = sub == rows - 1
    last_x = lax.axis_index("gx") == lax.axis_size("gx") - 1
    last_y = lax.axis_index(GY_WA) == lax.axis_size(GY_WA) - 1
    cut_x = jnp.logical_and(last_lane, last_x)
    cut_y = jnp.logical_and(last_sub, last_y)
    nf = 2 + 4 * ndir

    def cells_of(pr, sr, dr, wr, k):
        out = [pr[k], sr[k]]
        for half in range(2):
            out += [dr[d, half, k] for d in range(ndir)]
        for half in range(2):
            out += [wr[d, half, k] for d in range(ndir)]
        return out

    def group(flat):
        return (
            flat[0],
            flat[1],
            flat[2 : 2 + ndir],
            flat[2 + ndir : 2 + 2 * ndir],
            flat[2 + 2 * ndir : 2 + 3 * ndir],
            flat[2 + 3 * ndir : 2 + 4 * ndir],
        )

    def col(ref, k, f):
        return jnp.broadcast_to(ref[k, :, pl.ds(f, 1)], (rows, cols))

    def row(ref, k, f):
        return jnp.broadcast_to(ref[k, pl.ds(f, 1), :], (rows, cols))

    def store(k, vals):
        for i in range(nf):
            if i < 2:
                ref, idx = r_out, (i, k)
            elif i < 2 + 2 * ndir:
                j = i - 2
                ref, idx = jv_out, (j % ndir, j // ndir, k)
            else:
                j = i - 2 - 2 * ndir
                ref, idx = jt_out, (j % ndir, j // ndir, k)
            ref[idx] = vals[i]

    def layer(k, carry, above):
        here = cells_of(p_ref, s_ref, d_ref, w_ref, k)
        left = [jnp.where(first_lane, col(hxl_ref, k, f), pltpu.roll(x, 1, 1)) for f, x in enumerate(here)]
        right = [jnp.where(last_lane, col(hxr_ref, k, f), pltpu.roll(x, cols - 1, 1)) for f, x in enumerate(here)]
        down = [jnp.where(first_sub, row(hyd_ref, k, f), pltpu.roll(x, 1, 0)) for f, x in enumerate(here)]
        up_ = [jnp.where(last_sub, row(hyu_ref, k, f), pltpu.roll(x, rows - 1, 0)) for f, x in enumerate(here)]

        tx = tx_ref[k]
        ux = ux_ref[k].astype(jnp.float32)
        ty = ty_ref[k]
        uy = uy_ref[k].astype(jnp.float32)
        tx_f = jnp.where(cut_x, 0.0, tx)
        ty_f = jnp.where(cut_y, 0.0, ty)
        tx_b = jnp.where(first_lane, col(hxl_ref, k, nf), pltpu.roll(tx, 1, 1))
        ux_b = jnp.where(first_lane, col(hxl_ref, k, nf + 1), pltpu.roll(ux, 1, 1))
        ty_b = jnp.where(first_sub, row(hyd_ref, k, nf), pltpu.roll(ty, 1, 0))
        uy_b = jnp.where(first_sub, row(hyd_ref, k, nf + 1), pltpu.roll(uy, 1, 0))
        tz = jnp.where(block * span + k < layers - 1, tz_ref[k], 0.0)
        uz = uz_ref[k] == 1

        g_here = group(here)
        acc, _ = face_terms(tx_f, ux > 0.5, g_here, group(right), (0.0, 0.0), ndir)
        _, xb = face_terms(tx_b, ux_b > 0.5, group(left), g_here, (0.0, 0.0), ndir)
        yf, _ = face_terms(ty_f, uy > 0.5, g_here, group(up_), (0.0, 0.0), ndir)
        _, yb = face_terms(ty_b, uy_b > 0.5, group(down), g_here, (0.0, 0.0), ndir)
        zf, zb = face_terms(tz, uz, g_here, group(above), (water_head, oil_head), ndir)
        acc = [a + b + c + e for a, b, c, e in zip(acc, xb, yf, yb)]
        acc = [a + z for a, z in zip(acc, zf)]

        change = here[1] - so_ref[k]
        pore = pore_ref[k]
        acc[0] = acc[0] + pore * change
        acc[1] = acc[1] - pore * change
        for d in range(ndir):
            vs = here[2 + ndir + d]
            acc[2 + d] = acc[2 + d] + pore * vs
            acc[2 + ndir + d] = acc[2 + ndir + d] - pore * vs
            jt_s = 2 + 3 * ndir + d
            acc[jt_s] = acc[jt_s] + pore * (here[2 + 2 * ndir + d] - here[2 + 3 * ndir + d])
        acc = [a + c for a, c in zip(acc, carry)]
        store(k, acc)
        return tuple(zb)

    @pl.when(block == 0)
    def _():
        carry_ref[...] = jnp.zeros_like(carry_ref)

    def inner(k, carry):
        return layer(k, carry, cells_of(p_ref, s_ref, d_ref, w_ref, k + 1))

    carry = tuple(carry_ref[i] for i in range(nf))
    carry = lax.fori_loop(0, span - 1, inner, carry)
    carry = layer(span - 1, carry, cells_of(pn_ref, sn_ref, dn_ref, wn_ref, 0))
    for i in range(nf):
        carry_ref[i] = carry[i]


def layer_body(
    pressure,
    saturation,
    sat_old,
    pore,
    trans_x,
    trans_y,
    trans_z,
    upwind_x,
    upwind_y,
    upwind_z,
    directions,
    adjoint_weights,
    perf_well,
    perf_col,
    perf_top,
    perf_span,
    perf_index,
    bhp,
    target,
):
    layers, rows, cols = pressure.shape
    spatial = (layers, rows, cols)
    ndir = directions.shape[0]

    nf = 2 + 4 * ndir
    vmem = pl.BlockSpec(memory_space=pltpu.VMEM)
    x_low, x_high, y_low, y_high = pl.pallas_call(
        pack_kernel,
        out_shape=[
            jax.ShapeDtypeStruct((layers, rows, nf + 2), jnp.float32),
            jax.ShapeDtypeStruct((layers, rows, nf), jnp.float32),
            jax.ShapeDtypeStruct((layers, nf + 2, cols), jnp.float32),
            jax.ShapeDtypeStruct((layers, nf, cols), jnp.float32),
        ],
        in_specs=[vmem] * 8,
        out_specs=[vmem] * 4,
        cost_estimate=pl.CostEstimate(
            flops=layers * rows * cols * 160,
            transcendentals=0,
            bytes_accessed=(6 + 4 * ndir) * layers * rows * cols * 4,
        ),
    )(pressure, saturation, directions, adjoint_weights, trans_x, upwind_x, trans_y, upwind_y)
    x_low, x_high, y_low, y_high, pressure, saturation, directions, adjoint_weights = lax.optimization_barrier(
        (x_low, x_high, y_low, y_high, pressure, saturation, directions, adjoint_weights)
    )
    hxl = shift_along(x_low, "gx", True)
    hxr = shift_along(x_high, "gx", False)
    hyd = shift_along(y_low, GY_WA, True)
    hyu = shift_along(y_high, GY_WA, False)

    lane_hit = (jnp.arange(cols)[:, None] == (perf_col % cols)[None, :]).astype(jnp.float32)
    row_hit = (jnp.arange(rows)[:, None] == (perf_col // cols)[None, :]).astype(jnp.float32)

    def at_perfs(field):
        by_lane = jnp.dot(field, lane_hit, precision=lax.Precision.HIGHEST)
        return jnp.sum(by_lane * row_hit, axis=-2)

    p_cells = at_perfs(pressure)
    s_cells = at_perfs(saturation)
    dir_cells = at_perfs(directions)
    wts_cells = at_perfs(adjoint_weights)
    depth = jnp.arange(layers)[:, None]
    open_layer = jnp.logical_and(
        depth >= perf_top[None, :], depth < (perf_top + perf_span)[None, :]
    )
    weight = jnp.where(open_layer, perf_index[None, :], 0.0)
    row_bhp, row_target = jnp.take(jnp.stack([bhp, target]), perf_well, axis=1)
    drive = p_cells - row_bhp
    mob = mobility(s_cells)
    slope = mobility_slope(s_cells)
    mob_total = mob[0] + mob[1]
    slope_total = slope[0] + slope[1]
    rates = weight * mob * drive
    rate_tangent = weight * (mob * dir_cells[:, 0:1] + slope * drive * dir_cells[:, 1:2])
    grad_p = weight * (mob[0] * wts_cells[:, 0] + mob[1] * wts_cells[:, 1])
    grad_s = weight * drive * (slope[0] * wts_cells[:, 0] + slope[1] * wts_cells[:, 1])
    row_sums = jnp.concatenate(
        [
            jnp.sum(weight * mob_total, axis=0)[None],
            jnp.sum(rates[0] + rates[1], axis=0)[None],
            jnp.sum(rate_tangent[:, 0] + rate_tangent[:, 1], axis=1),
            jnp.sum(grad_p, axis=1),
        ],
        axis=0,
    )
    packed = jnp.concatenate([row_sums, perf_well.astype(jnp.float32)[None]], axis=0)
    everyone = gather_everywhere(packed)


    same_well = (perf_well.astype(jnp.float32)[:, None, None] == everyone[None, :, -1, :]).astype(jnp.float32)
    row_totals = jnp.einsum("dqc,rdc->qr", everyone[:, :-1], same_well, precision=lax.Precision.HIGHEST)
    row_factors = well_factors(row_totals, row_target)
    wells_res = rates - weight * mob * row_factors[0]
    wells_fwd = rate_tangent - (weight * mob)[None] * row_factors[1 : 1 + ndir][:, None, None, :]
    out_f = row_factors[1 + ndir :][:, None, :]
    wells_adj = jnp.stack(
        [grad_p - weight * mob_total * out_f, grad_s - weight * slope_total * drive * out_f], axis=1
    )
    combined = jnp.concatenate([wells_res[None], wells_fwd, wells_adj], axis=0)
    by_row = combined[..., None, :] * row_hit
    spread = jnp.dot(by_row, lane_hit.T, precision=lax.Precision.HIGH)

    span = 6 if layers % 6 == 0 else layers
    blocks = layers // span

    def layer_block(*lead):
        return pl.BlockSpec(tuple(lead) + (span, rows, cols), lambda b: (0,) * len(lead) + (b, 0, 0))

    def next_layer(*lead):
        return pl.BlockSpec(
            tuple(lead) + (1, rows, cols),
            lambda b: (0,) * len(lead) + (jnp.minimum((b + 1) * span, layers - 1), 0, 0),
        )

    def halo_block(mid, last):
        return pl.BlockSpec((span, mid, last), lambda b: (b, 0, 0))

    flux = pl.pallas_call(
        stencil_kernel,
        grid=(blocks,),
        out_shape=[
            jax.ShapeDtypeStruct((2,) + spatial, jnp.float32),
            jax.ShapeDtypeStruct((ndir, 2) + spatial, jnp.float32),
            jax.ShapeDtypeStruct((ndir, 2) + spatial, jnp.float32),
        ],
        in_specs=[layer_block()] * 10
        + [layer_block(ndir, 2)] * 2
        + [next_layer()] * 2
        + [next_layer(ndir, 2)] * 2
        + [
            halo_block(rows, nf + 2),
            halo_block(rows, nf),
            halo_block(nf + 2, cols),
            halo_block(nf, cols),
        ],
        out_specs=[layer_block(2), layer_block(ndir, 2), layer_block(ndir, 2)],
        scratch_shapes=[pltpu.VMEM((nf, rows, cols), jnp.float32)],
        compiler_params=pltpu.CompilerParams(dimension_semantics=("arbitrary",)),
        cost_estimate=pl.CostEstimate(
            flops=layers * rows * cols * 1200,
            transcendentals=0,
            bytes_accessed=(10 + 4 * 4 * ndir + 2 + 2 * 2 * ndir) * layers * rows * cols * 4,
        ),
    )(
        pressure,
        saturation,
        sat_old,
        pore,
        trans_x,
        trans_y,
        trans_z,
        upwind_x,
        upwind_y,
        upwind_z,
        directions,
        adjoint_weights,
        pressure,
        saturation,
        directions,
        adjoint_weights,
        hxl,
        hxr,
        hyd,
        hyu,
    )
    reduced_residual, forward_products, adjoint_products = flux
    reduced_residual = reduced_residual + spread[0]
    forward_products = forward_products + spread[1 : 1 + ndir]
    adjoint_products = adjoint_products + spread[1 + ndir :]
    return (reduced_residual, forward_products, adjoint_products)


def solution(mesh):
    split = Mesh(
        mesh.devices.reshape(mesh.shape["gx"], 4, 4, mesh.shape["wa"]), ("gx", "gy_0", "gy_1", "wa")
    )
    return jax.shard_map(
        layer_body,
        mesh=split,
        in_specs=(
            P(None, GY_WA, "gx"),
            P(None, GY_WA, "gx"),
            P(None, GY_WA, "gx"),
            P(None, GY_WA, "gx"),
            P(None, GY_WA, "gx"),
            P(None, GY_WA, "gx"),
            P(None, GY_WA, "gx"),
            P(None, GY_WA, "gx"),
            P(None, GY_WA, "gx"),
            P(None, GY_WA, "gx"),
            P(None, None, None, GY_WA, "gx"),
            P(None, None, None, GY_WA, "gx"),
            P(GX_GY_WA),
            P(GX_GY_WA),
            P(GX_GY_WA),
            P(GX_GY_WA),
            P(GX_GY_WA),
            P(),
            P(),
        ),
        out_specs=(
            P(None, None, GY_WA, "gx"),
            P(None, None, None, GY_WA, "gx"),
            P(None, None, None, GY_WA, "gx"),
        ),
        check_vma=False,
    )
```
